32 devices in a mesh: ta: 8 (over z, y), col: 4 (over x, core).
Axes of the slice: x: 2, y: 2, z: 4, core: 2. Of those that a mesh axis runs over, the one named last changes fastest.
Arguments:
- strain: bfloat16 [2048, 512], P('col', 'ta'), may hold values from -6 to 6
- filter_taps: float32 [64], replicated, may hold values from -0.75 to 0.75
Outputs:
- cross_spectra: bfloat16 [4, 512, 128, 256], P('col', 'ta')
The draws below stay inside these ranges and needn't reach their ends.
All inputs are finite; a program needn't handle non-finite values.
Results may differ from the reference program's by a relative error of at most 0.0066.
Values may be sent and summed in bfloat16 or wider, within the bound.
No kernel may reach another device: no remote copies, remote signals or barrier semaphores. Data moves between devices by JAX's collectives and lax.ppermute only.
A program may use at most 64 MiB of HBM per device.

```python
import jax
import jax.numpy as jnp
from jax import lax

TAPS = 64
NFFT = 256
NF = 128
LAGS = 128
CHD = 64
TIME = 512
SEG = 1
CHC = 512
CH = 2048
N_COL = 4


def level_of(stream_key, shape, shards, low, top_value):
    loudness = 1.0
    for position, shards_of in shards:
        steps = jax.random.uniform(jax.random.fold_in(jax.random.fold_in(stream_key, 6), position), (shards_of,), jnp.float32, low / len(shards), top_value / len(shards))
        loudness = loudness * jnp.repeat(jnp.exp(steps), shape[position] // shards_of).reshape((-1,) + (1,) * (len(shape) - 1 - position))
    return loudness


def bell_draw(rng, extent, deviation, most, split=(), kind=jnp.bfloat16):
    array = jax.random.normal(rng, extent, jnp.float32) * deviation
    if len(split) > 0:
        array = level_of(rng, extent, split, -0.22, 0.18) * array
    return jnp.clip(array, min=-most, max=most).astype(kind)


def setup_inputs(seed: int = 0) -> dict:
    key_list = jax.random.split(jax.random.key(seed), 3)
    strain = bell_draw(key_list[0], (CH, TIME), 1.0, 6.0, ((0, 4), (1, 8)))
    filter_taps = bell_draw(key_list[1], (TAPS,), TAPS ** -0.5, 0.75, (), jnp.float32)
    return dict(strain=strain, filter_taps=filter_taps)


def tap_rows(filter_taps, outputs):
    tap_count = filter_taps.shape[0]
    window = 2 * outputs + tap_count
    flipped = filter_taps[::-1]
    period = jnp.concatenate([flipped, jnp.zeros((window + 2 - tap_count,), jnp.float32)])
    repeated = jnp.tile(period, outputs)[:outputs * window]
    return repeated.reshape(outputs, window)

def decimate(history, samples, filter_taps):
    channels, length = samples.shape
    tap_count = filter_taps.shape[0]
    outputs = min(length, NFFT) // 2
    blocks = length // (2 * outputs)
    joined = jnp.concatenate([history, samples, jnp.zeros((channels, 2 * outputs - tap_count), jnp.float32)], axis=1)
    joined = joined.reshape(channels, blocks + 1, 2 * outputs)
    windows = jnp.concatenate([joined[:, :-1], joined[:, 1:, :tap_count]], axis=2)
    matrix = tap_rows(filter_taps, outputs)
    result = jnp.einsum('cbw,tw->cbt', windows, matrix, precision=lax.Precision.HIGHEST)
    return result.reshape(channels, blocks * outputs).astype(jnp.bfloat16)

def fourier_table():
    moment = lax.broadcasted_iota(jnp.int32, (NFFT, NF), 0)
    frequency = lax.broadcasted_iota(jnp.int32, (NFFT, NF), 1) + 1
    phase_index = moment * frequency % NFFT
    angles = phase_index.astype(jnp.float32) * (2.0 * jnp.pi / NFFT)
    window_taper = 0.5 - 0.5 * jnp.cos(moment.astype(jnp.float32) * (2.0 * jnp.pi / NFFT))
    return jnp.concatenate([window_taper * jnp.cos(angles), -window_taper * jnp.sin(angles)], axis=1)

def whiten(filtered):
    channels, length = filtered.shape
    pieces = filtered.reshape(channels, length // NF, NF)
    segment_rows = jnp.concatenate([pieces[:, :-1], pieces[:, 1:]], axis=2)
    spectrum = jnp.einsum('csn,nf->csf', segment_rows.astype(jnp.float32), fourier_table(), precision=lax.Precision.HIGHEST)
    real_part = spectrum[..., :NF]
    imag_part = spectrum[..., NF:]
    powers = real_part * real_part + imag_part * imag_part
    mean_power = lax.optimization_barrier(jnp.mean(powers, axis=-1, keepdims=True))
    whitening = 1.0 / jnp.sqrt(powers + mean_power + 1e-06)
    return jnp.concatenate([real_part * whitening, imag_part * whitening], axis=-1).astype(jnp.bfloat16)

def cross_block(own_rows, extended):
    own_real = own_rows[..., :NF].astype(jnp.float32)
    own_imag = own_rows[..., NF:].astype(jnp.float32)
    far_real = extended[..., :NF].astype(jnp.float32)
    far_imag = extended[..., NF:].astype(jnp.float32)
    real_sum = jnp.einsum('csf,dsf->cdf', own_real, far_real) + jnp.einsum('csf,dsf->cdf', own_imag, far_imag)
    imag_sum = jnp.einsum('csf,dsf->cdf', own_imag, far_real) - jnp.einsum('csf,dsf->cdf', own_real, far_imag)
    combined = jnp.concatenate([real_sum, imag_sum], axis=-1) / own_rows.shape[1]
    rows = own_rows.shape[0]
    reach = extended.shape[0]
    repeated = combined.reshape(rows * reach, NFFT)
    repeated = jnp.concatenate([repeated, jnp.zeros((rows, NFFT), jnp.float32)], axis=0)
    banded = repeated.reshape(rows, reach + 1, NFFT)[:, :LAGS]
    return banded.astype(jnp.bfloat16)

def reference(strain, filter_taps):
    blocks = strain.reshape(CH // CHD, CHD, TIME)

    def filter_block(channel_block):
        return decimate(jnp.zeros((CHD, TAPS), jnp.float32), channel_block.astype(jnp.float32), filter_taps)
    filtered = lax.map(filter_block, blocks)
    whitened = lax.map(whiten, filtered).reshape(CH, SEG, NFFT)
    padded = jnp.concatenate([whitened, jnp.zeros((LAGS, SEG, NFFT), jnp.bfloat16)], axis=0)

    def per_block(block_index):
        first_row = (block_index * CHD).astype(jnp.int32)
        own_rows = lax.dynamic_slice_in_dim(padded, first_row, CHD, 0)
        extended = lax.dynamic_slice_in_dim(padded, first_row, CHD + LAGS, 0)
        return cross_block(own_rows, extended)
    result = lax.map(per_block, jnp.arange(CH // CHD, dtype=jnp.int32))
    return result.reshape(N_COL, CHC, LAGS, NFFT)
```

```python
import functools

import jax
import jax.numpy as jnp
from jax import lax
from jax.experimental import pallas as pl
from jax.experimental.pallas import tpu as pltpu
from jax.sharding import PartitionSpec as P

NFFT = 256
NF = 128
LAGS = 128


def tap_rows(filter_taps, outputs):
    tap_count = filter_taps.shape[0]
    window = 2 * outputs + tap_count
    flipped = filter_taps[::-1]
    period = jnp.concatenate([flipped, jnp.zeros((window + 2 - tap_count,), jnp.float32)])
    repeated = jnp.tile(period, outputs)[: outputs * window]
    return repeated.reshape(outputs, window)


def decimate(history, samples, filter_taps):
    channels, length = samples.shape
    tap_count = filter_taps.shape[0]
    outputs = min(length, NFFT) // 2
    blocks = length // (2 * outputs)
    joined = jnp.concatenate(
        [history, samples, jnp.zeros((channels, 2 * outputs - tap_count), jnp.float32)], axis=1
    )
    joined = joined.reshape(channels, blocks + 1, 2 * outputs)
    windows = jnp.concatenate([joined[:, :-1], joined[:, 1:, :tap_count]], axis=2)
    matrix = tap_rows(filter_taps, outputs)
    result = jnp.einsum("cbw,tw->cbt", windows, matrix, precision=lax.Precision.HIGHEST)
    return result.reshape(channels, blocks * outputs).astype(jnp.bfloat16)


def fourier_table():
    moment = lax.broadcasted_iota(jnp.int32, (NFFT, NF), 0)
    frequency = lax.broadcasted_iota(jnp.int32, (NFFT, NF), 1) + 1
    phase_index = moment * frequency % NFFT
    angles = phase_index.astype(jnp.float32) * (2.0 * jnp.pi / NFFT)
    window_taper = 0.5 - 0.5 * jnp.cos(moment.astype(jnp.float32) * (2.0 * jnp.pi / NFFT))
    return jnp.concatenate(
        [window_taper * jnp.cos(angles), -window_taper * jnp.sin(angles)], axis=1
    )


def whiten(filtered):
    channels, length = filtered.shape
    pieces = filtered.reshape(channels, length // NF, NF)
    segment_rows = jnp.concatenate([pieces[:, :-1], pieces[:, 1:]], axis=2)
    spectrum = jnp.einsum(
        "csn,nf->csf",
        segment_rows.astype(jnp.float32),
        fourier_table(),
        precision=lax.Precision.HIGHEST,
    )
    real_part = spectrum[..., :NF]
    imag_part = spectrum[..., NF:]
    powers = real_part * real_part + imag_part * imag_part
    mean_power = jnp.mean(powers, axis=-1, keepdims=True)
    whitening = 1.0 / jnp.sqrt(powers + mean_power + 1e-06)
    return jnp.concatenate([real_part * whitening, imag_part * whitening], axis=-1).astype(
        jnp.bfloat16
    )


def gather_time(strain):
    extent = lax.axis_size("ta")
    if extent > 8:
        return lax.all_to_all(strain, "ta", split_axis=0, concat_axis=1, tiled=True)
    position = lax.axis_index("ta")
    rows = strain.shape[0] // extent
    blocks = strain.reshape(extent, rows, strain.shape[1])
    received = [blocks[position]]
    for distance in range(1, extent):
        payload = blocks[(position + distance) % extent]
        route = [(i, (i + distance) % extent) for i in range(extent)]
        received.append(lax.ppermute(payload, "ta", route))
    turned = jnp.stack([received[(-m) % extent] for m in range(extent)])
    ordered = jnp.roll(turned, position, axis=0)
    return ordered.transpose(1, 0, 2).reshape(rows, extent * strain.shape[1])


def cross_kernel(segments, rows_per_step, own_ref, ext_ref, out_ref):
    step = pl.program_id(0)
    base = pl.multiple_of(step * rows_per_step, rows_per_step)
    for i in range(rows_per_step):
        c = base + i
        acc_re = None
        acc_im = None
        for s in range(segments):
            a = own_ref[s, pl.ds(c, 1), :]
            window = ext_ref[s, pl.ds(base, LAGS + rows_per_step), :]
            b = window[i : i + LAGS]
            ar = a[:, :NF]
            ai = a[:, NF:]
            br = b[:, :NF]
            bi = b[:, NF:]
            t1 = ar * br
            t2 = ai * bi
            t3 = ai * br
            t4 = ar * bi
            if acc_re is None:
                acc_re = [t1, t2]
                acc_im = [t3, t4]
            else:
                acc_re = [acc_re[0] + t1, acc_re[1] + t2]
                acc_im = [acc_im[0] + t3, acc_im[1] + t4]
        re = (acc_re[0] + acc_re[1]) / segments
        im = (acc_im[0] - acc_im[1]) / segments
        out_ref[i, :, :NF] = re.astype(out_ref.dtype)
        out_ref[i, :, NF:] = im.astype(out_ref.dtype)


def cross_spectra(own, extended):
    rows, segments, columns = own.shape
    reach_rows = extended.shape[0]
    own_t = own.astype(jnp.float32).transpose(1, 0, 2)
    ext_t = extended.astype(jnp.float32).transpose(1, 0, 2)
    rows_per_step = 8
    return pl.pallas_call(
        functools.partial(cross_kernel, segments, rows_per_step),
        out_shape=jax.ShapeDtypeStruct((rows, LAGS, columns), jnp.bfloat16),
        grid=(rows // rows_per_step,),
        in_specs=[
            pl.BlockSpec((segments, rows, columns), lambda i: (0, 0, 0)),
            pl.BlockSpec((segments, reach_rows, columns), lambda i: (0, 0, 0)),
        ],
        out_specs=pl.BlockSpec((rows_per_step, LAGS, columns), lambda i: (i, 0, 0)),
        cost_estimate=pl.CostEstimate(
            flops=6 * rows * LAGS * NF * segments,
            transcendentals=0,
            bytes_accessed=rows * LAGS * columns * 2 + 4 * segments * (rows + reach_rows) * columns,
        ),
    )(own_t, ext_t)


def body(strain, filter_taps):
    tap_count = filter_taps.shape[0]
    regrouped = gather_time(strain)
    filtered = decimate(
        jnp.zeros((regrouped.shape[0], tap_count), jnp.float32),
        regrouped.astype(jnp.float32),
        filter_taps,
    )
    whitened = whiten(filtered)
    block_rows, segments, columns = whitened.shape
    reach = LAGS // block_rows
    columns_n = lax.axis_size("col")
    extent = lax.axis_size("ta")
    total = columns_n * extent

    def linear(block):
        return (block % extent) * columns_n + block // extent

    pieces = [whitened]
    for offset in range(1, reach + 1):
        route = [(linear(b + offset), linear(b)) for b in range(total) if b + offset < total]
        pieces.append(lax.ppermute(whitened, ("ta", "col"), route))
    extended = jnp.concatenate(pieces, axis=0)
    return cross_spectra(whitened, extended)[None]


def solution(mesh):
    return jax.shard_map(
        body,
        mesh=mesh,
        in_specs=(P("col", "ta"), P()),
        out_specs=P("col", "ta", None, None),
        check_vma=False,
    )
```

```python
import functools

import jax
import jax.numpy as jnp
from jax import lax
from jax.experimental import pallas as pl
from jax.experimental.pallas import tpu as pltpu
from jax.sharding import PartitionSpec as P

NFFT = 256
NF = 128
LAGS = 128


def tap_rows(filter_taps, outputs):
    tap_count = filter_taps.shape[0]
    window = 2 * outputs + tap_count
    flipped = filter_taps[::-1]
    period = jnp.concatenate([flipped, jnp.zeros((window + 2 - tap_count,), jnp.float32)])
    repeated = jnp.tile(period, outputs)[: outputs * window]
    return repeated.reshape(outputs, window)


def decimate(history, samples, filter_taps):
    channels, length = samples.shape
    tap_count = filter_taps.shape[0]
    outputs = min(length, NFFT) // 2
    blocks = length // (2 * outputs)
    joined = jnp.concatenate(
        [history, samples, jnp.zeros((channels, 2 * outputs - tap_count), jnp.float32)], axis=1
    )
    joined = joined.reshape(channels, blocks + 1, 2 * outputs)
    windows = jnp.concatenate([joined[:, :-1], joined[:, 1:, :tap_count]], axis=2)
    matrix = tap_rows(filter_taps, outputs)
    result = jnp.einsum("cbw,tw->cbt", windows, matrix, precision=lax.Precision.HIGHEST)
    return result.reshape(channels, blocks * outputs).astype(jnp.bfloat16)


def fourier_table():
    moment = lax.broadcasted_iota(jnp.int32, (NFFT, NF), 0)
    frequency = lax.broadcasted_iota(jnp.int32, (NFFT, NF), 1) + 1
    phase_index = moment * frequency % NFFT
    angles = phase_index.astype(jnp.float32) * (2.0 * jnp.pi / NFFT)
    window_taper = 0.5 - 0.5 * jnp.cos(moment.astype(jnp.float32) * (2.0 * jnp.pi / NFFT))
    return jnp.concatenate(
        [window_taper * jnp.cos(angles), -window_taper * jnp.sin(angles)], axis=1
    )


def whiten(filtered):
    channels, length = filtered.shape
    pieces = filtered.reshape(channels, length // NF, NF)
    segment_rows = jnp.concatenate([pieces[:, :-1], pieces[:, 1:]], axis=2)
    spectrum = jnp.einsum(
        "csn,nf->csf",
        segment_rows.astype(jnp.float32),
        fourier_table(),
        precision=lax.Precision.HIGHEST,
    )
    real_part = spectrum[..., :NF]
    imag_part = spectrum[..., NF:]
    powers = real_part * real_part + imag_part * imag_part
    mean_power = jnp.mean(powers, axis=-1, keepdims=True)
    whitening = 1.0 / jnp.sqrt(powers + mean_power + 1e-06)
    return jnp.concatenate([real_part * whitening, imag_part * whitening], axis=-1).astype(
        jnp.bfloat16
    )


def cross_kernel(segments, rows_per_step, own_ref, ext_ref, out_ref):
    step = pl.program_id(0)
    base = pl.multiple_of(step * rows_per_step, rows_per_step)
    for i in range(rows_per_step):
        c = base + i
        acc_re = None
        acc_im = None
        for s in range(segments):
            a = own_ref[s, pl.ds(c, 1), :]
            window = ext_ref[s, pl.ds(base, LAGS + rows_per_step), :]
            b = window[i : i + LAGS]
            ar = a[:, :NF]
            ai = a[:, NF:]
            br = b[:, :NF]
            bi = b[:, NF:]
            t1 = ar * br
            t2 = ai * bi
            t3 = ai * br
            t4 = ar * bi
            if acc_re is None:
                acc_re = [t1, t2]
                acc_im = [t3, t4]
            else:
                acc_re = [acc_re[0] + t1, acc_re[1] + t2]
                acc_im = [acc_im[0] + t3, acc_im[1] + t4]
        re = (acc_re[0] + acc_re[1]) / segments
        im = (acc_im[0] - acc_im[1]) / segments
        out_ref[i, :, :NF] = re.astype(out_ref.dtype)
        out_ref[i, :, NF:] = im.astype(out_ref.dtype)


def cross_spectra(own, extended):
    rows, segments, columns = own.shape
    reach_rows = extended.shape[0]
    own_t = own.astype(jnp.float32).transpose(1, 0, 2)
    ext_t = extended.astype(jnp.float32).transpose(1, 0, 2)
    rows_per_step = 8
    return pl.pallas_call(
        functools.partial(cross_kernel, segments, rows_per_step),
        out_shape=jax.ShapeDtypeStruct((rows, LAGS, columns), jnp.bfloat16),
        grid=(rows // rows_per_step,),
        in_specs=[
            pl.BlockSpec((segments, rows, columns), lambda i: (0, 0, 0)),
            pl.BlockSpec((segments, reach_rows, columns), lambda i: (0, 0, 0)),
        ],
        out_specs=pl.BlockSpec((rows_per_step, LAGS, columns), lambda i: (i, 0, 0)),
        cost_estimate=pl.CostEstimate(
            flops=6 * rows * LAGS * NF * segments,
            transcendentals=0,
            bytes_accessed=rows * LAGS * columns * 2 + 4 * segments * (rows + reach_rows) * columns,
        ),
    )(own_t, ext_t)


def body(strain, filter_taps):
    tap_count = filter_taps.shape[0]
    extent = lax.axis_size("ta")
    columns_n = lax.axis_size("col")
    position = lax.axis_index("ta")
    section_rows, slab = strain.shape
    block_rows = section_rows // extent
    reach = LAGS // block_rows
    window = 2 * reach
    before = (reach - 1) * block_rows
    padded = jnp.concatenate(
        [
            jnp.zeros((before, slab), strain.dtype),
            strain,
            jnp.zeros((reach * block_rows, slab), strain.dtype),
        ],
        axis=0,
    )
    outgoing = jnp.concatenate(
        [padded[j * block_rows : (j + window) * block_rows] for j in range(extent)], axis=0
    )
    regrouped = lax.all_to_all(outgoing, "ta", split_axis=0, concat_axis=1, tiled=True)
    filtered = decimate(
        jnp.zeros((regrouped.shape[0], tap_count), jnp.float32),
        regrouped.astype(jnp.float32),
        filter_taps,
    )
    whitened = whiten(filtered)
    segments, columns = whitened.shape[1:]
    first_of_section = reach - 1 - jnp.minimum(position, reach - 1)
    payload = lax.dynamic_slice_in_dim(whitened, first_of_section * block_rows, reach * block_rows, 0)

    def linear(ta_index, col_index):
        return ta_index * columns_n + col_index

    route = [
        (linear(m, c + 1), linear(extent - reach + m, c))
        for c in range(columns_n - 1)
        for m in range(reach)
    ]
    next_section = lax.ppermute(payload, ("ta", "col"), route)
    local = whitened[before : before + (reach + 1) * block_rows]
    extended = local
    for j in range(extent - reach, extent):
        kept = (extent - j) * block_rows
        candidate = jnp.concatenate(
            [local[:kept], next_section[: (reach + 1) * block_rows - kept]], axis=0
        )
        extended = jnp.where(position == j, candidate, extended)
    own = local[:block_rows]
    return cross_spectra(own, extended)[None]


def solution(mesh):
    return jax.shard_map(
        body,
        mesh=mesh,
        in_specs=(P("col", "ta"), P()),
        out_specs=P("col", "ta", None, None),
        check_vma=False,
    )
```

```python
import functools

import jax
import jax.numpy as jnp
from jax import lax
from jax.experimental import pallas as pl
from jax.experimental.pallas import tpu as pltpu
from jax.sharding import PartitionSpec as P

NFFT = 256
NF = 128
LAGS = 128


def tap_rows(filter_taps, outputs):
    tap_count = filter_taps.shape[0]
    window = 2 * outputs + tap_count
    flipped = filter_taps[::-1]
    period = jnp.concatenate([flipped, jnp.zeros((window + 2 - tap_count,), jnp.float32)])
    repeated = jnp.tile(period, outputs)[: outputs * window]
    return repeated.reshape(outputs, window)


def decimate(history, samples, filter_taps):
    channels, length = samples.shape
    tap_count = filter_taps.shape[0]
    outputs = min(length, NFFT) // 2
    blocks = length // (2 * outputs)
    joined = jnp.concatenate(
        [history, samples, jnp.zeros((channels, 2 * outputs - tap_count), jnp.float32)], axis=1
    )
    joined = joined.reshape(channels, blocks + 1, 2 * outputs)
    windows = jnp.concatenate([joined[:, :-1], joined[:, 1:, :tap_count]], axis=2)
    matrix = tap_rows(filter_taps, outputs)
    result = jnp.einsum("cbw,tw->cbt", windows, matrix, precision=lax.Precision.HIGHEST)
    return result.reshape(channels, blocks * outputs).astype(jnp.bfloat16)


def fourier_table():
    moment = lax.broadcasted_iota(jnp.int32, (NFFT, NF), 0)
    frequency = lax.broadcasted_iota(jnp.int32, (NFFT, NF), 1) + 1
    phase_index = moment * frequency % NFFT
    angles = phase_index.astype(jnp.float32) * (2.0 * jnp.pi / NFFT)
    window_taper = 0.5 - 0.5 * jnp.cos(moment.astype(jnp.float32) * (2.0 * jnp.pi / NFFT))
    return jnp.concatenate(
        [window_taper * jnp.cos(angles), -window_taper * jnp.sin(angles)], axis=1
    )


def whiten(filtered):
    channels, length = filtered.shape
    pieces = filtered.reshape(channels, length // NF, NF)
    segment_rows = jnp.concatenate([pieces[:, :-1], pieces[:, 1:]], axis=2)
    spectrum = jnp.einsum(
        "csn,nf->csf",
        segment_rows.astype(jnp.float32),
        fourier_table(),
        precision=lax.Precision.HIGHEST,
    )
    real_part = spectrum[..., :NF]
    imag_part = spectrum[..., NF:]
    powers = real_part * real_part + imag_part * imag_part
    mean_power = jnp.mean(powers, axis=-1, keepdims=True)
    whitening = 1.0 / jnp.sqrt(powers + mean_power + 1e-06)
    return jnp.concatenate([real_part * whitening, imag_part * whitening], axis=-1).astype(
        jnp.bfloat16
    )


def cross_kernel(segments, rows_per_step, own_ref, ext_ref, out_ref):
    step = pl.program_id(0)
    base = pl.multiple_of(step * rows_per_step, rows_per_step)
    for i in range(rows_per_step):
        acc_re = None
        acc_im = None
        for s in range(segments):
            a = own_ref[pl.ds(base, rows_per_step), pl.ds(s * NFFT, NFFT)]
            a = a.astype(jnp.float32)[i : i + 1]
            window = ext_ref[pl.ds(base, LAGS + rows_per_step), pl.ds(s * NFFT, NFFT)]
            b = window.astype(jnp.float32)[i : i + LAGS]
            terms = product_terms(a, b)
            if acc_re is None:
                acc_re, acc_im = terms
            else:
                acc_re = [x + y for x, y in zip(acc_re, terms[0])]
                acc_im = [x + y for x, y in zip(acc_im, terms[1])]
        store_row(out_ref, i, acc_re, acc_im, segments)


def product_terms(a, b):
    ar = a[:, :NF]
    ai = a[:, NF:]
    br = b[:, :NF]
    bi = b[:, NF:]
    return [ar * br, ai * bi], [ai * br, ar * bi]


def store_row(out_ref, i, acc_re, acc_im, segments):
    re = (acc_re[0] + acc_re[1]) / segments
    im = (acc_im[0] - acc_im[1]) / segments
    out_ref[i, :, :NF] = re.astype(out_ref.dtype)
    out_ref[i, :, NF:] = im.astype(out_ref.dtype)


def cross_kernel_shifted(segments, rows_per_step, own_ref, ext_ref, out_ref, own_f32, shifted):
    step = pl.program_id(0)
    span = shifted.shape[1]

    @pl.when(step == 0)
    def _():
        own_f32[...] = own_ref[...].astype(jnp.float32)
        whole = ext_ref[...].astype(jnp.float32)
        for i in range(rows_per_step):
            shifted[i] = whole[i : i + span]

    base = pl.multiple_of(step * rows_per_step, rows_per_step)
    for i in range(rows_per_step):
        acc_re = None
        acc_im = None
        for s in range(segments):
            a = own_f32[pl.ds(base + i, 1), pl.ds(s * NFFT, NFFT)]
            b = shifted[i, pl.ds(base, LAGS), pl.ds(s * NFFT, NFFT)]
            terms = product_terms(a, b)
            if acc_re is None:
                acc_re, acc_im = terms
            else:
                acc_re = [x + y for x, y in zip(acc_re, terms[0])]
                acc_im = [x + y for x, y in zip(acc_im, terms[1])]
        store_row(out_ref, i, acc_re, acc_im, segments)


def cross_spectra(own, extended):
    rows, segments, columns = own.shape
    reach_rows = extended.shape[0]
    own_flat = own.reshape(rows, segments * columns)
    ext_flat = extended.reshape(reach_rows, segments * columns)
    rows_per_step = 8
    span = reach_rows - rows_per_step
    scratch_bytes = rows_per_step * span * segments * columns * 4
    cost = pl.CostEstimate(
        flops=6 * rows * LAGS * NF * segments,
        transcendentals=0,
        bytes_accessed=rows * LAGS * columns * 2 + 2 * segments * (rows + reach_rows) * columns,
    )
    common = dict(
        out_shape=jax.ShapeDtypeStruct((rows, LAGS, columns), jnp.bfloat16),
        grid=(rows // rows_per_step,),
        in_specs=[
            pl.BlockSpec((rows, segments * columns), lambda i: (0, 0)),
            pl.BlockSpec((reach_rows, segments * columns), lambda i: (0, 0)),
        ],
        out_specs=pl.BlockSpec((rows_per_step, LAGS, columns), lambda i: (i, 0, 0)),
        cost_estimate=cost,
    )
    if scratch_bytes <= 8 * 1024 * 1024:
        return pl.pallas_call(
            functools.partial(cross_kernel_shifted, segments, rows_per_step),
            scratch_shapes=[
                pltpu.VMEM((rows, segments * columns), jnp.float32),
                pltpu.VMEM((rows_per_step, span, segments * columns), jnp.float32),
            ],
            compiler_params=pltpu.CompilerParams(dimension_semantics=("arbitrary",)),
            **common,
        )(own_flat, ext_flat)
    return pl.pallas_call(
        functools.partial(cross_kernel, segments, rows_per_step), **common
    )(own_flat, ext_flat)


def body(strain, filter_taps):
    tap_count = filter_taps.shape[0]
    extent = lax.axis_size("ta")
    columns_n = lax.axis_size("col")
    position = lax.axis_index("ta")
    section_rows, slab = strain.shape
    block_rows = section_rows // extent
    reach = LAGS // block_rows
    window = 2 * reach
    before = (reach - 1) * block_rows
    padded = jnp.concatenate(
        [
            jnp.zeros((before, slab), strain.dtype),
            strain,
            jnp.zeros((reach * block_rows, slab), strain.dtype),
        ],
        axis=0,
    )
    blocks = padded.reshape(extent + window - 1, block_rows, slab)
    outgoing = jnp.stack([blocks[w : w + extent] for w in range(window)], axis=1)
    outgoing = outgoing.reshape(extent * window * block_rows, slab)
    regrouped = lax.all_to_all(outgoing, "ta", split_axis=0, concat_axis=1, tiled=True)
    filtered = decimate(
        jnp.zeros((regrouped.shape[0], tap_count), jnp.float32),
        regrouped.astype(jnp.float32),
        filter_taps,
    )
    whitened = whiten(filtered)
    segments, columns = whitened.shape[1:]
    first_of_section = reach - 1 - jnp.minimum(position, reach - 1)
    payload = lax.dynamic_slice_in_dim(whitened, first_of_section * block_rows, reach * block_rows, 0)

    def linear(ta_index, col_index):
        return ta_index * columns_n + col_index

    route = [
        (linear(m, c + 1), linear(extent - reach + m, c))
        for c in range(columns_n - 1)
        for m in range(reach)
    ]
    next_section = lax.ppermute(payload, ("ta", "col"), route)
    local = whitened[before : before + (reach + 1) * block_rows]
    extended = local
    for j in range(extent - reach, extent):
        kept = (extent - j) * block_rows
        candidate = jnp.concatenate(
            [local[:kept], next_section[: (reach + 1) * block_rows - kept]], axis=0
        )
        extended = jnp.where(position == j, candidate, extended)
    own = local[:block_rows]
    return cross_spectra(own, extended)[None]


def solution(mesh):
    return jax.shard_map(
        body,
        mesh=mesh,
        in_specs=(P("col", "ta"), P()),
        out_specs=P("col", "ta", None, None),
        check_vma=False,
    )
```

```python
import functools

import jax
import jax.numpy as jnp
from jax import lax
from jax.experimental import pallas as pl
from jax.experimental.pallas import tpu as pltpu
from jax.sharding import PartitionSpec as P

NFFT = 256
NF = 128
LAGS = 128


def tap_rows(filter_taps, outputs):
    tap_count = filter_taps.shape[0]
    window = 2 * outputs + tap_count
    flipped = filter_taps[::-1]
    period = jnp.concatenate([flipped, jnp.zeros((window + 2 - tap_count,), jnp.float32)])
    repeated = jnp.tile(period, outputs)[: outputs * window]
    return repeated.reshape(outputs, window)


def decimate_t(samples, filter_taps):
    length, channels = samples.shape
    tap_count = filter_taps.shape[0]
    outputs = min(length, NFFT) // 2
    blocks = length // (2 * outputs)
    joined = jnp.concatenate(
        [
            jnp.zeros((tap_count, channels), jnp.float32),
            samples,
            jnp.zeros((2 * outputs - tap_count, channels), jnp.float32),
        ],
        axis=0,
    )
    joined = joined.reshape(blocks + 1, 2 * outputs, channels)
    windows = jnp.concatenate([joined[:-1], joined[1:, :tap_count]], axis=1)
    matrix = tap_rows(filter_taps, outputs)
    result = jnp.einsum("tw,bwc->btc", matrix, windows, precision=lax.Precision.HIGHEST)
    return result.reshape(blocks * outputs, channels).astype(jnp.bfloat16)


def fourier_table():
    moment = lax.broadcasted_iota(jnp.int32, (NFFT, NF), 0)
    frequency = lax.broadcasted_iota(jnp.int32, (NFFT, NF), 1) + 1
    phase_index = moment * frequency % NFFT
    angles = phase_index.astype(jnp.float32) * (2.0 * jnp.pi / NFFT)
    window_taper = 0.5 - 0.5 * jnp.cos(moment.astype(jnp.float32) * (2.0 * jnp.pi / NFFT))
    return jnp.concatenate(
        [window_taper * jnp.cos(angles), -window_taper * jnp.sin(angles)], axis=1
    )


def whiten_t(filtered):
    length, channels = filtered.shape
    pieces = filtered.reshape(length // NF, NF, channels)
    segment_rows = jnp.concatenate([pieces[:-1], pieces[1:]], axis=1)
    spectrum = jnp.einsum(
        "nf,snc->sfc",
        fourier_table(),
        segment_rows.astype(jnp.float32),
        precision=lax.Precision.HIGHEST,
    )
    real_part = spectrum[:, :NF]
    imag_part = spectrum[:, NF:]
    powers = real_part * real_part + imag_part * imag_part
    mean_power = jnp.mean(powers, axis=1, keepdims=True)
    whitening = 1.0 / jnp.sqrt(powers + mean_power + 1e-06)
    return jnp.concatenate([real_part * whitening, imag_part * whitening], axis=1).astype(
        jnp.bfloat16
    )


def xor_order(chunks, position, extent):
    bit = 1
    while bit < extent:
        shape = chunks.shape
        swapped = chunks.reshape((extent // (2 * bit), 2, bit) + shape[1:])[:, ::-1].reshape(shape)
        chunks = jnp.where((position & bit) != 0, swapped, chunks)
        bit *= 2
    return chunks


def exchange_time(windows, position, extent):
    if extent & (extent - 1) or extent > 16:
        return lax.all_to_all(windows, "ta", split_axis=0, concat_axis=0, tiled=True)
    chunks = xor_order(windows, position, extent)
    bit = 1
    while bit < extent:
        shape = chunks.shape
        view = chunks.reshape((extent // (2 * bit), 2, bit) + shape[1:])
        route = [(i, i ^ bit) for i in range(extent)]
        arrived = lax.ppermute(view[:, 1], "ta", route)
        chunks = jnp.stack([view[:, 0], arrived], axis=1).reshape(shape)
        bit *= 2
    return xor_order(chunks, position, extent)


def cross_kernel(segments, rows_per_step, own_ref, ext_ref, out_ref):
    step = pl.program_id(0)
    base = pl.multiple_of(step * rows_per_step, rows_per_step)
    for i in range(rows_per_step):
        acc_re = None
        acc_im = None
        for s in range(segments):
            a = own_ref[pl.ds(base, rows_per_step), pl.ds(s * NFFT, NFFT)]
            a = a.astype(jnp.float32)[i : i + 1]
            window = ext_ref[pl.ds(base, LAGS + rows_per_step), pl.ds(s * NFFT, NFFT)]
            b = window.astype(jnp.float32)[i : i + LAGS]
            terms = product_terms(a, b)
            if acc_re is None:
                acc_re, acc_im = terms
            else:
                acc_re = [x + y for x, y in zip(acc_re, terms[0])]
                acc_im = [x + y for x, y in zip(acc_im, terms[1])]
        store_row(out_ref, i, acc_re, acc_im, segments)


def product_terms(a, b):
    ar = a[:, :NF]
    ai = a[:, NF:]
    br = b[:, :NF]
    bi = b[:, NF:]
    return [ar * br, ai * bi], [ai * br, ar * bi]


def store_row(out_ref, i, acc_re, acc_im, segments):
    re = (acc_re[0] + acc_re[1]) / segments
    im = (acc_im[0] - acc_im[1]) / segments
    out_ref[i, :, :NF] = re.astype(out_ref.dtype)
    out_ref[i, :, NF:] = im.astype(out_ref.dtype)


def cross_kernel_shifted(segments, rows_per_step, own_ref, ext_ref, out_ref, own_f32, shifted):
    step = pl.program_id(0)
    span = shifted.shape[1]

    @pl.when(step == 0)
    def _():
        own_f32[...] = own_ref[...].astype(jnp.float32)
        whole = ext_ref[...].astype(jnp.float32)
        for i in range(rows_per_step):
            shifted[i] = whole[i : i + span]

    base = pl.multiple_of(step * rows_per_step, rows_per_step)
    for i in range(rows_per_step):
        acc_re = None
        acc_im = None
        for s in range(segments):
            a = own_f32[pl.ds(base + i, 1), pl.ds(s * NFFT, NFFT)]
            b = shifted[i, pl.ds(base, LAGS), pl.ds(s * NFFT, NFFT)]
            terms = product_terms(a, b)
            if acc_re is None:
                acc_re, acc_im = terms
            else:
                acc_re = [x + y for x, y in zip(acc_re, terms[0])]
                acc_im = [x + y for x, y in zip(acc_im, terms[1])]
        store_row(out_ref, i, acc_re, acc_im, segments)


def cross_spectra(own, extended):
    rows, segments, columns = own.shape
    reach_rows = extended.shape[0]
    own_flat = own.reshape(rows, segments * columns)
    ext_flat = extended.reshape(reach_rows, segments * columns)
    rows_per_step = 8
    span = reach_rows - rows_per_step
    scratch_bytes = rows_per_step * span * segments * columns * 4
    cost = pl.CostEstimate(
        flops=6 * rows * LAGS * NF * segments,
        transcendentals=0,
        bytes_accessed=rows * LAGS * columns * 2 + 2 * segments * (rows + reach_rows) * columns,
    )
    common = dict(
        out_shape=jax.ShapeDtypeStruct((rows, LAGS, columns), jnp.bfloat16),
        grid=(rows // rows_per_step,),
        in_specs=[
            pl.BlockSpec((rows, segments * columns), lambda i: (0, 0)),
            pl.BlockSpec((reach_rows, segments * columns), lambda i: (0, 0)),
        ],
        out_specs=pl.BlockSpec((rows_per_step, LAGS, columns), lambda i: (i, 0, 0)),
        cost_estimate=cost,
    )
    if scratch_bytes <= 8 * 1024 * 1024:
        return pl.pallas_call(
            functools.partial(cross_kernel_shifted, segments, rows_per_step),
            scratch_shapes=[
                pltpu.VMEM((rows, segments * columns), jnp.float32),
                pltpu.VMEM((rows_per_step, span, segments * columns), jnp.float32),
            ],
            compiler_params=pltpu.CompilerParams(dimension_semantics=("arbitrary",)),
            **common,
        )(own_flat, ext_flat)
    return pl.pallas_call(
        functools.partial(cross_kernel, segments, rows_per_step), **common
    )(own_flat, ext_flat)


def body(strain, filter_taps):
    extent = lax.axis_size("ta")
    columns_n = lax.axis_size("col")
    position = lax.axis_index("ta")
    section_rows, slab = strain.shape
    block_rows = section_rows // extent
    reach = LAGS // block_rows
    window = 2 * reach
    before = (reach - 1) * block_rows
    turned = strain.T
    padded = jnp.concatenate(
        [
            jnp.zeros((slab, before), strain.dtype),
            turned,
            jnp.zeros((slab, reach * block_rows), strain.dtype),
        ],
        axis=1,
    )
    windows = jnp.stack(
        [padded[:, j * block_rows : (j + window) * block_rows] for j in range(extent)]
    )
    gathered = exchange_time(windows, position, extent)
    samples = gathered.reshape(extent * slab, window * block_rows)
    filtered = decimate_t(samples.astype(jnp.float32), filter_taps)
    whitened = whiten_t(filtered).transpose(2, 0, 1)
    segments, columns = whitened.shape[1:]
    first_of_section = reach - 1 - jnp.minimum(position, reach - 1)
    payload = lax.dynamic_slice_in_dim(whitened, first_of_section * block_rows, reach * block_rows, 0)

    def linear(ta_index, col_index):
        return ta_index * columns_n + col_index

    route = [
        (linear(m, c + 1), linear(extent - reach + m, c))
        for c in range(columns_n - 1)
        for m in range(reach)
    ]
    next_section = lax.ppermute(payload, ("ta", "col"), route)
    local = whitened[before : before + (reach + 1) * block_rows]
    extended = local
    for j in range(extent - reach, extent):
        kept = (extent - j) * block_rows
        candidate = jnp.concatenate(
            [local[:kept], next_section[: (reach + 1) * block_rows - kept]], axis=0
        )
        extended = jnp.where(position == j, candidate, extended)
    own = local[:block_rows]
    return cross_spectra(own, extended)[None]


def solution(mesh):
    return jax.shard_map(
        body,
        mesh=mesh,
        in_specs=(P("col", "ta"), P()),
        out_specs=P("col", "ta", None, None),
        check_vma=False,
    )
```

```python
import functools

import jax
import jax.numpy as jnp
from jax import lax
from jax.experimental import pallas as pl
from jax.experimental.pallas import tpu as pltpu
from jax.sharding import PartitionSpec as P

NFFT = 256
NF = 128
LAGS = 128


def tap_rows(filter_taps, outputs):
    tap_count = filter_taps.shape[0]
    window = 2 * outputs + tap_count
    flipped = filter_taps[::-1]
    period = jnp.concatenate([flipped, jnp.zeros((window + 2 - tap_count,), jnp.float32)])
    repeated = jnp.tile(period, outputs)[: outputs * window]
    return repeated.reshape(outputs, window)


def decimate_t(samples, filter_taps):
    length, channels = samples.shape
    tap_count = filter_taps.shape[0]
    outputs = min(length, NFFT) // 2
    blocks = length // (2 * outputs)
    joined = jnp.concatenate(
        [
            jnp.zeros((tap_count, channels), jnp.float32),
            samples,
            jnp.zeros((2 * outputs - tap_count, channels), jnp.float32),
        ],
        axis=0,
    )
    joined = joined.reshape(blocks + 1, 2 * outputs, channels)
    windows = jnp.concatenate([joined[:-1], joined[1:, :tap_count]], axis=1)
    matrix = tap_rows(filter_taps, outputs)
    result = jnp.einsum("tw,bwc->btc", matrix, windows, precision=lax.Precision.HIGHEST)
    return result.reshape(blocks * outputs, channels).astype(jnp.bfloat16)


def fourier_table():
    moment = lax.broadcasted_iota(jnp.int32, (NFFT, NF), 0)
    frequency = lax.broadcasted_iota(jnp.int32, (NFFT, NF), 1) + 1
    phase_index = moment * frequency % NFFT
    angles = phase_index.astype(jnp.float32) * (2.0 * jnp.pi / NFFT)
    window_taper = 0.5 - 0.5 * jnp.cos(moment.astype(jnp.float32) * (2.0 * jnp.pi / NFFT))
    return jnp.concatenate(
        [window_taper * jnp.cos(angles), -window_taper * jnp.sin(angles)], axis=1
    )


def whiten_t(filtered):
    length, channels = filtered.shape
    pieces = filtered.reshape(length // NF, NF, channels)
    segment_rows = jnp.concatenate([pieces[:-1], pieces[1:]], axis=1)
    spectrum = jnp.einsum(
        "nf,snc->sfc",
        fourier_table(),
        segment_rows.astype(jnp.float32),
        precision=lax.Precision.HIGHEST,
    )
    real_part = spectrum[:, :NF]
    imag_part = spectrum[:, NF:]
    powers = real_part * real_part + imag_part * imag_part
    mean_power = jnp.mean(powers, axis=1, keepdims=True)
    whitening = 1.0 / jnp.sqrt(powers + mean_power + 1e-06)
    return jnp.concatenate([real_part * whitening, imag_part * whitening], axis=1).astype(
        jnp.bfloat16
    )


def windows_kernel(before, after, width, x_ref, out_ref):
    x = x_ref[...].astype(jnp.float32)
    slab = x.shape[0]
    step = (x.shape[1] + before + after - width) // (out_ref.shape[0] - 1)
    padded = jnp.concatenate(
        [jnp.zeros((slab, before), jnp.float32), x, jnp.zeros((slab, after), jnp.float32)], axis=1
    )
    for j in range(out_ref.shape[0]):
        out_ref[j] = padded[:, j * step : j * step + width].astype(out_ref.dtype)


def channel_windows(turned, extent, before, after, width):
    slab, rows = turned.shape
    return pl.pallas_call(
        functools.partial(windows_kernel, before, after, width),
        out_shape=jax.ShapeDtypeStruct((extent, slab, width), turned.dtype),
        cost_estimate=pl.CostEstimate(
            flops=0, transcendentals=0, bytes_accessed=2 * (slab * rows + extent * slab * width)
        ),
    )(turned)


def cross_kernel(segments, rows_per_step, own_ref, ext_ref, out_ref):
    step = pl.program_id(0)
    base = pl.multiple_of(step * rows_per_step, rows_per_step)
    for i in range(rows_per_step):
        acc_re = None
        acc_im = None
        for s in range(segments):
            a = own_ref[pl.ds(base, rows_per_step), pl.ds(s * NFFT, NFFT)]
            a = a.astype(jnp.float32)[i : i + 1]
            window = ext_ref[pl.ds(base, LAGS + rows_per_step), pl.ds(s * NFFT, NFFT)]
            b = window.astype(jnp.float32)[i : i + LAGS]
            terms = product_terms(a, b)
            if acc_re is None:
                acc_re, acc_im = terms
            else:
                acc_re = [x + y for x, y in zip(acc_re, terms[0])]
                acc_im = [x + y for x, y in zip(acc_im, terms[1])]
        store_row(out_ref, i, acc_re, acc_im, segments)


def product_terms(a, b):
    ar = a[:, :NF]
    ai = a[:, NF:]
    br = b[:, :NF]
    bi = b[:, NF:]
    return [ar * br, ai * bi], [ai * br, ar * bi]


def store_row(out_ref, i, acc_re, acc_im, segments):
    re = (acc_re[0] + acc_re[1]) / segments
    im = (acc_im[0] - acc_im[1]) / segments
    out_ref[i, :, :NF] = re.astype(out_ref.dtype)
    out_ref[i, :, NF:] = im.astype(out_ref.dtype)


def cross_kernel_shifted(segments, rows_per_step, own_ref, ext_ref, out_ref, own_f32, shifted):
    step = pl.program_id(0)
    span = shifted.shape[1]

    @pl.when(step == 0)
    def _():
        own_f32[...] = own_ref[...].astype(jnp.float32)
        whole = ext_ref[...].astype(jnp.float32)
        for i in range(rows_per_step):
            shifted[i] = whole[i : i + span]

    base = pl.multiple_of(step * rows_per_step, rows_per_step)
    for i in range(rows_per_step):
        acc_re = None
        acc_im = None
        for s in range(segments):
            a = own_f32[pl.ds(base + i, 1), pl.ds(s * NFFT, NFFT)]
            b = shifted[i, pl.ds(base, LAGS), pl.ds(s * NFFT, NFFT)]
            terms = product_terms(a, b)
            if acc_re is None:
                acc_re, acc_im = terms
            else:
                acc_re = [x + y for x, y in zip(acc_re, terms[0])]
                acc_im = [x + y for x, y in zip(acc_im, terms[1])]
        store_row(out_ref, i, acc_re, acc_im, segments)


def cross_spectra(own, extended):
    rows, segments, columns = own.shape
    reach_rows = extended.shape[0]
    own_flat = own.reshape(rows, segments * columns)
    ext_flat = extended.reshape(reach_rows, segments * columns)
    rows_per_step = 8
    span = reach_rows - rows_per_step
    scratch_bytes = rows_per_step * span * segments * columns * 4
    cost = pl.CostEstimate(
        flops=6 * rows * LAGS * NF * segments,
        transcendentals=0,
        bytes_accessed=rows * LAGS * columns * 2 + 2 * segments * (rows + reach_rows) * columns,
    )
    common = dict(
        out_shape=jax.ShapeDtypeStruct((rows, LAGS, columns), jnp.bfloat16),
        grid=(rows // rows_per_step,),
        in_specs=[
            pl.BlockSpec((rows, segments * columns), lambda i: (0, 0)),
            pl.BlockSpec((reach_rows, segments * columns), lambda i: (0, 0)),
        ],
        out_specs=pl.BlockSpec((rows_per_step, LAGS, columns), lambda i: (i, 0, 0)),
        cost_estimate=cost,
    )
    if scratch_bytes <= 8 * 1024 * 1024:
        return pl.pallas_call(
            functools.partial(cross_kernel_shifted, segments, rows_per_step),
            scratch_shapes=[
                pltpu.VMEM((rows, segments * columns), jnp.float32),
                pltpu.VMEM((rows_per_step, span, segments * columns), jnp.float32),
            ],
            compiler_params=pltpu.CompilerParams(dimension_semantics=("arbitrary",)),
            **common,
        )(own_flat, ext_flat)
    return pl.pallas_call(
        functools.partial(cross_kernel, segments, rows_per_step), **common
    )(own_flat, ext_flat)


def body(strain, filter_taps):
    extent = lax.axis_size("ta")
    columns_n = lax.axis_size("col")
    position = lax.axis_index("ta")
    section_rows, slab = strain.shape
    block_rows = section_rows // extent
    reach = LAGS // block_rows
    window = 2 * reach
    before = (reach - 1) * block_rows
    windows = channel_windows(
        strain.T, extent, before, reach * block_rows, window * block_rows
    )
    gathered = lax.all_to_all(windows, "ta", split_axis=0, concat_axis=0, tiled=True)
    samples = gathered.reshape(extent * slab, window * block_rows)
    filtered = decimate_t(samples.astype(jnp.float32), filter_taps)
    whitened = whiten_t(filtered).transpose(2, 0, 1)
    segments, columns = whitened.shape[1:]
    first_of_section = reach - 1 - jnp.minimum(position, reach - 1)
    payload = lax.dynamic_slice_in_dim(whitened, first_of_section * block_rows, reach * block_rows, 0)

    def linear(ta_index, col_index):
        return ta_index * columns_n + col_index

    route = [
        (linear(m, c + 1), linear(extent - reach + m, c))
        for c in range(columns_n - 1)
        for m in range(reach)
    ]
    next_section = lax.ppermute(payload, ("ta", "col"), route)
    local = whitened[before : before + (reach + 1) * block_rows]
    extended = local
    for j in range(extent - reach, extent):
        kept = (extent - j) * block_rows
        candidate = jnp.concatenate(
            [local[:kept], next_section[: (reach + 1) * block_rows - kept]], axis=0
        )
        extended = jnp.where(position == j, candidate, extended)
    own = local[:block_rows]
    return cross_spectra(own, extended)[None]


def solution(mesh):
    return jax.shard_map(
        body,
        mesh=mesh,
        in_specs=(P("col", "ta"), P()),
        out_specs=P("col", "ta", None, None),
        check_vma=False,
    )
```

```python
import functools

import jax
import jax.numpy as jnp
from jax import lax
from jax.experimental import pallas as pl
from jax.experimental.pallas import tpu as pltpu
from jax.sharding import PartitionSpec as P

NFFT = 256
NF = 128
LAGS = 128


def tap_rows(filter_taps, outputs):
    tap_count = filter_taps.shape[0]
    window = 2 * outputs + tap_count
    flipped = filter_taps[::-1]
    period = jnp.concatenate([flipped, jnp.zeros((window + 2 - tap_count,), jnp.float32)])
    repeated = jnp.tile(period, outputs)[: outputs * window]
    return repeated.reshape(outputs, window)


def decimate_t(samples, filter_taps):
    length, channels = samples.shape
    tap_count = filter_taps.shape[0]
    outputs = min(length, NFFT) // 2
    blocks = length // (2 * outputs)
    joined = jnp.concatenate(
        [
            jnp.zeros((tap_count, channels), jnp.float32),
            samples,
            jnp.zeros((2 * outputs - tap_count, channels), jnp.float32),
        ],
        axis=0,
    )
    joined = joined.reshape(blocks + 1, 2 * outputs, channels)
    windows = jnp.concatenate([joined[:-1], joined[1:, :tap_count]], axis=1)
    matrix = tap_rows(filter_taps, outputs)
    result = jnp.einsum("tw,bwc->btc", matrix, windows, precision=lax.Precision.HIGHEST)
    return result.reshape(blocks * outputs, channels).astype(jnp.bfloat16)


def fourier_table():
    moment = lax.broadcasted_iota(jnp.int32, (NFFT, NF), 0)
    frequency = lax.broadcasted_iota(jnp.int32, (NFFT, NF), 1) + 1
    phase_index = moment * frequency % NFFT
    angles = phase_index.astype(jnp.float32) * (2.0 * jnp.pi / NFFT)
    window_taper = 0.5 - 0.5 * jnp.cos(moment.astype(jnp.float32) * (2.0 * jnp.pi / NFFT))
    return jnp.concatenate(
        [window_taper * jnp.cos(angles), -window_taper * jnp.sin(angles)], axis=1
    )


def whiten_t(filtered):
    length, channels = filtered.shape
    pieces = filtered.reshape(length // NF, NF, channels)
    segment_rows = jnp.concatenate([pieces[:-1], pieces[1:]], axis=1)
    spectrum = jnp.einsum(
        "nf,snc->sfc",
        fourier_table(),
        segment_rows.astype(jnp.float32),
        precision=lax.Precision.HIGHEST,
    )
    real_part = spectrum[:, :NF]
    imag_part = spectrum[:, NF:]
    powers = real_part * real_part + imag_part * imag_part
    mean_power = jnp.mean(powers, axis=1, keepdims=True)
    whitening = 1.0 / jnp.sqrt(powers + mean_power + 1e-06)
    return jnp.concatenate([real_part * whitening, imag_part * whitening], axis=1).astype(
        jnp.bfloat16
    )


def windows_kernel(before, after, width, x_ref, out_ref):
    x = x_ref[...].astype(jnp.float32)
    slab = x.shape[0]
    step = (x.shape[1] + before + after - width) // (out_ref.shape[0] - 1)
    padded = jnp.concatenate(
        [jnp.zeros((slab, before), jnp.float32), x, jnp.zeros((slab, after), jnp.float32)], axis=1
    )
    for j in range(out_ref.shape[0]):
        out_ref[j] = padded[:, j * step : j * step + width].astype(out_ref.dtype)


def channel_windows(turned, extent, before, after, width):
    slab, rows = turned.shape
    return pl.pallas_call(
        functools.partial(windows_kernel, before, after, width),
        out_shape=jax.ShapeDtypeStruct((extent, slab, width), turned.dtype),
        cost_estimate=pl.CostEstimate(
            flops=0, transcendentals=0, bytes_accessed=2 * (slab * rows + extent * slab * width)
        ),
    )(turned)


def cross_kernel(segments, rows_per_step, own_ref, ext_ref, out_ref):
    step = pl.program_id(0)
    base = pl.multiple_of(step * rows_per_step, rows_per_step)
    for i in range(rows_per_step):
        acc_re = None
        acc_im = None
        for s in range(segments):
            a = own_ref[pl.ds(base, rows_per_step), pl.ds(s * NFFT, NFFT)]
            a = a.astype(jnp.float32)[i : i + 1]
            window = ext_ref[pl.ds(base, LAGS + rows_per_step), pl.ds(s * NFFT, NFFT)]
            b = window.astype(jnp.float32)[i : i + LAGS]
            terms = product_terms(a, b)
            if acc_re is None:
                acc_re, acc_im = terms
            else:
                acc_re = [x + y for x, y in zip(acc_re, terms[0])]
                acc_im = [x + y for x, y in zip(acc_im, terms[1])]
        store_row(out_ref, i, acc_re, acc_im, segments)


def product_terms(a, b):
    ar = a[:, :NF]
    ai = a[:, NF:]
    br = b[:, :NF]
    bi = b[:, NF:]
    return [ar * br, ai * bi], [ai * br, ar * bi]


def store_row(out_ref, i, acc_re, acc_im, segments):
    re = (acc_re[0] + acc_re[1]) / segments
    im = (acc_im[0] - acc_im[1]) / segments
    out_ref[i, :, :NF] = re.astype(out_ref.dtype)
    out_ref[i, :, NF:] = im.astype(out_ref.dtype)


def cross_kernel_shifted(segments, rows_per_step, own_ref, ext_ref, out_ref, own_f32, shifted):
    step = pl.program_id(0)
    span = shifted.shape[1]

    @pl.when(step == 0)
    def _():
        own_f32[...] = own_ref[...].astype(jnp.float32)
        whole = ext_ref[...].astype(jnp.float32)
        for i in range(rows_per_step):
            shifted[i] = whole[i : i + span]

    base = pl.multiple_of(step * rows_per_step, rows_per_step)
    for i in range(rows_per_step):
        acc_re = None
        acc_im = None
        for s in range(segments):
            a = own_f32[pl.ds(base + i, 1), pl.ds(s * NFFT, NFFT)]
            b = shifted[i, pl.ds(base, LAGS), pl.ds(s * NFFT, NFFT)]
            terms = product_terms(a, b)
            if acc_re is None:
                acc_re, acc_im = terms
            else:
                acc_re = [x + y for x, y in zip(acc_re, terms[0])]
                acc_im = [x + y for x, y in zip(acc_im, terms[1])]
        store_row(out_ref, i, acc_re, acc_im, segments)


def cross_kernel_direct(segments, rows, reach, extent, before, chunk,
                        pos_ref, win_ref, next_ref, out_hbm, own_f32, shifted, buffers, sems):
    span = shifted.shape[1]
    position = pos_ref[0]
    own_f32[...] = win_ref[before : before + rows].astype(jnp.float32)
    local = win_ref[before : before + (reach + 1) * rows].astype(jnp.float32)
    following = next_ref[...].astype(jnp.float32)
    extended = local
    for j in range(extent - reach, extent):
        kept = (extent - j) * rows
        candidate = jnp.concatenate([local[:kept], following[: (reach + 1) * rows - kept]], axis=0)
        extended = jnp.where(position == j, candidate, extended)
    for i in range(chunk):
        shifted[i] = extended[i : i + span]
    copies = []
    for m in range(rows // chunk):
        slot = m % 2
        if m >= 2:
            copies[m - 2].wait()
        base = m * chunk
        for i in range(chunk):
            acc_re = None
            acc_im = None
            for s in range(segments):
                a = own_f32[base + i : base + i + 1, s * NFFT : (s + 1) * NFFT]
                b = shifted[i, base : base + LAGS, s * NFFT : (s + 1) * NFFT]
                terms = product_terms(a, b)
                if acc_re is None:
                    acc_re, acc_im = terms
                else:
                    acc_re = [x + y for x, y in zip(acc_re, terms[0])]
                    acc_im = [x + y for x, y in zip(acc_im, terms[1])]
            store_row(buffers.at[slot], i, acc_re, acc_im, segments)
        copy = pltpu.make_async_copy(
            buffers.at[slot], out_hbm.at[pl.ds(base, chunk)], sems.at[slot]
        )
        copy.start()
        copies.append(copy)
    for copy in copies[-2:]:
        copy.wait()


def cross_spectra_direct(whitened, following, position, rows, reach, extent, before):
    window_rows, segments, columns = whitened.shape
    chunk = 8
    reach_rows = (reach + 1) * rows
    span = reach_rows - chunk
    width = segments * columns
    return pl.pallas_call(
        functools.partial(cross_kernel_direct, segments, rows, reach, extent, before, chunk),
        out_shape=jax.ShapeDtypeStruct((rows, LAGS, columns), jnp.bfloat16),
        in_specs=[
            pl.BlockSpec(memory_space=pltpu.SMEM),
            pl.BlockSpec(memory_space=pltpu.VMEM),
            pl.BlockSpec(memory_space=pltpu.VMEM),
        ],
        out_specs=pl.BlockSpec(memory_space=pl.ANY),
        scratch_shapes=[
            pltpu.VMEM((rows, width), jnp.float32),
            pltpu.VMEM((chunk, span, width), jnp.float32),
            pltpu.VMEM((2, chunk, LAGS, columns), jnp.bfloat16),
            pltpu.SemaphoreType.DMA((2,)),
        ],
        cost_estimate=pl.CostEstimate(
            flops=6 * rows * LAGS * NF * segments,
            transcendentals=0,
            bytes_accessed=rows * LAGS * columns * 2 + 2 * (window_rows + following.shape[0]) * width,
        ),
    )(
        position.reshape(1).astype(jnp.int32),
        whitened.reshape(window_rows, width),
        following.reshape(following.shape[0], width),
    )


def cross_spectra(own, extended):
    rows, segments, columns = own.shape
    reach_rows = extended.shape[0]
    own_flat = own.reshape(rows, segments * columns)
    ext_flat = extended.reshape(reach_rows, segments * columns)
    rows_per_step = 8
    span = reach_rows - rows_per_step
    scratch_bytes = rows_per_step * span * segments * columns * 4
    cost = pl.CostEstimate(
        flops=6 * rows * LAGS * NF * segments,
        transcendentals=0,
        bytes_accessed=rows * LAGS * columns * 2 + 2 * segments * (rows + reach_rows) * columns,
    )
    common = dict(
        out_shape=jax.ShapeDtypeStruct((rows, LAGS, columns), jnp.bfloat16),
        grid=(rows // rows_per_step,),
        in_specs=[
            pl.BlockSpec((rows, segments * columns), lambda i: (0, 0)),
            pl.BlockSpec((reach_rows, segments * columns), lambda i: (0, 0)),
        ],
        out_specs=pl.BlockSpec((rows_per_step, LAGS, columns), lambda i: (i, 0, 0)),
        cost_estimate=cost,
    )
    if scratch_bytes <= 8 * 1024 * 1024:
        return pl.pallas_call(
            functools.partial(cross_kernel_shifted, segments, rows_per_step),
            scratch_shapes=[
                pltpu.VMEM((rows, segments * columns), jnp.float32),
                pltpu.VMEM((rows_per_step, span, segments * columns), jnp.float32),
            ],
            compiler_params=pltpu.CompilerParams(dimension_semantics=("arbitrary",)),
            **common,
        )(own_flat, ext_flat)
    return pl.pallas_call(
        functools.partial(cross_kernel, segments, rows_per_step), **common
    )(own_flat, ext_flat)


def body(strain, filter_taps):
    extent = lax.axis_size("ta")
    columns_n = lax.axis_size("col")
    position = lax.axis_index("ta")
    section_rows, slab = strain.shape
    block_rows = section_rows // extent
    reach = LAGS // block_rows
    window = 2 * reach
    before = (reach - 1) * block_rows
    windows = channel_windows(
        strain.T, extent, before, reach * block_rows, window * block_rows
    )
    gathered = lax.all_to_all(windows, "ta", split_axis=0, concat_axis=0, tiled=True)
    samples = gathered.reshape(extent * slab, window * block_rows)
    filtered = decimate_t(samples.astype(jnp.float32), filter_taps)
    whitened = whiten_t(filtered).transpose(2, 0, 1)
    segments, columns = whitened.shape[1:]
    first_of_section = reach - 1 - jnp.minimum(position, reach - 1)
    payload = lax.dynamic_slice_in_dim(whitened, first_of_section * block_rows, reach * block_rows, 0)

    def linear(ta_index, col_index):
        return ta_index * columns_n + col_index

    route = [
        (linear(m, c + 1), linear(extent - reach + m, c))
        for c in range(columns_n - 1)
        for m in range(reach)
    ]
    next_section = lax.ppermute(payload, ("ta", "col"), route)
    if segments * 8 * (reach + 1) * block_rows * columns * 4 <= 8 * 1024 * 1024:
        return cross_spectra_direct(
            whitened, next_section, position, block_rows, reach, extent, before
        )[None]
    local = whitened[before : before + (reach + 1) * block_rows]
    extended = local
    for j in range(extent - reach, extent):
        kept = (extent - j) * block_rows
        candidate = jnp.concatenate(
            [local[:kept], next_section[: (reach + 1) * block_rows - kept]], axis=0
        )
        extended = jnp.where(position == j, candidate, extended)
    own = local[:block_rows]
    return cross_spectra(own, extended)[None]


def solution(mesh):
    return jax.shard_map(
        body,
        mesh=mesh,
        in_specs=(P("col", "ta"), P()),
        out_specs=P("col", "ta", None, None),
        check_vma=False,
    )
```

```python
import functools

import jax
import jax.numpy as jnp
from jax import lax
from jax.experimental import pallas as pl
from jax.experimental.pallas import tpu as pltpu
from jax.sharding import PartitionSpec as P

NFFT = 256
NF = 128
LAGS = 128


def tap_rows(filter_taps, outputs):
    tap_count = filter_taps.shape[0]
    window = 2 * outputs + tap_count
    flipped = filter_taps[::-1]
    period = jnp.concatenate([flipped, jnp.zeros((window + 2 - tap_count,), jnp.float32)])
    repeated = jnp.tile(period, outputs)[: outputs * window]
    return repeated.reshape(outputs, window)


def decimate_t(samples, filter_taps):
    length, channels = samples.shape
    tap_count = filter_taps.shape[0]
    outputs = min(length, NFFT) // 2
    blocks = length // (2 * outputs)
    joined = jnp.concatenate(
        [
            jnp.zeros((tap_count, channels), jnp.float32),
            samples,
            jnp.zeros((2 * outputs - tap_count, channels), jnp.float32),
        ],
        axis=0,
    )
    joined = joined.reshape(blocks + 1, 2 * outputs, channels)
    windows = jnp.concatenate([joined[:-1], joined[1:, :tap_count]], axis=1)
    matrix = tap_rows(filter_taps, outputs)
    result = jnp.einsum("tw,bwc->btc", matrix, windows, precision=lax.Precision.HIGHEST)
    return result.reshape(blocks * outputs, channels).astype(jnp.bfloat16)


def fourier_table():
    moment = lax.broadcasted_iota(jnp.int32, (NFFT, NF), 0)
    frequency = lax.broadcasted_iota(jnp.int32, (NFFT, NF), 1) + 1
    phase_index = moment * frequency % NFFT
    angles = phase_index.astype(jnp.float32) * (2.0 * jnp.pi / NFFT)
    window_taper = 0.5 - 0.5 * jnp.cos(moment.astype(jnp.float32) * (2.0 * jnp.pi / NFFT))
    return jnp.concatenate(
        [window_taper * jnp.cos(angles), -window_taper * jnp.sin(angles)], axis=1
    )


def whiten_t(filtered):
    length, channels = filtered.shape
    pieces = filtered.reshape(length // NF, NF, channels)
    segment_rows = jnp.concatenate([pieces[:-1], pieces[1:]], axis=1)
    spectrum = jnp.einsum(
        "nf,snc->sfc",
        fourier_table(),
        segment_rows.astype(jnp.float32),
        precision=lax.Precision.HIGHEST,
    )
    real_part = spectrum[:, :NF]
    imag_part = spectrum[:, NF:]
    powers = real_part * real_part + imag_part * imag_part
    mean_power = jnp.mean(powers, axis=1, keepdims=True)
    whitening = 1.0 / jnp.sqrt(powers + mean_power + 1e-06)
    return jnp.concatenate([real_part * whitening, imag_part * whitening], axis=1).astype(
        jnp.bfloat16
    )


def windows_kernel(before, after, width, x_ref, out_ref):
    x = x_ref[...].astype(jnp.float32)
    slab = x.shape[0]
    step = (x.shape[1] + before + after - width) // (out_ref.shape[0] - 1)
    padded = jnp.concatenate(
        [jnp.zeros((slab, before), jnp.float32), x, jnp.zeros((slab, after), jnp.float32)], axis=1
    )
    for j in range(out_ref.shape[0]):
        out_ref[j] = padded[:, j * step : j * step + width].astype(out_ref.dtype)


def channel_windows(turned, extent, before, after, width):
    slab, rows = turned.shape
    return pl.pallas_call(
        functools.partial(windows_kernel, before, after, width),
        out_shape=jax.ShapeDtypeStruct((extent, slab, width), turned.dtype),
        cost_estimate=pl.CostEstimate(
            flops=0, transcendentals=0, bytes_accessed=2 * (slab * rows + extent * slab * width)
        ),
    )(turned)


def cross_kernel(segments, rows_per_step, own_ref, ext_ref, out_ref):
    step = pl.program_id(0)
    base = pl.multiple_of(step * rows_per_step, rows_per_step)
    for i in range(rows_per_step):
        acc_re = None
        acc_im = None
        for s in range(segments):
            a = own_ref[pl.ds(base, rows_per_step), pl.ds(s * NFFT, NFFT)]
            a = a.astype(jnp.float32)[i : i + 1]
            window = ext_ref[pl.ds(base, LAGS + rows_per_step), pl.ds(s * NFFT, NFFT)]
            b = window.astype(jnp.float32)[i : i + LAGS]
            terms = product_terms(a, b)
            if acc_re is None:
                acc_re, acc_im = terms
            else:
                acc_re = [x + y for x, y in zip(acc_re, terms[0])]
                acc_im = [x + y for x, y in zip(acc_im, terms[1])]
        store_row(out_ref, i, acc_re, acc_im, segments)


def product_terms(a, b):
    ar = a[:, :NF]
    ai = a[:, NF:]
    br = b[:, :NF]
    bi = b[:, NF:]
    return [ar * br, ai * bi], [ai * br, ar * bi]


def store_row(out_ref, i, acc_re, acc_im, segments):
    re = acc_re[0] + acc_re[1]
    im = acc_im[0] - acc_im[1]
    if segments > 1:
        re = re / segments
        im = im / segments
    out_ref[i, :, :NF] = re.astype(out_ref.dtype)
    out_ref[i, :, NF:] = im.astype(out_ref.dtype)


def cross_kernel_shifted(segments, rows_per_step, own_ref, ext_ref, out_ref, own_f32, shifted):
    step = pl.program_id(0)
    span = shifted.shape[1]

    @pl.when(step == 0)
    def _():
        own_f32[...] = own_ref[...].astype(jnp.float32)
        whole = ext_ref[...].astype(jnp.float32)
        for i in range(rows_per_step):
            shifted[i] = whole[i : i + span]

    base = pl.multiple_of(step * rows_per_step, rows_per_step)
    for i in range(rows_per_step):
        acc_re = None
        acc_im = None
        for s in range(segments):
            a = own_f32[pl.ds(base + i, 1), pl.ds(s * NFFT, NFFT)]
            b = shifted[i, pl.ds(base, LAGS), pl.ds(s * NFFT, NFFT)]
            terms = product_terms(a, b)
            if acc_re is None:
                acc_re, acc_im = terms
            else:
                acc_re = [x + y for x, y in zip(acc_re, terms[0])]
                acc_im = [x + y for x, y in zip(acc_im, terms[1])]
        store_row(out_ref, i, acc_re, acc_im, segments)


def cross_kernel_direct(segments, rows, reach, extent, before, chunk,
                        pos_ref, win_ref, next_hbm, out_hbm, own_f32, shifted, following,
                        buffers, sems, next_sem):
    fetch = pltpu.make_async_copy(next_hbm, following, next_sem)
    fetch.start()
    span = shifted.shape[1]
    position = pos_ref[0]
    width = (reach + 1) * rows
    local = jnp.concatenate(
        [
            win_ref[s * NFFT : (s + 1) * NFFT, before : before + width].astype(jnp.float32).T
            for s in range(segments)
        ],
        axis=1,
    )
    own_f32[...] = local[:rows]
    fetch.wait()
    arrived = jnp.concatenate(
        [following[s * NFFT : (s + 1) * NFFT, :].astype(jnp.float32).T for s in range(segments)],
        axis=1,
    )
    extended = local
    for j in range(extent - reach, extent):
        kept = (extent - j) * rows
        candidate = jnp.concatenate([local[:kept], arrived[: width - kept]], axis=0)
        extended = jnp.where(position == j, candidate, extended)
    for i in range(chunk):
        shifted[i] = extended[i : i + span]
    copies = []
    for m in range(rows // chunk):
        slot = m % 2
        if m >= 2:
            copies[m - 2].wait()
        base = m * chunk
        for i in range(chunk):
            acc_re = None
            acc_im = None
            for s in range(segments):
                a = own_f32[base + i : base + i + 1, s * NFFT : (s + 1) * NFFT]
                b = shifted[i, base : base + LAGS, s * NFFT : (s + 1) * NFFT]
                terms = product_terms(a, b)
                if acc_re is None:
                    acc_re, acc_im = terms
                else:
                    acc_re = [x + y for x, y in zip(acc_re, terms[0])]
                    acc_im = [x + y for x, y in zip(acc_im, terms[1])]
            store_row(buffers.at[slot], i, acc_re, acc_im, segments)
        copy = pltpu.make_async_copy(
            buffers.at[slot], out_hbm.at[pl.ds(base, chunk)], sems.at[slot]
        )
        copy.start()
        copies.append(copy)
    for copy in copies[-2:]:
        copy.wait()


def cross_spectra_direct(whitened_t, following_t, position, rows, reach, extent, before):
    width, window_rows = whitened_t.shape
    segments = width // NFFT
    chunk = 8
    reach_rows = (reach + 1) * rows
    span = reach_rows - chunk
    return pl.pallas_call(
        functools.partial(cross_kernel_direct, segments, rows, reach, extent, before, chunk),
        out_shape=jax.ShapeDtypeStruct((rows, LAGS, NFFT), jnp.bfloat16),
        in_specs=[
            pl.BlockSpec(memory_space=pltpu.SMEM),
            pl.BlockSpec(memory_space=pltpu.VMEM),
            pl.BlockSpec(memory_space=pl.ANY),
        ],
        out_specs=pl.BlockSpec(memory_space=pl.ANY),
        scratch_shapes=[
            pltpu.VMEM((rows, width), jnp.float32),
            pltpu.VMEM((chunk, span, width), jnp.float32),
            pltpu.VMEM(following_t.shape, following_t.dtype),
            pltpu.VMEM((2, chunk, LAGS, NFFT), jnp.bfloat16),
            pltpu.SemaphoreType.DMA((2,)),
            pltpu.SemaphoreType.DMA(()),
        ],
        cost_estimate=pl.CostEstimate(
            flops=6 * rows * LAGS * NF * segments,
            transcendentals=0,
            bytes_accessed=rows * LAGS * NFFT * 2 + 2 * (window_rows + following_t.shape[1]) * width,
        ),
    )(position.reshape(1).astype(jnp.int32), whitened_t, following_t)


def cross_spectra(own, extended):
    rows, segments, columns = own.shape
    reach_rows = extended.shape[0]
    own_flat = own.reshape(rows, segments * columns)
    ext_flat = extended.reshape(reach_rows, segments * columns)
    rows_per_step = 8
    span = reach_rows - rows_per_step
    scratch_bytes = rows_per_step * span * segments * columns * 4
    cost = pl.CostEstimate(
        flops=6 * rows * LAGS * NF * segments,
        transcendentals=0,
        bytes_accessed=rows * LAGS * columns * 2 + 2 * segments * (rows + reach_rows) * columns,
    )
    common = dict(
        out_shape=jax.ShapeDtypeStruct((rows, LAGS, columns), jnp.bfloat16),
        grid=(rows // rows_per_step,),
        in_specs=[
            pl.BlockSpec((rows, segments * columns), lambda i: (0, 0)),
            pl.BlockSpec((reach_rows, segments * columns), lambda i: (0, 0)),
        ],
        out_specs=pl.BlockSpec((rows_per_step, LAGS, columns), lambda i: (i, 0, 0)),
        cost_estimate=cost,
    )
    if scratch_bytes <= 8 * 1024 * 1024:
        return pl.pallas_call(
            functools.partial(cross_kernel_shifted, segments, rows_per_step),
            scratch_shapes=[
                pltpu.VMEM((rows, segments * columns), jnp.float32),
                pltpu.VMEM((rows_per_step, span, segments * columns), jnp.float32),
            ],
            compiler_params=pltpu.CompilerParams(dimension_semantics=("arbitrary",)),
            **common,
        )(own_flat, ext_flat)
    return pl.pallas_call(
        functools.partial(cross_kernel, segments, rows_per_step), **common
    )(own_flat, ext_flat)


def body(strain, filter_taps):
    extent = lax.axis_size("ta")
    columns_n = lax.axis_size("col")
    position = lax.axis_index("ta")
    section_rows, slab = strain.shape
    block_rows = section_rows // extent
    reach = LAGS // block_rows
    window = 2 * reach
    before = (reach - 1) * block_rows
    windows = channel_windows(
        strain.T, extent, before, reach * block_rows, window * block_rows
    )
    gathered = lax.all_to_all(windows, "ta", split_axis=0, concat_axis=0, tiled=True)
    samples = gathered.reshape(extent * slab, window * block_rows)
    filtered = decimate_t(samples.astype(jnp.float32), filter_taps)
    whitened_t = whiten_t(filtered)
    segments, columns, window_rows = whitened_t.shape
    first_of_section = reach - 1 - jnp.minimum(position, reach - 1)

    def linear(ta_index, col_index):
        return ta_index * columns_n + col_index

    route = [
        (linear(m, c + 1), linear(extent - reach + m, c))
        for c in range(columns_n - 1)
        for m in range(reach)
    ]
    if segments * 8 * (reach + 1) * block_rows * columns * 4 <= 8 * 1024 * 1024:
        flat = whitened_t.reshape(segments * columns, window_rows)
        payload = lax.dynamic_slice_in_dim(flat, first_of_section * block_rows, reach * block_rows, 1)
        next_section = lax.ppermute(payload, ("ta", "col"), route)
        return cross_spectra_direct(
            flat, next_section, position, block_rows, reach, extent, before
        )[None]
    whitened = whitened_t.transpose(2, 0, 1)
    payload = lax.dynamic_slice_in_dim(whitened, first_of_section * block_rows, reach * block_rows, 0)
    next_section = lax.ppermute(payload, ("ta", "col"), route)
    local = whitened[before : before + (reach + 1) * block_rows]
    extended = local
    for j in range(extent - reach, extent):
        kept = (extent - j) * block_rows
        candidate = jnp.concatenate(
            [local[:kept], next_section[: (reach + 1) * block_rows - kept]], axis=0
        )
        extended = jnp.where(position == j, candidate, extended)
    own = local[:block_rows]
    return cross_spectra(own, extended)[None]


def solution(mesh):
    return jax.shard_map(
        body,
        mesh=mesh,
        in_specs=(P("col", "ta"), P()),
        out_specs=P("col", "ta", None, None),
        check_vma=False,
    )
```

```python
import functools

import jax
import jax.numpy as jnp
from jax import lax
from jax.experimental import pallas as pl
from jax.experimental.pallas import tpu as pltpu
from jax.sharding import PartitionSpec as P

NFFT = 256
NF = 128
LAGS = 128


def tap_rows(filter_taps, outputs):
    tap_count = filter_taps.shape[0]
    window = 2 * outputs + tap_count
    flipped = filter_taps[::-1]
    period = jnp.concatenate([flipped, jnp.zeros((window + 2 - tap_count,), jnp.float32)])
    repeated = jnp.tile(period, outputs)[: outputs * window]
    return repeated.reshape(outputs, window)


def decimate_t(samples, filter_taps):
    length, channels = samples.shape
    tap_count = filter_taps.shape[0]
    outputs = min(length, NFFT) // 2
    blocks = length // (2 * outputs)
    joined = jnp.concatenate(
        [
            jnp.zeros((tap_count, channels), jnp.float32),
            samples,
            jnp.zeros((2 * outputs - tap_count, channels), jnp.float32),
        ],
        axis=0,
    )
    joined = joined.reshape(blocks + 1, 2 * outputs, channels)
    windows = jnp.concatenate([joined[:-1], joined[1:, :tap_count]], axis=1)
    matrix = tap_rows(filter_taps, outputs)
    result = jnp.einsum("tw,bwc->btc", matrix, windows, precision=lax.Precision.HIGHEST)
    return result.reshape(blocks * outputs, channels).astype(jnp.bfloat16)


def fourier_table():
    moment = lax.broadcasted_iota(jnp.int32, (NFFT, NF), 0)
    frequency = lax.broadcasted_iota(jnp.int32, (NFFT, NF), 1) + 1
    phase_index = moment * frequency % NFFT
    angles = phase_index.astype(jnp.float32) * (2.0 * jnp.pi / NFFT)
    window_taper = 0.5 - 0.5 * jnp.cos(moment.astype(jnp.float32) * (2.0 * jnp.pi / NFFT))
    return jnp.concatenate(
        [window_taper * jnp.cos(angles), -window_taper * jnp.sin(angles)], axis=1
    )


def whiten_t(filtered):
    length, channels = filtered.shape
    pieces = filtered.reshape(length // NF, NF, channels)
    segment_rows = jnp.concatenate([pieces[:-1], pieces[1:]], axis=1)
    spectrum = jnp.einsum(
        "nf,snc->sfc",
        fourier_table(),
        segment_rows.astype(jnp.float32),
        precision=lax.Precision.HIGHEST,
    )
    real_part = spectrum[:, :NF]
    imag_part = spectrum[:, NF:]
    powers = real_part * real_part + imag_part * imag_part
    mean_power = jnp.mean(powers, axis=1, keepdims=True)
    whitening = 1.0 / jnp.sqrt(powers + mean_power + 1e-06)
    return jnp.concatenate([real_part * whitening, imag_part * whitening], axis=1).astype(
        jnp.bfloat16
    )


def windows_kernel(before, after, width, x_ref, out_ref):
    x = x_ref[...].astype(jnp.float32)
    slab = x.shape[0]
    step = (x.shape[1] + before + after - width) // (out_ref.shape[0] - 1)
    padded = jnp.concatenate(
        [jnp.zeros((slab, before), jnp.float32), x, jnp.zeros((slab, after), jnp.float32)], axis=1
    )
    for j in range(out_ref.shape[0]):
        out_ref[j] = padded[:, j * step : j * step + width].astype(out_ref.dtype)


def channel_windows(turned, extent, before, after, width):
    slab, rows = turned.shape
    return pl.pallas_call(
        functools.partial(windows_kernel, before, after, width),
        out_shape=jax.ShapeDtypeStruct((extent, slab, width), turned.dtype),
        cost_estimate=pl.CostEstimate(
            flops=0, transcendentals=0, bytes_accessed=2 * (slab * rows + extent * slab * width)
        ),
    )(turned)


def cross_kernel(segments, rows_per_step, own_ref, ext_ref, out_ref):
    step = pl.program_id(0)
    base = pl.multiple_of(step * rows_per_step, rows_per_step)
    for i in range(rows_per_step):
        acc_re = None
        acc_im = None
        for s in range(segments):
            a = own_ref[pl.ds(base, rows_per_step), pl.ds(s * NFFT, NFFT)]
            a = a.astype(jnp.float32)[i : i + 1]
            window = ext_ref[pl.ds(base, LAGS + rows_per_step), pl.ds(s * NFFT, NFFT)]
            b = window.astype(jnp.float32)[i : i + LAGS]
            terms = product_terms(a, b)
            if acc_re is None:
                acc_re, acc_im = terms
            else:
                acc_re = [x + y for x, y in zip(acc_re, terms[0])]
                acc_im = [x + y for x, y in zip(acc_im, terms[1])]
        store_row(out_ref, i, acc_re, acc_im, segments)


def product_terms(a, b):
    ar = a[:, :NF]
    ai = a[:, NF:]
    br = b[:, :NF]
    bi = b[:, NF:]
    return [ar * br, ai * bi], [ai * br, ar * bi]


def store_row(out_ref, i, acc_re, acc_im, segments):
    re = acc_re[0] + acc_re[1]
    im = acc_im[0] - acc_im[1]
    if segments > 1:
        re = re / segments
        im = im / segments
    out_ref[i, :, :NF] = re.astype(out_ref.dtype)
    out_ref[i, :, NF:] = im.astype(out_ref.dtype)


def cross_kernel_shifted(segments, rows_per_step, own_ref, ext_ref, out_ref, own_f32, shifted):
    step = pl.program_id(0)
    span = shifted.shape[1]

    @pl.when(step == 0)
    def _():
        own_f32[...] = own_ref[...].astype(jnp.float32)
        whole = ext_ref[...].astype(jnp.float32)
        for i in range(rows_per_step):
            shifted[i] = whole[i : i + span]

    base = pl.multiple_of(step * rows_per_step, rows_per_step)
    for i in range(rows_per_step):
        acc_re = None
        acc_im = None
        for s in range(segments):
            a = own_f32[pl.ds(base + i, 1), pl.ds(s * NFFT, NFFT)]
            b = shifted[i, pl.ds(base, LAGS), pl.ds(s * NFFT, NFFT)]
            terms = product_terms(a, b)
            if acc_re is None:
                acc_re, acc_im = terms
            else:
                acc_re = [x + y for x, y in zip(acc_re, terms[0])]
                acc_im = [x + y for x, y in zip(acc_im, terms[1])]
        store_row(out_ref, i, acc_re, acc_im, segments)


def cross_kernel_direct(segments, rows, reach, extent, before, chunk,
                        pos_ref, win_ref, next_hbm, out_hbm, own_f32, shifted, following,
                        buffers, sems, next_sem):
    fetch = pltpu.make_async_copy(next_hbm, following, next_sem)
    fetch.start()
    span = shifted.shape[1]
    position = pos_ref[0]
    width = (reach + 1) * rows
    local = jnp.concatenate(
        [
            win_ref[s * NFFT : (s + 1) * NFFT, before : before + width].astype(jnp.float32).T
            for s in range(segments)
        ],
        axis=1,
    )
    own_f32[...] = local[:rows]
    fetch.wait()
    arrived = jnp.concatenate(
        [following[s * NFFT : (s + 1) * NFFT, :].astype(jnp.float32).T for s in range(segments)],
        axis=1,
    )
    extended = local
    for j in range(extent - reach, extent):
        kept = (extent - j) * rows
        candidate = jnp.concatenate([local[:kept], arrived[: width - kept]], axis=0)
        extended = jnp.where(position == j, candidate, extended)
    for i in range(chunk):
        shifted[i] = extended[i : i + span]
    slots, parts = buffers.shape[0], sems.shape[1]
    part = chunk // parts
    copies = []
    for m in range(rows // chunk):
        slot = m % slots
        if m >= slots:
            for copy in copies[m - slots]:
                copy.wait()
        base = m * chunk
        for i in range(chunk):
            acc_re = None
            acc_im = None
            for s in range(segments):
                a = own_f32[base + i : base + i + 1, s * NFFT : (s + 1) * NFFT]
                b = shifted[i, base : base + LAGS, s * NFFT : (s + 1) * NFFT]
                terms = product_terms(a, b)
                if acc_re is None:
                    acc_re, acc_im = terms
                else:
                    acc_re = [x + y for x, y in zip(acc_re, terms[0])]
                    acc_im = [x + y for x, y in zip(acc_im, terms[1])]
            store_row(buffers.at[slot], i, acc_re, acc_im, segments)
        group = []
        for p in range(parts):
            copy = pltpu.make_async_copy(
                buffers.at[slot, pl.ds(p * part, part)],
                out_hbm.at[pl.ds(base + p * part, part)],
                sems.at[slot, p],
            )
            copy.start()
            group.append(copy)
        copies.append(group)
    for group in copies[-slots:]:
        for copy in group:
            copy.wait()


def cross_spectra_direct(whitened_t, following_t, position, rows, reach, extent, before):
    width, window_rows = whitened_t.shape
    segments = width // NFFT
    chunk = 8
    reach_rows = (reach + 1) * rows
    span = reach_rows - chunk
    return pl.pallas_call(
        functools.partial(cross_kernel_direct, segments, rows, reach, extent, before, chunk),
        out_shape=jax.ShapeDtypeStruct((rows, LAGS, NFFT), jnp.bfloat16),
        in_specs=[
            pl.BlockSpec(memory_space=pltpu.SMEM),
            pl.BlockSpec(memory_space=pltpu.VMEM),
            pl.BlockSpec(memory_space=pl.ANY),
        ],
        out_specs=pl.BlockSpec(memory_space=pl.ANY),
        scratch_shapes=[
            pltpu.VMEM((rows, width), jnp.float32),
            pltpu.VMEM((chunk, span, width), jnp.float32),
            pltpu.VMEM(following_t.shape, following_t.dtype),
            pltpu.VMEM((4, chunk, LAGS, NFFT), jnp.bfloat16),
            pltpu.SemaphoreType.DMA((4, 4)),
            pltpu.SemaphoreType.DMA(()),
        ],
        cost_estimate=pl.CostEstimate(
            flops=6 * rows * LAGS * NF * segments,
            transcendentals=0,
            bytes_accessed=rows * LAGS * NFFT * 2 + 2 * (window_rows + following_t.shape[1]) * width,
        ),
    )(position.reshape(1).astype(jnp.int32), whitened_t, following_t)


def cross_spectra(own, extended):
    rows, segments, columns = own.shape
    reach_rows = extended.shape[0]
    own_flat = own.reshape(rows, segments * columns)
    ext_flat = extended.reshape(reach_rows, segments * columns)
    rows_per_step = 8
    span = reach_rows - rows_per_step
    scratch_bytes = rows_per_step * span * segments * columns * 4
    cost = pl.CostEstimate(
        flops=6 * rows * LAGS * NF * segments,
        transcendentals=0,
        bytes_accessed=rows * LAGS * columns * 2 + 2 * segments * (rows + reach_rows) * columns,
    )
    common = dict(
        out_shape=jax.ShapeDtypeStruct((rows, LAGS, columns), jnp.bfloat16),
        grid=(rows // rows_per_step,),
        in_specs=[
            pl.BlockSpec((rows, segments * columns), lambda i: (0, 0)),
            pl.BlockSpec((reach_rows, segments * columns), lambda i: (0, 0)),
        ],
        out_specs=pl.BlockSpec((rows_per_step, LAGS, columns), lambda i: (i, 0, 0)),
        cost_estimate=cost,
    )
    if scratch_bytes <= 8 * 1024 * 1024:
        return pl.pallas_call(
            functools.partial(cross_kernel_shifted, segments, rows_per_step),
            scratch_shapes=[
                pltpu.VMEM((rows, segments * columns), jnp.float32),
                pltpu.VMEM((rows_per_step, span, segments * columns), jnp.float32),
            ],
            compiler_params=pltpu.CompilerParams(dimension_semantics=("arbitrary",)),
            **common,
        )(own_flat, ext_flat)
    return pl.pallas_call(
        functools.partial(cross_kernel, segments, rows_per_step), **common
    )(own_flat, ext_flat)


def body(strain, filter_taps):
    extent = lax.axis_size("ta")
    columns_n = lax.axis_size("col")
    position = lax.axis_index("ta")
    section_rows, slab = strain.shape
    block_rows = section_rows // extent
    reach = LAGS // block_rows
    window = 2 * reach
    before = (reach - 1) * block_rows
    windows = channel_windows(
        strain.T, extent, before, reach * block_rows, window * block_rows
    )
    gathered = lax.all_to_all(windows, "ta", split_axis=0, concat_axis=0, tiled=True)
    samples = gathered.reshape(extent * slab, window * block_rows)
    filtered = decimate_t(samples.astype(jnp.float32), filter_taps)
    whitened_t = whiten_t(filtered)
    segments, columns, window_rows = whitened_t.shape
    first_of_section = reach - 1 - jnp.minimum(position, reach - 1)

    def linear(ta_index, col_index):
        return ta_index * columns_n + col_index

    route = [
        (linear(m, c + 1), linear(extent - reach + m, c))
        for c in range(columns_n - 1)
        for m in range(reach)
    ]
    if segments * 8 * (reach + 1) * block_rows * columns * 4 <= 8 * 1024 * 1024:
        flat = whitened_t.reshape(segments * columns, window_rows)
        payload = lax.dynamic_slice_in_dim(flat, first_of_section * block_rows, reach * block_rows, 1)
        next_section = lax.ppermute(payload, ("ta", "col"), route)
        return cross_spectra_direct(
            flat, next_section, position, block_rows, reach, extent, before
        )[None]
    whitened = whitened_t.transpose(2, 0, 1)
    payload = lax.dynamic_slice_in_dim(whitened, first_of_section * block_rows, reach * block_rows, 0)
    next_section = lax.ppermute(payload, ("ta", "col"), route)
    local = whitened[before : before + (reach + 1) * block_rows]
    extended = local
    for j in range(extent - reach, extent):
        kept = (extent - j) * block_rows
        candidate = jnp.concatenate(
            [local[:kept], next_section[: (reach + 1) * block_rows - kept]], axis=0
        )
        extended = jnp.where(position == j, candidate, extended)
    own = local[:block_rows]
    return cross_spectra(own, extended)[None]


def solution(mesh):
    return jax.shard_map(
        body,
        mesh=mesh,
        in_specs=(P("col", "ta"), P()),
        out_specs=P("col", "ta", None, None),
        check_vma=False,
    )
```

```python
import functools

import jax
import jax.numpy as jnp
from jax import lax
from jax.experimental import pallas as pl
from jax.experimental.pallas import tpu as pltpu
from jax.sharding import PartitionSpec as P

NFFT = 256
NF = 128
LAGS = 128


def tap_rows(filter_taps, outputs):
    tap_count = filter_taps.shape[0]
    window = 2 * outputs + tap_count
    flipped = filter_taps[::-1]
    period = jnp.concatenate([flipped, jnp.zeros((window + 2 - tap_count,), jnp.float32)])
    repeated = jnp.tile(period, outputs)[: outputs * window]
    return repeated.reshape(outputs, window)


def decimate_t(samples, filter_taps):
    length, channels = samples.shape
    tap_count = filter_taps.shape[0]
    outputs = min(length, NFFT) // 2
    blocks = length // (2 * outputs)
    joined = jnp.concatenate(
        [
            jnp.zeros((tap_count, channels), jnp.float32),
            samples,
            jnp.zeros((2 * outputs - tap_count, channels), jnp.float32),
        ],
        axis=0,
    )
    joined = joined.reshape(blocks + 1, 2 * outputs, channels)
    windows = jnp.concatenate([joined[:-1], joined[1:, :tap_count]], axis=1)
    matrix = tap_rows(filter_taps, outputs)
    result = jnp.einsum("tw,bwc->btc", matrix, windows, precision=lax.Precision.HIGHEST)
    return result.reshape(blocks * outputs, channels).astype(jnp.bfloat16)


def fourier_table():
    moment = lax.broadcasted_iota(jnp.int32, (NFFT, NF), 0)
    frequency = lax.broadcasted_iota(jnp.int32, (NFFT, NF), 1) + 1
    phase_index = moment * frequency % NFFT
    angles = phase_index.astype(jnp.float32) * (2.0 * jnp.pi / NFFT)
    window_taper = 0.5 - 0.5 * jnp.cos(moment.astype(jnp.float32) * (2.0 * jnp.pi / NFFT))
    return jnp.concatenate(
        [window_taper * jnp.cos(angles), -window_taper * jnp.sin(angles)], axis=1
    )


def whiten_t(filtered):
    length, channels = filtered.shape
    pieces = filtered.reshape(length // NF, NF, channels)
    segment_rows = jnp.concatenate([pieces[:-1], pieces[1:]], axis=1)
    spectrum = jnp.einsum(
        "nf,snc->sfc",
        fourier_table(),
        segment_rows.astype(jnp.float32),
        precision=lax.Precision.HIGHEST,
    )
    real_part = spectrum[:, :NF]
    imag_part = spectrum[:, NF:]
    powers = real_part * real_part + imag_part * imag_part
    mean_power = jnp.mean(powers, axis=1, keepdims=True)
    whitening = 1.0 / jnp.sqrt(powers + mean_power + 1e-06)
    return jnp.concatenate([real_part * whitening, imag_part * whitening], axis=1).astype(
        jnp.bfloat16
    )


def windows_kernel(before, after, width, x_ref, out_ref):
    x = x_ref[...].astype(jnp.float32)
    slab = x.shape[0]
    step = (x.shape[1] + before + after - width) // (out_ref.shape[0] - 1)
    parts = [x]
    if before:
        parts.insert(0, jnp.zeros((slab, before), jnp.float32))
    if after:
        parts.append(jnp.zeros((slab, after), jnp.float32))
    padded = jnp.concatenate(parts, axis=1) if len(parts) > 1 else x
    for j in range(out_ref.shape[0]):
        out_ref[j] = padded[:, j * step : j * step + width].astype(out_ref.dtype)


def channel_windows(turned, extent, before, after, width):
    slab, rows = turned.shape
    return pl.pallas_call(
        functools.partial(windows_kernel, before, after, width),
        out_shape=jax.ShapeDtypeStruct((extent, slab, width), turned.dtype),
        cost_estimate=pl.CostEstimate(
            flops=0, transcendentals=0, bytes_accessed=2 * (slab * rows + extent * slab * width)
        ),
    )(turned)


def xor_order(chunks, position, extent):
    bit = 1
    while bit < extent:
        shape = chunks.shape
        swapped = chunks.reshape((extent // (2 * bit), 2, bit) + shape[1:])[:, ::-1].reshape(shape)
        chunks = jnp.where((position & bit) != 0, swapped, chunks)
        bit *= 2
    return chunks


def exchange_time(windows, position, extent):
    if extent & (extent - 1) or extent > 16:
        return lax.all_to_all(windows, "ta", split_axis=0, concat_axis=0, tiled=True)
    chunks = xor_order(windows, position, extent)
    bit = 1
    while bit < extent:
        shape = chunks.shape
        view = chunks.reshape((extent // (2 * bit), 2, bit) + shape[1:])
        route = [(i, i ^ bit) for i in range(extent)]
        arrived = lax.ppermute(view[:, 1], "ta", route)
        chunks = jnp.stack([view[:, 0], arrived], axis=1).reshape(shape)
        bit *= 2
    return xor_order(chunks, position, extent)


def cross_kernel(segments, rows_per_step, own_ref, ext_ref, out_ref):
    step = pl.program_id(0)
    base = pl.multiple_of(step * rows_per_step, rows_per_step)
    for i in range(rows_per_step):
        acc_re = None
        acc_im = None
        for s in range(segments):
            a = own_ref[pl.ds(base, rows_per_step), pl.ds(s * NFFT, NFFT)]
            a = a.astype(jnp.float32)[i : i + 1]
            window = ext_ref[pl.ds(base, LAGS + rows_per_step), pl.ds(s * NFFT, NFFT)]
            b = window.astype(jnp.float32)[i : i + LAGS]
            terms = product_terms(a, b)
            if acc_re is None:
                acc_re, acc_im = terms
            else:
                acc_re = [x + y for x, y in zip(acc_re, terms[0])]
                acc_im = [x + y for x, y in zip(acc_im, terms[1])]
        store_row(out_ref, i, acc_re, acc_im, segments)


def product_terms(a, b):
    ar = a[:, :NF]
    ai = a[:, NF:]
    br = b[:, :NF]
    bi = b[:, NF:]
    return [ar * br, ai * bi], [ai * br, ar * bi]


def store_row(out_ref, i, acc_re, acc_im, segments):
    re = acc_re[0] + acc_re[1]
    im = acc_im[0] - acc_im[1]
    if segments > 1:
        re = re / segments
        im = im / segments
    out_ref[i, :, :NF] = re.astype(out_ref.dtype)
    out_ref[i, :, NF:] = im.astype(out_ref.dtype)


def cross_kernel_shifted(segments, rows_per_step, own_ref, ext_ref, out_ref, own_f32, shifted):
    step = pl.program_id(0)
    span = shifted.shape[1]

    @pl.when(step == 0)
    def _():
        own_f32[...] = own_ref[...].astype(jnp.float32)
        whole = ext_ref[...].astype(jnp.float32)
        for i in range(rows_per_step):
            shifted[i] = whole[i : i + span]

    base = pl.multiple_of(step * rows_per_step, rows_per_step)
    for i in range(rows_per_step):
        acc_re = None
        acc_im = None
        for s in range(segments):
            a = own_f32[pl.ds(base + i, 1), pl.ds(s * NFFT, NFFT)]
            b = shifted[i, pl.ds(base, LAGS), pl.ds(s * NFFT, NFFT)]
            terms = product_terms(a, b)
            if acc_re is None:
                acc_re, acc_im = terms
            else:
                acc_re = [x + y for x, y in zip(acc_re, terms[0])]
                acc_im = [x + y for x, y in zip(acc_im, terms[1])]
        store_row(out_ref, i, acc_re, acc_im, segments)


def cross_kernel(segments, rows_per_step, own_ref, ext_ref, out_ref):
    step = pl.program_id(0)
    base = pl.multiple_of(step * rows_per_step, rows_per_step)
    for i in range(rows_per_step):
        acc_re = None
        acc_im = None
        for s in range(segments):
            a = own_ref[pl.ds(base, rows_per_step), pl.ds(s * NFFT, NFFT)]
            a = a.astype(jnp.float32)[i : i + 1]
            window = ext_ref[pl.ds(base, LAGS + rows_per_step), pl.ds(s * NFFT, NFFT)]
            b = window.astype(jnp.float32)[i : i + LAGS]
            terms = product_terms(a, b)
            if acc_re is None:
                acc_re, acc_im = terms
            else:
                acc_re = [x + y for x, y in zip(acc_re, terms[0])]
                acc_im = [x + y for x, y in zip(acc_im, terms[1])]
        store_row(out_ref, i, acc_re, acc_im, segments)


def product_terms(a, b):
    ar = a[:, :NF]
    ai = a[:, NF:]
    br = b[:, :NF]
    bi = b[:, NF:]
    return [ar * br, ai * bi], [ai * br, ar * bi]


def store_row(out_ref, i, acc_re, acc_im, segments):
    re = acc_re[0] + acc_re[1]
    im = acc_im[0] - acc_im[1]
    if segments > 1:
        re = re / segments
        im = im / segments
    out_ref[i, :, :NF] = re.astype(out_ref.dtype)
    out_ref[i, :, NF:] = im.astype(out_ref.dtype)


def cross_kernel_shifted(segments, rows_per_step, own_ref, ext_ref, out_ref, own_f32, shifted):
    step = pl.program_id(0)
    span = shifted.shape[1]

    @pl.when(step == 0)
    def _():
        own_f32[...] = own_ref[...].astype(jnp.float32)
        whole = ext_ref[...].astype(jnp.float32)
        for i in range(rows_per_step):
            shifted[i] = whole[i : i + span]

    base = pl.multiple_of(step * rows_per_step, rows_per_step)
    for i in range(rows_per_step):
        acc_re = None
        acc_im = None
        for s in range(segments):
            a = own_f32[pl.ds(base + i, 1), pl.ds(s * NFFT, NFFT)]
            b = shifted[i, pl.ds(base, LAGS), pl.ds(s * NFFT, NFFT)]
            terms = product_terms(a, b)
            if acc_re is None:
                acc_re, acc_im = terms
            else:
                acc_re = [x + y for x, y in zip(acc_re, terms[0])]
                acc_im = [x + y for x, y in zip(acc_im, terms[1])]
        store_row(out_ref, i, acc_re, acc_im, segments)


def cross_kernel_direct(segments, rows, reach, extent, before, chunk,
                        pos_ref, win_ref, next_hbm, out_hbm, own_f32, shifted, following,
                        buffers, sems, next_sem):
    fetch = pltpu.make_async_copy(next_hbm, following, next_sem)
    fetch.start()
    span = shifted.shape[1]
    position = pos_ref[0]
    width = (reach + 1) * rows
    local = jnp.concatenate(
        [
            win_ref[s * NFFT : (s + 1) * NFFT, before : before + width].astype(jnp.float32).T
            for s in range(segments)
        ],
        axis=1,
    )
    own_f32[...] = local[:rows]
    fetch.wait()
    arrived = jnp.concatenate(
        [following[s * NFFT : (s + 1) * NFFT, :].astype(jnp.float32).T for s in range(segments)],
        axis=1,
    )
    extended = local
    for j in range(extent - reach, extent):
        kept = (extent - j) * rows
        candidate = jnp.concatenate([local[:kept], arrived[: width - kept]], axis=0)
        extended = jnp.where(position == j, candidate, extended)
    for i in range(chunk):
        shifted[i] = extended[i : i + span]
    slots, parts = buffers.shape[0], sems.shape[1]
    part = chunk // parts
    copies = []
    for m in range(rows // chunk):
        slot = m % slots
        if m >= slots:
            for copy in copies[m - slots]:
                copy.wait()
        base = m * chunk
        for i in range(chunk):
            acc_re = None
            acc_im = None
            for s in range(segments):
                a = own_f32[base + i : base + i + 1, s * NFFT : (s + 1) * NFFT]
                b = shifted[i, base : base + LAGS, s * NFFT : (s + 1) * NFFT]
                terms = product_terms(a, b)
                if acc_re is None:
                    acc_re, acc_im = terms
                else:
                    acc_re = [x + y for x, y in zip(acc_re, terms[0])]
                    acc_im = [x + y for x, y in zip(acc_im, terms[1])]
            store_row(buffers.at[slot], i, acc_re, acc_im, segments)
        group = []
        for p in range(parts):
            copy = pltpu.make_async_copy(
                buffers.at[slot, pl.ds(p * part, part)],
                out_hbm.at[pl.ds(base + p * part, part)],
                sems.at[slot, p],
            )
            copy.start()
            group.append(copy)
        copies.append(group)
    for group in copies[-slots:]:
        for copy in group:
            copy.wait()


def cross_spectra_direct(whitened_t, following_t, position, rows, reach, extent, before):
    width, window_rows = whitened_t.shape
    segments = width // NFFT
    chunk = 8
    reach_rows = (reach + 1) * rows
    span = reach_rows - chunk
    return pl.pallas_call(
        functools.partial(cross_kernel_direct, segments, rows, reach, extent, before, chunk),
        out_shape=jax.ShapeDtypeStruct((rows, LAGS, NFFT), jnp.bfloat16),
        in_specs=[
            pl.BlockSpec(memory_space=pltpu.SMEM),
            pl.BlockSpec(memory_space=pltpu.VMEM),
            pl.BlockSpec(memory_space=pl.ANY),
        ],
        out_specs=pl.BlockSpec(memory_space=pl.ANY),
        scratch_shapes=[
            pltpu.VMEM((rows, width), jnp.float32),
            pltpu.VMEM((chunk, span, width), jnp.float32),
            pltpu.VMEM(following_t.shape, following_t.dtype),
            pltpu.VMEM((4, chunk, LAGS, NFFT), jnp.bfloat16),
            pltpu.SemaphoreType.DMA((4, 4)),
            pltpu.SemaphoreType.DMA(()),
        ],
        cost_estimate=pl.CostEstimate(
            flops=6 * rows * LAGS * NF * segments,
            transcendentals=0,
            bytes_accessed=rows * LAGS * NFFT * 2 + 2 * (window_rows + following_t.shape[1]) * width,
        ),
    )(position.reshape(1).astype(jnp.int32), whitened_t, following_t)


def cross_kernel_pieces(segments, rows, chunk, *refs):
    pieces = refs[:-5]
    out_hbm, own_f32, shifted, buffers, sems = refs[-5:]
    span = shifted.shape[1]
    extended = jnp.concatenate(
        [
            jnp.concatenate(
                [piece[s * NFFT : (s + 1) * NFFT, :].astype(jnp.float32).T for s in range(segments)],
                axis=1,
            )
            for piece in pieces
        ],
        axis=0,
    )
    own_f32[...] = extended[:rows]
    for i in range(chunk):
        shifted[i] = extended[i : i + span]
    slots, parts = buffers.shape[0], sems.shape[1]
    part = chunk // parts
    copies = []
    for m in range(rows // chunk):
        slot = m % slots
        if m >= slots:
            for copy in copies[m - slots]:
                copy.wait()
        base = m * chunk
        for i in range(chunk):
            acc_re = None
            acc_im = None
            for s in range(segments):
                a = own_f32[base + i : base + i + 1, s * NFFT : (s + 1) * NFFT]
                b = shifted[i, base : base + LAGS, s * NFFT : (s + 1) * NFFT]
                terms = product_terms(a, b)
                if acc_re is None:
                    acc_re, acc_im = terms
                else:
                    acc_re = [x + y for x, y in zip(acc_re, terms[0])]
                    acc_im = [x + y for x, y in zip(acc_im, terms[1])]
            store_row(buffers.at[slot], i, acc_re, acc_im, segments)
        group = []
        for p in range(parts):
            copy = pltpu.make_async_copy(
                buffers.at[slot, pl.ds(p * part, part)],
                out_hbm.at[pl.ds(base + p * part, part)],
                sems.at[slot, p],
            )
            copy.start()
            group.append(copy)
        copies.append(group)
    for group in copies[-slots:]:
        for copy in group:
            copy.wait()


def cross_spectra_pieces(pieces):
    width, rows = pieces[0].shape
    segments = width // NFFT
    chunk = 8
    span = len(pieces) * rows - chunk
    return pl.pallas_call(
        functools.partial(cross_kernel_pieces, segments, rows, chunk),
        out_shape=jax.ShapeDtypeStruct((rows, LAGS, NFFT), jnp.bfloat16),
        in_specs=[pl.BlockSpec(memory_space=pltpu.VMEM)] * len(pieces),
        out_specs=pl.BlockSpec(memory_space=pl.ANY),
        scratch_shapes=[
            pltpu.VMEM((rows, width), jnp.float32),
            pltpu.VMEM((chunk, span, width), jnp.float32),
            pltpu.VMEM((4, chunk, LAGS, NFFT), jnp.bfloat16),
            pltpu.SemaphoreType.DMA((4, 4)),
        ],
        cost_estimate=pl.CostEstimate(
            flops=6 * rows * LAGS * NF * segments,
            transcendentals=0,
            bytes_accessed=rows * LAGS * NFFT * 2 + 2 * len(pieces) * rows * width,
        ),
    )(*pieces)


def cross_spectra(own, extended):
    rows, segments, columns = own.shape
    reach_rows = extended.shape[0]
    own_flat = own.reshape(rows, segments * columns)
    ext_flat = extended.reshape(reach_rows, segments * columns)
    rows_per_step = 8
    span = reach_rows - rows_per_step
    scratch_bytes = rows_per_step * span * segments * columns * 4
    cost = pl.CostEstimate(
        flops=6 * rows * LAGS * NF * segments,
        transcendentals=0,
        bytes_accessed=rows * LAGS * columns * 2 + 2 * segments * (rows + reach_rows) * columns,
    )
    common = dict(
        out_shape=jax.ShapeDtypeStruct((rows, LAGS, columns), jnp.bfloat16),
        grid=(rows // rows_per_step,),
        in_specs=[
            pl.BlockSpec((rows, segments * columns), lambda i: (0, 0)),
            pl.BlockSpec((reach_rows, segments * columns), lambda i: (0, 0)),
        ],
        out_specs=pl.BlockSpec((rows_per_step, LAGS, columns), lambda i: (i, 0, 0)),
        cost_estimate=cost,
    )
    if scratch_bytes <= 8 * 1024 * 1024:
        return pl.pallas_call(
            functools.partial(cross_kernel_shifted, segments, rows_per_step),
            scratch_shapes=[
                pltpu.VMEM((rows, segments * columns), jnp.float32),
                pltpu.VMEM((rows_per_step, span, segments * columns), jnp.float32),
            ],
            compiler_params=pltpu.CompilerParams(dimension_semantics=("arbitrary",)),
            **common,
        )(own_flat, ext_flat)
    return pl.pallas_call(
        functools.partial(cross_kernel, segments, rows_per_step), **common
    )(own_flat, ext_flat)


def body(strain, filter_taps):
    extent = lax.axis_size("ta")
    columns_n = lax.axis_size("col")
    position = lax.axis_index("ta")
    section_rows, slab = strain.shape
    block_rows = section_rows // extent
    reach = LAGS // block_rows
    chunks = channel_windows(strain.T, extent, 0, 0, block_rows)
    gathered = exchange_time(chunks, position, extent)
    samples = gathered.reshape(extent * slab, block_rows)
    filtered = decimate_t(samples.astype(jnp.float32), filter_taps)
    whitened_t = whiten_t(filtered)
    segments, columns, _ = whitened_t.shape
    flat = whitened_t.reshape(segments * columns, block_rows)
    total = columns_n * extent

    def linear(block):
        return (block % extent) * columns_n + block // extent

    pieces = [flat]
    for offset in range(1, reach + 1):
        route = [(linear(b + offset), linear(b)) for b in range(total) if b + offset < total]
        pieces.append(lax.ppermute(flat, ("ta", "col"), route))
    if segments * 8 * (reach + 1) * block_rows * columns * 4 <= 8 * 1024 * 1024:
        return cross_spectra_pieces(pieces)[None]
    extended = jnp.concatenate(pieces, axis=1).reshape(segments, columns, -1).transpose(2, 0, 1)
    return cross_spectra(extended[:block_rows], extended)[None]


def solution(mesh):
    return jax.shard_map(
        body,
        mesh=mesh,
        in_specs=(P("col", "ta"), P()),
        out_specs=P("col", "ta", None, None),
        check_vma=False,
    )
```

```python
import functools

import jax
import jax.numpy as jnp
from jax import lax
from jax.experimental import pallas as pl
from jax.experimental.pallas import tpu as pltpu
from jax.sharding import PartitionSpec as P

NFFT = 256
NF = 128
LAGS = 128


def tap_rows(filter_taps, outputs):
    tap_count = filter_taps.shape[0]
    window = 2 * outputs + tap_count
    flipped = filter_taps[::-1]
    period = jnp.concatenate([flipped, jnp.zeros((window + 2 - tap_count,), jnp.float32)])
    repeated = jnp.tile(period, outputs)[: outputs * window]
    return repeated.reshape(outputs, window)


def decimate_t(samples, filter_taps):
    length, channels = samples.shape
    tap_count = filter_taps.shape[0]
    outputs = min(length, NFFT) // 2
    blocks = length // (2 * outputs)
    joined = jnp.concatenate(
        [
            jnp.zeros((tap_count, channels), jnp.float32),
            samples,
            jnp.zeros((2 * outputs - tap_count, channels), jnp.float32),
        ],
        axis=0,
    )
    joined = joined.reshape(blocks + 1, 2 * outputs, channels)
    windows = jnp.concatenate([joined[:-1], joined[1:, :tap_count]], axis=1)
    matrix = tap_rows(filter_taps, outputs)
    result = jnp.einsum("tw,bwc->btc", matrix, windows, precision=lax.Precision.HIGHEST)
    return result.reshape(blocks * outputs, channels).astype(jnp.bfloat16)


def fourier_table():
    moment = lax.broadcasted_iota(jnp.int32, (NFFT, NF), 0)
    frequency = lax.broadcasted_iota(jnp.int32, (NFFT, NF), 1) + 1
    phase_index = moment * frequency % NFFT
    angles = phase_index.astype(jnp.float32) * (2.0 * jnp.pi / NFFT)
    window_taper = 0.5 - 0.5 * jnp.cos(moment.astype(jnp.float32) * (2.0 * jnp.pi / NFFT))
    return jnp.concatenate(
        [window_taper * jnp.cos(angles), -window_taper * jnp.sin(angles)], axis=1
    )


def whiten_t(filtered):
    length, channels = filtered.shape
    pieces = filtered.reshape(length // NF, NF, channels)
    segment_rows = jnp.concatenate([pieces[:-1], pieces[1:]], axis=1)
    spectrum = jnp.einsum(
        "nf,snc->sfc",
        fourier_table(),
        segment_rows.astype(jnp.float32),
        precision=lax.Precision.HIGHEST,
    )
    real_part = spectrum[:, :NF]
    imag_part = spectrum[:, NF:]
    powers = real_part * real_part + imag_part * imag_part
    mean_power = jnp.mean(powers, axis=1, keepdims=True)
    whitening = 1.0 / jnp.sqrt(powers + mean_power + 1e-06)
    return jnp.concatenate([real_part * whitening, imag_part * whitening], axis=1).astype(
        jnp.bfloat16
    )


def windows_kernel(width, x_ref, tail_ref, out_ref):
    padded = jnp.concatenate(
        [x_ref[...].astype(jnp.float32), tail_ref[...].astype(jnp.float32)], axis=1
    )
    step = (padded.shape[1] - width) // (out_ref.shape[0] - 1)
    for j in range(out_ref.shape[0]):
        out_ref[j] = padded[:, j * step : j * step + width].astype(out_ref.dtype)


def channel_windows(turned, tail, extent, width):
    slab, rows = turned.shape
    return pl.pallas_call(
        functools.partial(windows_kernel, width),
        out_shape=jax.ShapeDtypeStruct((extent, slab, width), turned.dtype),
        cost_estimate=pl.CostEstimate(
            flops=0,
            transcendentals=0,
            bytes_accessed=2 * (slab * (rows + tail.shape[1]) + extent * slab * width),
        ),
    )(turned, tail)


def cross_kernel(segments, rows_per_step, own_ref, ext_ref, out_ref):
    step = pl.program_id(0)
    base = pl.multiple_of(step * rows_per_step, rows_per_step)
    for i in range(rows_per_step):
        acc_re = None
        acc_im = None
        for s in range(segments):
            a = own_ref[pl.ds(base, rows_per_step), pl.ds(s * NFFT, NFFT)]
            a = a.astype(jnp.float32)[i : i + 1]
            window = ext_ref[pl.ds(base, LAGS + rows_per_step), pl.ds(s * NFFT, NFFT)]
            b = window.astype(jnp.float32)[i : i + LAGS]
            terms = product_terms(a, b)
            if acc_re is None:
                acc_re, acc_im = terms
            else:
                acc_re = [x + y for x, y in zip(acc_re, terms[0])]
                acc_im = [x + y for x, y in zip(acc_im, terms[1])]
        store_row(out_ref, i, acc_re, acc_im, segments)


def product_terms(a, b):
    ar = a[:, :NF]
    ai = a[:, NF:]
    br = b[:, :NF]
    bi = b[:, NF:]
    return [ar * br, ai * bi], [ai * br, ar * bi]


def store_row(out_ref, i, acc_re, acc_im, segments):
    re = acc_re[0] + acc_re[1]
    im = acc_im[0] - acc_im[1]
    if segments > 1:
        re = re / segments
        im = im / segments
    out_ref[i, :, :NF] = re.astype(out_ref.dtype)
    out_ref[i, :, NF:] = im.astype(out_ref.dtype)


def cross_kernel_shifted(segments, rows_per_step, own_ref, ext_ref, out_ref, own_f32, shifted):
    step = pl.program_id(0)
    span = shifted.shape[1]

    @pl.when(step == 0)
    def _():
        own_f32[...] = own_ref[...].astype(jnp.float32)
        whole = ext_ref[...].astype(jnp.float32)
        for i in range(rows_per_step):
            shifted[i] = whole[i : i + span]

    base = pl.multiple_of(step * rows_per_step, rows_per_step)
    for i in range(rows_per_step):
        acc_re = None
        acc_im = None
        for s in range(segments):
            a = own_f32[pl.ds(base + i, 1), pl.ds(s * NFFT, NFFT)]
            b = shifted[i, pl.ds(base, LAGS), pl.ds(s * NFFT, NFFT)]
            terms = product_terms(a, b)
            if acc_re is None:
                acc_re, acc_im = terms
            else:
                acc_re = [x + y for x, y in zip(acc_re, terms[0])]
                acc_im = [x + y for x, y in zip(acc_im, terms[1])]
        store_row(out_ref, i, acc_re, acc_im, segments)


def cross_kernel_pieces(segments, rows, chunk, *refs):
    pieces = refs[:-5]
    out_hbm, own_f32, shifted, buffers, sems = refs[-5:]
    span = shifted.shape[1]
    extended = jnp.concatenate(
        [
            jnp.concatenate(
                [piece[s * NFFT : (s + 1) * NFFT, :].astype(jnp.float32).T for s in range(segments)],
                axis=1,
            )
            for piece in pieces
        ],
        axis=0,
    )
    own_f32[...] = extended[:rows]
    for i in range(chunk):
        shifted[i] = extended[i : i + span]
    slots, parts = buffers.shape[0], sems.shape[1]
    part = chunk // parts
    copies = []
    for m in range(rows // chunk):
        slot = m % slots
        if m >= slots:
            for copy in copies[m - slots]:
                copy.wait()
        base = m * chunk
        for i in range(chunk):
            acc_re = None
            acc_im = None
            for s in range(segments):
                a = own_f32[base + i : base + i + 1, s * NFFT : (s + 1) * NFFT]
                b = shifted[i, base : base + LAGS, s * NFFT : (s + 1) * NFFT]
                terms = product_terms(a, b)
                if acc_re is None:
                    acc_re, acc_im = terms
                else:
                    acc_re = [x + y for x, y in zip(acc_re, terms[0])]
                    acc_im = [x + y for x, y in zip(acc_im, terms[1])]
            store_row(buffers.at[slot], i, acc_re, acc_im, segments)
        group = []
        for p in range(parts):
            copy = pltpu.make_async_copy(
                buffers.at[slot, pl.ds(p * part, part)],
                out_hbm.at[pl.ds(base + p * part, part)],
                sems.at[slot, p],
            )
            copy.start()
            group.append(copy)
        copies.append(group)
    for group in copies[-slots:]:
        for copy in group:
            copy.wait()


def cross_spectra_pieces(pieces):
    width = pieces[0].shape[0]
    rows = sum(piece.shape[1] for piece in pieces) - LAGS
    segments = width // NFFT
    chunk = 8
    span = rows + LAGS - chunk
    return pl.pallas_call(
        functools.partial(cross_kernel_pieces, segments, rows, chunk),
        out_shape=jax.ShapeDtypeStruct((rows, LAGS, NFFT), jnp.bfloat16),
        in_specs=[pl.BlockSpec(memory_space=pltpu.VMEM)] * len(pieces),
        out_specs=pl.BlockSpec(memory_space=pl.ANY),
        scratch_shapes=[
            pltpu.VMEM((rows, width), jnp.float32),
            pltpu.VMEM((chunk, span, width), jnp.float32),
            pltpu.VMEM((4, chunk, LAGS, NFFT), jnp.bfloat16),
            pltpu.SemaphoreType.DMA((4, 4)),
        ],
        cost_estimate=pl.CostEstimate(
            flops=6 * rows * LAGS * NF * segments,
            transcendentals=0,
            bytes_accessed=rows * LAGS * NFFT * 2 + 2 * (rows + LAGS) * width,
        ),
    )(*pieces)


def cross_spectra(own, extended):
    rows, segments, columns = own.shape
    reach_rows = extended.shape[0]
    own_flat = own.reshape(rows, segments * columns)
    ext_flat = extended.reshape(reach_rows, segments * columns)
    rows_per_step = 8
    span = reach_rows - rows_per_step
    scratch_bytes = rows_per_step * span * segments * columns * 4
    cost = pl.CostEstimate(
        flops=6 * rows * LAGS * NF * segments,
        transcendentals=0,
        bytes_accessed=rows * LAGS * columns * 2 + 2 * segments * (rows + reach_rows) * columns,
    )
    common = dict(
        out_shape=jax.ShapeDtypeStruct((rows, LAGS, columns), jnp.bfloat16),
        grid=(rows // rows_per_step,),
        in_specs=[
            pl.BlockSpec((rows, segments * columns), lambda i: (0, 0)),
            pl.BlockSpec((reach_rows, segments * columns), lambda i: (0, 0)),
        ],
        out_specs=pl.BlockSpec((rows_per_step, LAGS, columns), lambda i: (i, 0, 0)),
        cost_estimate=cost,
    )
    if scratch_bytes <= 8 * 1024 * 1024:
        return pl.pallas_call(
            functools.partial(cross_kernel_shifted, segments, rows_per_step),
            scratch_shapes=[
                pltpu.VMEM((rows, segments * columns), jnp.float32),
                pltpu.VMEM((rows_per_step, span, segments * columns), jnp.float32),
            ],
            compiler_params=pltpu.CompilerParams(dimension_semantics=("arbitrary",)),
            **common,
        )(own_flat, ext_flat)
    return pl.pallas_call(
        functools.partial(cross_kernel, segments, rows_per_step), **common
    )(own_flat, ext_flat)


def body(strain, filter_taps):
    extent = lax.axis_size("ta")
    columns_n = lax.axis_size("col")
    section_rows, slab = strain.shape
    block_rows = section_rows // extent
    reach = LAGS // block_rows
    turned = strain.T
    route = [(c + 1, c) for c in range(columns_n - 1)]
    tail = lax.ppermute(turned[:, : reach * block_rows], "col", route)
    width = (reach + 1) * block_rows
    windows = channel_windows(turned, tail, extent, width)
    gathered = lax.all_to_all(windows, "ta", split_axis=0, concat_axis=0, tiled=True)
    samples = gathered.reshape(extent * slab, width)
    filtered = decimate_t(samples.astype(jnp.float32), filter_taps)
    whitened_t = whiten_t(filtered)
    segments, columns, _ = whitened_t.shape
    if segments * 8 * width * columns * 4 <= 8 * 1024 * 1024:
        flat = whitened_t.reshape(segments * columns, width)
        return cross_spectra_pieces([flat])[None]
    extended = whitened_t.transpose(2, 0, 1)
    return cross_spectra(extended[:block_rows], extended)[None]


def solution(mesh):
    return jax.shard_map(
        body,
        mesh=mesh,
        in_specs=(P("col", "ta"), P()),
        out_specs=P("col", "ta", None, None),
        check_vma=False,
    )
```

```python
import functools

import jax
import jax.numpy as jnp
from jax import lax
from jax.experimental import pallas as pl
from jax.experimental.pallas import tpu as pltpu
from jax.sharding import PartitionSpec as P

NFFT = 256
NF = 128
LAGS = 128


def tap_rows(filter_taps, outputs):
    tap_count = filter_taps.shape[0]
    window = 2 * outputs + tap_count
    flipped = filter_taps[::-1]
    period = jnp.concatenate([flipped, jnp.zeros((window + 2 - tap_count,), jnp.float32)])
    repeated = jnp.tile(period, outputs)[: outputs * window]
    return repeated.reshape(outputs, window)


def decimate_t(samples, filter_taps):
    length, channels = samples.shape
    tap_count = filter_taps.shape[0]
    outputs = min(length, NFFT) // 2
    blocks = length // (2 * outputs)
    joined = jnp.concatenate(
        [
            jnp.zeros((tap_count, channels), jnp.float32),
            samples,
            jnp.zeros((2 * outputs - tap_count, channels), jnp.float32),
        ],
        axis=0,
    )
    joined = joined.reshape(blocks + 1, 2 * outputs, channels)
    windows = jnp.concatenate([joined[:-1], joined[1:, :tap_count]], axis=1)
    matrix = tap_rows(filter_taps, outputs)
    result = jnp.einsum("tw,bwc->btc", matrix, windows, precision=lax.Precision.HIGHEST)
    return result.reshape(blocks * outputs, channels).astype(jnp.bfloat16)


def fourier_table():
    moment = lax.broadcasted_iota(jnp.int32, (NFFT, NF), 0)
    frequency = lax.broadcasted_iota(jnp.int32, (NFFT, NF), 1) + 1
    phase_index = moment * frequency % NFFT
    angles = phase_index.astype(jnp.float32) * (2.0 * jnp.pi / NFFT)
    window_taper = 0.5 - 0.5 * jnp.cos(moment.astype(jnp.float32) * (2.0 * jnp.pi / NFFT))
    return jnp.concatenate(
        [window_taper * jnp.cos(angles), -window_taper * jnp.sin(angles)], axis=1
    )


def whiten_t(filtered):
    length, channels = filtered.shape
    pieces = filtered.reshape(length // NF, NF, channels)
    segment_rows = jnp.concatenate([pieces[:-1], pieces[1:]], axis=1)
    spectrum = jnp.einsum(
        "nf,snc->sfc",
        fourier_table(),
        segment_rows.astype(jnp.float32),
        precision=lax.Precision.HIGHEST,
    )
    real_part = spectrum[:, :NF]
    imag_part = spectrum[:, NF:]
    powers = real_part * real_part + imag_part * imag_part
    mean_power = jnp.mean(powers, axis=1, keepdims=True)
    whitening = 1.0 / jnp.sqrt(powers + mean_power + 1e-06)
    return jnp.concatenate([real_part * whitening, imag_part * whitening], axis=1).astype(
        jnp.bfloat16
    )


def windows_kernel(width, tail_rows, x_ref, out_ref):
    x = x_ref[...].astype(jnp.float32)
    padded = jnp.concatenate([x, jnp.zeros((x.shape[0], tail_rows), jnp.float32)], axis=1)
    step = (padded.shape[1] - width) // (out_ref.shape[0] - 1)
    for j in range(out_ref.shape[0]):
        out_ref[j] = padded[:, j * step : j * step + width].astype(out_ref.dtype)


def tail_windows_kernel(width, count, x_ref, tail_ref, windows_hbm, out_hbm, fresh, sem):
    del windows_hbm
    x = x_ref[...].astype(jnp.float32)
    tail = tail_ref[...].astype(jnp.float32)
    extent = out_hbm.shape[0]
    rows = x.shape[1]
    step = (rows + tail.shape[1] - width) // (extent - 1)
    first = extent - count
    padded = jnp.concatenate([x[:, first * step :], tail], axis=1)
    for j in range(count):
        fresh[j] = padded[:, j * step : j * step + width].astype(fresh.dtype)
    copy = pltpu.make_async_copy(fresh, out_hbm.at[pl.ds(first, count)], sem)
    copy.start()
    copy.wait()


def channel_windows(turned, tail, extent, width, tail_rows):
    slab, rows = turned.shape
    windows = pl.pallas_call(
        functools.partial(windows_kernel, width, tail_rows),
        out_shape=jax.ShapeDtypeStruct((extent, slab, width), turned.dtype),
        cost_estimate=pl.CostEstimate(
            flops=0, transcendentals=0, bytes_accessed=2 * (slab * rows + extent * slab * width)
        ),
    )(turned)
    count = -(-tail_rows // ((rows + tail_rows - width) // (extent - 1)))
    return pl.pallas_call(
        functools.partial(tail_windows_kernel, width, count),
        out_shape=jax.ShapeDtypeStruct((extent, slab, width), turned.dtype),
        in_specs=[
            pl.BlockSpec(memory_space=pltpu.VMEM),
            pl.BlockSpec(memory_space=pltpu.VMEM),
            pl.BlockSpec(memory_space=pl.ANY),
        ],
        out_specs=pl.BlockSpec(memory_space=pl.ANY),
        scratch_shapes=[
            pltpu.VMEM((count, slab, width), turned.dtype),
            pltpu.SemaphoreType.DMA(()),
        ],
        input_output_aliases={2: 0},
        cost_estimate=pl.CostEstimate(
            flops=0, transcendentals=0, bytes_accessed=2 * (slab * rows + 2 * count * slab * width)
        ),
    )(turned, tail, windows)


def cross_kernel(segments, rows_per_step, own_ref, ext_ref, out_ref):
    step = pl.program_id(0)
    base = pl.multiple_of(step * rows_per_step, rows_per_step)
    for i in range(rows_per_step):
        acc_re = None
        acc_im = None
        for s in range(segments):
            a = own_ref[pl.ds(base, rows_per_step), pl.ds(s * NFFT, NFFT)]
            a = a.astype(jnp.float32)[i : i + 1]
            window = ext_ref[pl.ds(base, LAGS + rows_per_step), pl.ds(s * NFFT, NFFT)]
            b = window.astype(jnp.float32)[i : i + LAGS]
            terms = product_terms(a, b)
            if acc_re is None:
                acc_re, acc_im = terms
            else:
                acc_re = [x + y for x, y in zip(acc_re, terms[0])]
                acc_im = [x + y for x, y in zip(acc_im, terms[1])]
        store_row(out_ref, i, acc_re, acc_im, segments)


def product_terms(a, b):
    ar = a[:, :NF]
    ai = a[:, NF:]
    br = b[:, :NF]
    bi = b[:, NF:]
    return [ar * br, ai * bi], [ai * br, ar * bi]


def store_row(out_ref, i, acc_re, acc_im, segments):
    re = acc_re[0] + acc_re[1]
    im = acc_im[0] - acc_im[1]
    if segments > 1:
        re = re / segments
        im = im / segments
    out_ref[i, :, :NF] = re.astype(out_ref.dtype)
    out_ref[i, :, NF:] = im.astype(out_ref.dtype)


def cross_kernel_shifted(segments, rows_per_step, own_ref, ext_ref, out_ref, own_f32, shifted):
    step = pl.program_id(0)
    span = shifted.shape[1]

    @pl.when(step == 0)
    def _():
        own_f32[...] = own_ref[...].astype(jnp.float32)
        whole = ext_ref[...].astype(jnp.float32)
        for i in range(rows_per_step):
            shifted[i] = whole[i : i + span]

    base = pl.multiple_of(step * rows_per_step, rows_per_step)
    for i in range(rows_per_step):
        acc_re = None
        acc_im = None
        for s in range(segments):
            a = own_f32[pl.ds(base + i, 1), pl.ds(s * NFFT, NFFT)]
            b = shifted[i, pl.ds(base, LAGS), pl.ds(s * NFFT, NFFT)]
            terms = product_terms(a, b)
            if acc_re is None:
                acc_re, acc_im = terms
            else:
                acc_re = [x + y for x, y in zip(acc_re, terms[0])]
                acc_im = [x + y for x, y in zip(acc_im, terms[1])]
        store_row(out_ref, i, acc_re, acc_im, segments)


def cross_kernel_pieces(segments, rows, chunk, *refs):
    pieces = refs[:-5]
    out_hbm, own_f32, shifted, buffers, sems = refs[-5:]
    span = shifted.shape[1]
    extended = jnp.concatenate(
        [
            jnp.concatenate(
                [piece[s * NFFT : (s + 1) * NFFT, :].astype(jnp.float32).T for s in range(segments)],
                axis=1,
            )
            for piece in pieces
        ],
        axis=0,
    )
    own_f32[...] = extended[:rows]
    for i in range(chunk):
        shifted[i] = extended[i : i + span]
    slots, parts = buffers.shape[0], sems.shape[1]
    part = chunk // parts
    copies = []
    for m in range(rows // chunk):
        slot = m % slots
        if m >= slots:
            for copy in copies[m - slots]:
                copy.wait()
        base = m * chunk
        for i in range(chunk):
            acc_re = None
            acc_im = None
            for s in range(segments):
                a = own_f32[base + i : base + i + 1, s * NFFT : (s + 1) * NFFT]
                b = shifted[i, base : base + LAGS, s * NFFT : (s + 1) * NFFT]
                terms = product_terms(a, b)
                if acc_re is None:
                    acc_re, acc_im = terms
                else:
                    acc_re = [x + y for x, y in zip(acc_re, terms[0])]
                    acc_im = [x + y for x, y in zip(acc_im, terms[1])]
            store_row(buffers.at[slot], i, acc_re, acc_im, segments)
        group = []
        for p in range(parts):
            copy = pltpu.make_async_copy(
                buffers.at[slot, pl.ds(p * part, part)],
                out_hbm.at[pl.ds(base + p * part, part)],
                sems.at[slot, p],
            )
            copy.start()
            group.append(copy)
        copies.append(group)
    for group in copies[-slots:]:
        for copy in group:
            copy.wait()


def cross_spectra_pieces(pieces):
    width = pieces[0].shape[0]
    rows = sum(piece.shape[1] for piece in pieces) - LAGS
    segments = width // NFFT
    chunk = 8
    span = rows + LAGS - chunk
    return pl.pallas_call(
        functools.partial(cross_kernel_pieces, segments, rows, chunk),
        out_shape=jax.ShapeDtypeStruct((rows, LAGS, NFFT), jnp.bfloat16),
        in_specs=[pl.BlockSpec(memory_space=pltpu.VMEM)] * len(pieces),
        out_specs=pl.BlockSpec(memory_space=pl.ANY),
        scratch_shapes=[
            pltpu.VMEM((rows, width), jnp.float32),
            pltpu.VMEM((chunk, span, width), jnp.float32),
            pltpu.VMEM((4, chunk, LAGS, NFFT), jnp.bfloat16),
            pltpu.SemaphoreType.DMA((4, 4)),
        ],
        cost_estimate=pl.CostEstimate(
            flops=6 * rows * LAGS * NF * segments,
            transcendentals=0,
            bytes_accessed=rows * LAGS * NFFT * 2 + 2 * (rows + LAGS) * width,
        ),
    )(*pieces)


def cross_spectra(own, extended):
    rows, segments, columns = own.shape
    reach_rows = extended.shape[0]
    own_flat = own.reshape(rows, segments * columns)
    ext_flat = extended.reshape(reach_rows, segments * columns)
    rows_per_step = 8
    span = reach_rows - rows_per_step
    scratch_bytes = rows_per_step * span * segments * columns * 4
    cost = pl.CostEstimate(
        flops=6 * rows * LAGS * NF * segments,
        transcendentals=0,
        bytes_accessed=rows * LAGS * columns * 2 + 2 * segments * (rows + reach_rows) * columns,
    )
    common = dict(
        out_shape=jax.ShapeDtypeStruct((rows, LAGS, columns), jnp.bfloat16),
        grid=(rows // rows_per_step,),
        in_specs=[
            pl.BlockSpec((rows, segments * columns), lambda i: (0, 0)),
            pl.BlockSpec((reach_rows, segments * columns), lambda i: (0, 0)),
        ],
        out_specs=pl.BlockSpec((rows_per_step, LAGS, columns), lambda i: (i, 0, 0)),
        cost_estimate=cost,
    )
    if scratch_bytes <= 8 * 1024 * 1024:
        return pl.pallas_call(
            functools.partial(cross_kernel_shifted, segments, rows_per_step),
            scratch_shapes=[
                pltpu.VMEM((rows, segments * columns), jnp.float32),
                pltpu.VMEM((rows_per_step, span, segments * columns), jnp.float32),
            ],
            compiler_params=pltpu.CompilerParams(dimension_semantics=("arbitrary",)),
            **common,
        )(own_flat, ext_flat)
    return pl.pallas_call(
        functools.partial(cross_kernel, segments, rows_per_step), **common
    )(own_flat, ext_flat)


def body(strain, filter_taps):
    extent = lax.axis_size("ta")
    columns_n = lax.axis_size("col")
    section_rows, slab = strain.shape
    block_rows = section_rows // extent
    reach = LAGS // block_rows
    turned = strain.T
    route = [(c + 1, c) for c in range(columns_n - 1)]
    following = lax.ppermute(turned, "col", route)
    tail = following[:, : reach * block_rows]
    width = (reach + 1) * block_rows
    windows = channel_windows(turned, tail, extent, width, reach * block_rows)
    gathered = lax.all_to_all(windows, "ta", split_axis=0, concat_axis=0, tiled=True)
    samples = gathered.reshape(extent * slab, width)
    filtered = decimate_t(samples.astype(jnp.float32), filter_taps)
    whitened_t = whiten_t(filtered)
    segments, columns, _ = whitened_t.shape
    if segments * 8 * width * columns * 4 <= 8 * 1024 * 1024:
        flat = whitened_t.reshape(segments * columns, width)
        return cross_spectra_pieces([flat])[None]
    extended = whitened_t.transpose(2, 0, 1)
    return cross_spectra(extended[:block_rows], extended)[None]


def solution(mesh):
    return jax.shard_map(
        body,
        mesh=mesh,
        in_specs=(P("col", "ta"), P()),
        out_specs=P("col", "ta", None, None),
        check_vma=False,
    )
```

```python
import functools

import jax
import jax.numpy as jnp
from jax import lax
from jax.experimental import pallas as pl
from jax.experimental.pallas import tpu as pltpu
from jax.sharding import PartitionSpec as P

NFFT = 256
NF = 128
LAGS = 128


def tap_rows(filter_taps, outputs):
    tap_count = filter_taps.shape[0]
    window = 2 * outputs + tap_count
    flipped = filter_taps[::-1]
    period = jnp.concatenate([flipped, jnp.zeros((window + 2 - tap_count,), jnp.float32)])
    repeated = jnp.tile(period, outputs)[: outputs * window]
    return repeated.reshape(outputs, window)


def decimate_t(samples, filter_taps):
    length, channels = samples.shape
    tap_count = filter_taps.shape[0]
    outputs = min(length, NFFT) // 2
    blocks = length // (2 * outputs)
    joined = jnp.concatenate(
        [
            jnp.zeros((tap_count, channels), jnp.float32),
            samples,
            jnp.zeros((2 * outputs - tap_count, channels), jnp.float32),
        ],
        axis=0,
    )
    joined = joined.reshape(blocks + 1, 2 * outputs, channels)
    windows = jnp.concatenate([joined[:-1], joined[1:, :tap_count]], axis=1)
    matrix = tap_rows(filter_taps, outputs)
    result = jnp.einsum("tw,bwc->btc", matrix, windows, precision=lax.Precision.HIGHEST)
    return result.reshape(blocks * outputs, channels).astype(jnp.bfloat16)


def fourier_table():
    moment = lax.broadcasted_iota(jnp.int32, (NFFT, NF), 0)
    frequency = lax.broadcasted_iota(jnp.int32, (NFFT, NF), 1) + 1
    phase_index = moment * frequency % NFFT
    angles = phase_index.astype(jnp.float32) * (2.0 * jnp.pi / NFFT)
    window_taper = 0.5 - 0.5 * jnp.cos(moment.astype(jnp.float32) * (2.0 * jnp.pi / NFFT))
    return jnp.concatenate(
        [window_taper * jnp.cos(angles), -window_taper * jnp.sin(angles)], axis=1
    )


def whiten_t(filtered):
    length, channels = filtered.shape
    pieces = filtered.reshape(length // NF, NF, channels)
    segment_rows = jnp.concatenate([pieces[:-1], pieces[1:]], axis=1)
    spectrum = jnp.einsum(
        "nf,snc->sfc",
        fourier_table(),
        segment_rows.astype(jnp.float32),
        precision=lax.Precision.HIGHEST,
    )
    real_part = spectrum[:, :NF]
    imag_part = spectrum[:, NF:]
    powers = real_part * real_part + imag_part * imag_part
    mean_power = jnp.mean(powers, axis=1, keepdims=True)
    whitening = 1.0 / jnp.sqrt(powers + mean_power + 1e-06)
    return jnp.concatenate([real_part * whitening, imag_part * whitening], axis=1).astype(
        jnp.bfloat16
    )


def windows_kernel(width, tail_rows, x_ref, out_ref):
    x = x_ref[...].astype(jnp.float32)
    padded = jnp.concatenate([x, jnp.zeros((x.shape[0], tail_rows), jnp.float32)], axis=1)
    step = (padded.shape[1] - width) // (out_ref.shape[0] - 1)
    for j in range(out_ref.shape[0]):
        out_ref[j] = padded[:, j * step : j * step + width].astype(out_ref.dtype)


def tail_windows_kernel(width, count, x_ref, tail_ref, windows_hbm, out_hbm, fresh, sem):
    del windows_hbm
    x = x_ref[...].astype(jnp.float32)
    tail = tail_ref[...].astype(jnp.float32)
    extent = out_hbm.shape[0]
    rows = x.shape[1]
    step = (rows + tail.shape[1] - width) // (extent - 1)
    first = extent - count
    padded = jnp.concatenate([x[:, first * step :], tail], axis=1)
    for j in range(count):
        fresh[j] = padded[:, j * step : j * step + width].astype(fresh.dtype)
    copy = pltpu.make_async_copy(fresh, out_hbm.at[pl.ds(first, count)], sem)
    copy.start()
    copy.wait()


def channel_windows(turned, tail, extent, width, tail_rows):
    slab, rows = turned.shape
    windows = pl.pallas_call(
        functools.partial(windows_kernel, width, tail_rows),
        out_shape=jax.ShapeDtypeStruct((extent, slab, width), turned.dtype),
        cost_estimate=pl.CostEstimate(
            flops=0, transcendentals=0, bytes_accessed=2 * (slab * rows + extent * slab * width)
        ),
    )(turned)
    count = -(-tail_rows // ((rows + tail_rows - width) // (extent - 1)))
    return pl.pallas_call(
        functools.partial(tail_windows_kernel, width, count),
        out_shape=jax.ShapeDtypeStruct((extent, slab, width), turned.dtype),
        in_specs=[
            pl.BlockSpec(memory_space=pltpu.VMEM),
            pl.BlockSpec(memory_space=pltpu.VMEM),
            pl.BlockSpec(memory_space=pl.ANY),
        ],
        out_specs=pl.BlockSpec(memory_space=pl.ANY),
        scratch_shapes=[
            pltpu.VMEM((count, slab, width), turned.dtype),
            pltpu.SemaphoreType.DMA(()),
        ],
        input_output_aliases={2: 0},
        cost_estimate=pl.CostEstimate(
            flops=0, transcendentals=0, bytes_accessed=2 * (slab * rows + 2 * count * slab * width)
        ),
    )(turned, tail, windows)


def cross_kernel(segments, rows_per_step, own_ref, ext_ref, out_ref):
    step = pl.program_id(0)
    base = pl.multiple_of(step * rows_per_step, rows_per_step)
    for i in range(rows_per_step):
        acc_re = None
        acc_im = None
        for s in range(segments):
            a = own_ref[pl.ds(base, rows_per_step), pl.ds(s * NFFT, NFFT)]
            a = a.astype(jnp.float32)[i : i + 1]
            window = ext_ref[pl.ds(base, LAGS + rows_per_step), pl.ds(s * NFFT, NFFT)]
            b = window.astype(jnp.float32)[i : i + LAGS]
            terms = product_terms(a, b)
            if acc_re is None:
                acc_re, acc_im = terms
            else:
                acc_re = [x + y for x, y in zip(acc_re, terms[0])]
                acc_im = [x + y for x, y in zip(acc_im, terms[1])]
        store_row(out_ref, i, acc_re, acc_im, segments)


def product_terms(a, b):
    ar = a[:, :NF]
    ai = a[:, NF:]
    br = b[:, :NF]
    bi = b[:, NF:]
    return [ar * br, ai * bi], [ai * br, ar * bi]


def store_row(out_ref, i, acc_re, acc_im, segments):
    re = acc_re[0] + acc_re[1]
    im = acc_im[0] - acc_im[1]
    if segments > 1:
        re = re / segments
        im = im / segments
    out_ref[i, :, :NF] = re.astype(out_ref.dtype)
    out_ref[i, :, NF:] = im.astype(out_ref.dtype)


def cross_kernel_shifted(segments, rows_per_step, own_ref, ext_ref, out_ref, own_f32, shifted):
    step = pl.program_id(0)
    span = shifted.shape[1]

    @pl.when(step == 0)
    def _():
        own_f32[...] = own_ref[...].astype(jnp.float32)
        whole = ext_ref[...].astype(jnp.float32)
        for i in range(rows_per_step):
            shifted[i] = whole[i : i + span]

    base = pl.multiple_of(step * rows_per_step, rows_per_step)
    for i in range(rows_per_step):
        acc_re = None
        acc_im = None
        for s in range(segments):
            a = own_f32[pl.ds(base + i, 1), pl.ds(s * NFFT, NFFT)]
            b = shifted[i, pl.ds(base, LAGS), pl.ds(s * NFFT, NFFT)]
            terms = product_terms(a, b)
            if acc_re is None:
                acc_re, acc_im = terms
            else:
                acc_re = [x + y for x, y in zip(acc_re, terms[0])]
                acc_im = [x + y for x, y in zip(acc_im, terms[1])]
        store_row(out_ref, i, acc_re, acc_im, segments)


def cross_kernel_pieces(segments, rows, chunk, *refs):
    pieces = refs[:-5]
    out_hbm, own_f32, shifted, buffers, sems = refs[-5:]
    span = shifted.shape[1]
    extended = jnp.concatenate(
        [
            jnp.concatenate(
                [piece[s * NFFT : (s + 1) * NFFT, :].astype(jnp.float32).T for s in range(segments)],
                axis=1,
            )
            for piece in pieces
        ],
        axis=0,
    )
    own_f32[...] = extended[:rows]
    for i in range(chunk):
        shifted[i] = extended[i : i + span]
    slots, parts = buffers.shape[0], sems.shape[1]
    part = chunk // parts
    copies = []
    for m in range(rows // chunk):
        slot = m % slots
        if m >= slots:
            for copy in copies[m - slots]:
                copy.wait()
        base = m * chunk
        for i in range(chunk):
            acc_re = None
            acc_im = None
            for s in range(segments):
                a = own_f32[base + i : base + i + 1, s * NFFT : (s + 1) * NFFT]
                b = shifted[i, base : base + LAGS, s * NFFT : (s + 1) * NFFT]
                terms = product_terms(a, b)
                if acc_re is None:
                    acc_re, acc_im = terms
                else:
                    acc_re = [x + y for x, y in zip(acc_re, terms[0])]
                    acc_im = [x + y for x, y in zip(acc_im, terms[1])]
            store_row(buffers.at[slot], i, acc_re, acc_im, segments)
        group = []
        for p in range(parts):
            copy = pltpu.make_async_copy(
                buffers.at[slot, pl.ds(p * part, part)],
                out_hbm.at[pl.ds(base + p * part, part)],
                sems.at[slot, p],
            )
            copy.start()
            group.append(copy)
        copies.append(group)
    for group in copies[-slots:]:
        for copy in group:
            copy.wait()


def cross_spectra_pieces(pieces):
    width = pieces[0].shape[0]
    rows = sum(piece.shape[1] for piece in pieces) - LAGS
    segments = width // NFFT
    chunk = 8
    span = rows + LAGS - chunk
    return pl.pallas_call(
        functools.partial(cross_kernel_pieces, segments, rows, chunk),
        out_shape=jax.ShapeDtypeStruct((rows, LAGS, NFFT), jnp.bfloat16),
        in_specs=[pl.BlockSpec(memory_space=pltpu.VMEM)] * len(pieces),
        out_specs=pl.BlockSpec(memory_space=pl.ANY),
        scratch_shapes=[
            pltpu.VMEM((rows, width), jnp.float32),
            pltpu.VMEM((chunk, span, width), jnp.float32),
            pltpu.VMEM((4, chunk, LAGS, NFFT), jnp.bfloat16),
            pltpu.SemaphoreType.DMA((4, 4)),
        ],
        cost_estimate=pl.CostEstimate(
            flops=6 * rows * LAGS * NF * segments,
            transcendentals=0,
            bytes_accessed=rows * LAGS * NFFT * 2 + 2 * (rows + LAGS) * width,
        ),
    )(*pieces)


def fused_kernel(rows, chunk, samples_ref, matrix_ref, table_ref, out_hbm, own_f32, shifted,
                 buffers, sems):
    tap_count = matrix_ref.shape[1] - matrix_ref.shape[0] * 2
    outputs = matrix_ref.shape[0]
    length, channels = samples_ref.shape
    blocks = length // (2 * outputs)
    x = samples_ref[...].astype(jnp.float32)
    joined = jnp.concatenate(
        [
            jnp.zeros((tap_count, channels), jnp.float32),
            x,
            jnp.zeros((2 * outputs - tap_count, channels), jnp.float32),
        ],
        axis=0,
    )
    matrix = matrix_ref[...]
    filtered = jnp.concatenate(
        [
            jnp.dot(
                matrix,
                joined[b * 2 * outputs : b * 2 * outputs + 2 * outputs + tap_count],
                precision=lax.Precision.HIGHEST,
                preferred_element_type=jnp.float32,
            )
            for b in range(blocks)
        ],
        axis=0,
    )
    filtered = filtered.astype(jnp.bfloat16).astype(jnp.float32)
    spectrum = jnp.dot(
        table_ref[...], filtered, precision=lax.Precision.HIGHEST, preferred_element_type=jnp.float32
    )
    real_part = spectrum[:NF]
    imag_part = spectrum[NF:]
    powers = real_part * real_part + imag_part * imag_part
    mean_power = jnp.mean(powers, axis=0, keepdims=True)
    whitening = 1.0 / jnp.sqrt(powers + mean_power + 1e-06)
    whitened = jnp.concatenate([real_part * whitening, imag_part * whitening], axis=0)
    extended = whitened.astype(jnp.bfloat16).astype(jnp.float32).T
    span = shifted.shape[1]
    own_f32[...] = extended[:rows]
    for i in range(chunk):
        shifted[i] = extended[i : i + span]
    slots, parts = buffers.shape[0], sems.shape[1]
    part = chunk // parts
    copies = []
    for m in range(rows // chunk):
        slot = m % slots
        if m >= slots:
            for copy in copies[m - slots]:
                copy.wait()
        base = m * chunk
        for i in range(chunk):
            a = own_f32[base + i : base + i + 1, :]
            b = shifted[i, base : base + LAGS, :]
            acc_re, acc_im = product_terms(a, b)
            store_row(buffers.at[slot], i, acc_re, acc_im, 1)
        group = []
        for p in range(parts):
            copy = pltpu.make_async_copy(
                buffers.at[slot, pl.ds(p * part, part)],
                out_hbm.at[pl.ds(base + p * part, part)],
                sems.at[slot, p],
            )
            copy.start()
            group.append(copy)
        copies.append(group)
    for group in copies[-slots:]:
        for copy in group:
            copy.wait()


def fused_spectra(samples, matrix, table_t, rows):
    length, channels = samples.shape
    chunk = 8
    span = channels - chunk
    return pl.pallas_call(
        functools.partial(fused_kernel, rows, chunk),
        out_shape=jax.ShapeDtypeStruct((rows, LAGS, NFFT), jnp.bfloat16),
        in_specs=[pl.BlockSpec(memory_space=pltpu.VMEM)] * 3,
        out_specs=pl.BlockSpec(memory_space=pl.ANY),
        scratch_shapes=[
            pltpu.VMEM((rows, NFFT), jnp.float32),
            pltpu.VMEM((chunk, span, NFFT), jnp.float32),
            pltpu.VMEM((4, chunk, LAGS, NFFT), jnp.bfloat16),
            pltpu.SemaphoreType.DMA((4, 4)),
        ],
        cost_estimate=pl.CostEstimate(
            flops=6 * rows * LAGS * NF + 12 * channels * (matrix.size * length // 256 + NFFT * NFFT),
            transcendentals=2 * NF * channels,
            bytes_accessed=rows * LAGS * NFFT * 2 + 2 * samples.size + 4 * (matrix.size + table_t.size),
        ),
    )(samples, matrix, table_t)


def cross_spectra(own, extended):
    rows, segments, columns = own.shape
    reach_rows = extended.shape[0]
    own_flat = own.reshape(rows, segments * columns)
    ext_flat = extended.reshape(reach_rows, segments * columns)
    rows_per_step = 8
    span = reach_rows - rows_per_step
    scratch_bytes = rows_per_step * span * segments * columns * 4
    cost = pl.CostEstimate(
        flops=6 * rows * LAGS * NF * segments,
        transcendentals=0,
        bytes_accessed=rows * LAGS * columns * 2 + 2 * segments * (rows + reach_rows) * columns,
    )
    common = dict(
        out_shape=jax.ShapeDtypeStruct((rows, LAGS, columns), jnp.bfloat16),
        grid=(rows // rows_per_step,),
        in_specs=[
            pl.BlockSpec((rows, segments * columns), lambda i: (0, 0)),
            pl.BlockSpec((reach_rows, segments * columns), lambda i: (0, 0)),
        ],
        out_specs=pl.BlockSpec((rows_per_step, LAGS, columns), lambda i: (i, 0, 0)),
        cost_estimate=cost,
    )
    if scratch_bytes <= 8 * 1024 * 1024:
        return pl.pallas_call(
            functools.partial(cross_kernel_shifted, segments, rows_per_step),
            scratch_shapes=[
                pltpu.VMEM((rows, segments * columns), jnp.float32),
                pltpu.VMEM((rows_per_step, span, segments * columns), jnp.float32),
            ],
            compiler_params=pltpu.CompilerParams(dimension_semantics=("arbitrary",)),
            **common,
        )(own_flat, ext_flat)
    return pl.pallas_call(
        functools.partial(cross_kernel, segments, rows_per_step), **common
    )(own_flat, ext_flat)


def body(strain, filter_taps):
    extent = lax.axis_size("ta")
    columns_n = lax.axis_size("col")
    section_rows, slab = strain.shape
    block_rows = section_rows // extent
    reach = LAGS // block_rows
    turned = strain.T
    route = [(c + 1, c) for c in range(columns_n - 1)]
    following = lax.ppermute(turned, "col", route)
    tail = following[:, : reach * block_rows]
    width = (reach + 1) * block_rows
    windows = channel_windows(turned, tail, extent, width, reach * block_rows)
    gathered = lax.all_to_all(windows, "ta", split_axis=0, concat_axis=0, tiled=True)
    samples = gathered.reshape(extent * slab, width)
    if extent * slab == 2 * NFFT:
        matrix = tap_rows(filter_taps, NFFT // 2)
        return fused_spectra(samples, matrix, fourier_table().T, block_rows)[None]
    filtered = decimate_t(samples.astype(jnp.float32), filter_taps)
    whitened_t = whiten_t(filtered)
    segments, columns, _ = whitened_t.shape
    if segments * 8 * width * columns * 4 <= 8 * 1024 * 1024:
        flat = whitened_t.reshape(segments * columns, width)
        return cross_spectra_pieces([flat])[None]
    extended = whitened_t.transpose(2, 0, 1)
    return cross_spectra(extended[:block_rows], extended)[None]


def solution(mesh):
    return jax.shard_map(
        body,
        mesh=mesh,
        in_specs=(P("col", "ta"), P()),
        out_specs=P("col", "ta", None, None),
        check_vma=False,
    )
```

```python
import functools

import jax
import jax.numpy as jnp
from jax import lax
from jax.experimental import pallas as pl
from jax.experimental.pallas import tpu as pltpu
from jax.sharding import PartitionSpec as P

NFFT = 256
NF = 128
LAGS = 128


def tap_rows(filter_taps, outputs):
    tap_count = filter_taps.shape[0]
    window = 2 * outputs + tap_count
    flipped = filter_taps[::-1]
    period = jnp.concatenate([flipped, jnp.zeros((window + 2 - tap_count,), jnp.float32)])
    repeated = jnp.tile(period, outputs)[: outputs * window]
    return repeated.reshape(outputs, window)


def decimate_t(samples, filter_taps):
    length, channels = samples.shape
    tap_count = filter_taps.shape[0]
    outputs = min(length, NFFT) // 2
    blocks = length // (2 * outputs)
    joined = jnp.concatenate(
        [
            jnp.zeros((tap_count, channels), jnp.float32),
            samples,
            jnp.zeros((2 * outputs - tap_count, channels), jnp.float32),
        ],
        axis=0,
    )
    joined = joined.reshape(blocks + 1, 2 * outputs, channels)
    windows = jnp.concatenate([joined[:-1], joined[1:, :tap_count]], axis=1)
    matrix = tap_rows(filter_taps, outputs)
    result = jnp.einsum("tw,bwc->btc", matrix, windows, precision=lax.Precision.HIGHEST)
    return result.reshape(blocks * outputs, channels).astype(jnp.bfloat16)


def fourier_table():
    moment = lax.broadcasted_iota(jnp.int32, (NFFT, NF), 0)
    frequency = lax.broadcasted_iota(jnp.int32, (NFFT, NF), 1) + 1
    phase_index = moment * frequency % NFFT
    angles = phase_index.astype(jnp.float32) * (2.0 * jnp.pi / NFFT)
    window_taper = 0.5 - 0.5 * jnp.cos(moment.astype(jnp.float32) * (2.0 * jnp.pi / NFFT))
    return jnp.concatenate(
        [window_taper * jnp.cos(angles), -window_taper * jnp.sin(angles)], axis=1
    )


def fourier_table_t():
    moment = lax.broadcasted_iota(jnp.int32, (NFFT, NFFT), 1)
    frequency = lax.broadcasted_iota(jnp.int32, (NFFT, NFFT), 0) % NF + 1
    phase_index = moment * frequency % NFFT
    angles = phase_index.astype(jnp.float32) * (2.0 * jnp.pi / NFFT)
    window_taper = 0.5 - 0.5 * jnp.cos(moment.astype(jnp.float32) * (2.0 * jnp.pi / NFFT))
    real_rows = lax.broadcasted_iota(jnp.int32, (NFFT, NFFT), 0) < NF
    return jnp.where(real_rows, window_taper * jnp.cos(angles), -window_taper * jnp.sin(angles))


def whiten_t(filtered):
    length, channels = filtered.shape
    pieces = filtered.reshape(length // NF, NF, channels)
    segment_rows = jnp.concatenate([pieces[:-1], pieces[1:]], axis=1)
    spectrum = jnp.einsum(
        "nf,snc->sfc",
        fourier_table(),
        segment_rows.astype(jnp.float32),
        precision=lax.Precision.HIGHEST,
    )
    real_part = spectrum[:, :NF]
    imag_part = spectrum[:, NF:]
    powers = real_part * real_part + imag_part * imag_part
    mean_power = jnp.mean(powers, axis=1, keepdims=True)
    whitening = 1.0 / jnp.sqrt(powers + mean_power + 1e-06)
    return jnp.concatenate([real_part * whitening, imag_part * whitening], axis=1).astype(
        jnp.bfloat16
    )


def windows_kernel(width, tail_rows, x_ref, out_ref):
    x = x_ref[...].astype(jnp.float32)
    padded = jnp.concatenate([x, jnp.zeros((x.shape[0], tail_rows), jnp.float32)], axis=1)
    step = (padded.shape[1] - width) // (out_ref.shape[0] - 1)
    for j in range(out_ref.shape[0]):
        out_ref[j] = padded[:, j * step : j * step + width].astype(out_ref.dtype)


def tail_windows_kernel(width, count, x_ref, tail_ref, windows_hbm, out_hbm, fresh, sem):
    del windows_hbm
    x = x_ref[...].astype(jnp.float32)
    tail = tail_ref[...].astype(jnp.float32)
    extent = out_hbm.shape[0]
    rows = x.shape[1]
    step = (rows + tail.shape[1] - width) // (extent - 1)
    first = extent - count
    padded = jnp.concatenate([x[:, first * step :], tail], axis=1)
    for j in range(count):
        fresh[j] = padded[:, j * step : j * step + width].astype(fresh.dtype)
    copy = pltpu.make_async_copy(fresh, out_hbm.at[pl.ds(first, count)], sem)
    copy.start()
    copy.wait()


def channel_windows(turned, tail, extent, width, tail_rows):
    slab, rows = turned.shape
    windows = pl.pallas_call(
        functools.partial(windows_kernel, width, tail_rows),
        out_shape=jax.ShapeDtypeStruct((extent, slab, width), turned.dtype),
        cost_estimate=pl.CostEstimate(
            flops=0, transcendentals=0, bytes_accessed=2 * (slab * rows + extent * slab * width)
        ),
    )(turned)
    count = -(-tail_rows // ((rows + tail_rows - width) // (extent - 1)))
    return pl.pallas_call(
        functools.partial(tail_windows_kernel, width, count),
        out_shape=jax.ShapeDtypeStruct((extent, slab, width), turned.dtype),
        in_specs=[
            pl.BlockSpec(memory_space=pltpu.VMEM),
            pl.BlockSpec(memory_space=pltpu.VMEM),
            pl.BlockSpec(memory_space=pl.ANY),
        ],
        out_specs=pl.BlockSpec(memory_space=pl.ANY),
        scratch_shapes=[
            pltpu.VMEM((count, slab, width), turned.dtype),
            pltpu.SemaphoreType.DMA(()),
        ],
        input_output_aliases={2: 0},
        cost_estimate=pl.CostEstimate(
            flops=0, transcendentals=0, bytes_accessed=2 * (slab * rows + 2 * count * slab * width)
        ),
    )(turned, tail, windows)


def cross_kernel(segments, rows_per_step, own_ref, ext_ref, out_ref):
    step = pl.program_id(0)
    base = pl.multiple_of(step * rows_per_step, rows_per_step)
    for i in range(rows_per_step):
        acc_re = None
        acc_im = None
        for s in range(segments):
            a = own_ref[pl.ds(base, rows_per_step), pl.ds(s * NFFT, NFFT)]
            a = a.astype(jnp.float32)[i : i + 1]
            window = ext_ref[pl.ds(base, LAGS + rows_per_step), pl.ds(s * NFFT, NFFT)]
            b = window.astype(jnp.float32)[i : i + LAGS]
            terms = product_terms(a, b)
            if acc_re is None:
                acc_re, acc_im = terms
            else:
                acc_re = [x + y for x, y in zip(acc_re, terms[0])]
                acc_im = [x + y for x, y in zip(acc_im, terms[1])]
        store_row(out_ref, i, acc_re, acc_im, segments)


def product_terms(a, b):
    ar = a[:, :NF]
    ai = a[:, NF:]
    br = b[:, :NF]
    bi = b[:, NF:]
    return [ar * br, ai * bi], [ai * br, ar * bi]


def store_row(out_ref, i, acc_re, acc_im, segments):
    re = acc_re[0] + acc_re[1]
    im = acc_im[0] - acc_im[1]
    if segments > 1:
        re = re / segments
        im = im / segments
    out_ref[i, :, :NF] = re.astype(out_ref.dtype)
    out_ref[i, :, NF:] = im.astype(out_ref.dtype)


def cross_kernel_shifted(segments, rows_per_step, own_ref, ext_ref, out_ref, own_f32, shifted):
    step = pl.program_id(0)
    span = shifted.shape[1]

    @pl.when(step == 0)
    def _():
        own_f32[...] = own_ref[...].astype(jnp.float32)
        whole = ext_ref[...].astype(jnp.float32)
        for i in range(rows_per_step):
            shifted[i] = whole[i : i + span]

    base = pl.multiple_of(step * rows_per_step, rows_per_step)
    for i in range(rows_per_step):
        acc_re = None
        acc_im = None
        for s in range(segments):
            a = own_f32[pl.ds(base + i, 1), pl.ds(s * NFFT, NFFT)]
            b = shifted[i, pl.ds(base, LAGS), pl.ds(s * NFFT, NFFT)]
            terms = product_terms(a, b)
            if acc_re is None:
                acc_re, acc_im = terms
            else:
                acc_re = [x + y for x, y in zip(acc_re, terms[0])]
                acc_im = [x + y for x, y in zip(acc_im, terms[1])]
        store_row(out_ref, i, acc_re, acc_im, segments)


def cross_kernel_pieces(segments, rows, chunk, *refs):
    pieces = refs[:-5]
    out_hbm, own_f32, shifted, buffers, sems = refs[-5:]
    span = shifted.shape[1]
    extended = jnp.concatenate(
        [
            jnp.concatenate(
                [piece[s * NFFT : (s + 1) * NFFT, :].astype(jnp.float32).T for s in range(segments)],
                axis=1,
            )
            for piece in pieces
        ],
        axis=0,
    )
    own_f32[...] = extended[:rows]
    for i in range(chunk):
        shifted[i] = extended[i : i + span]
    slots, parts = buffers.shape[0], sems.shape[1]
    part = chunk // parts
    copies = []
    for m in range(rows // chunk):
        slot = m % slots
        if m >= slots:
            for copy in copies[m - slots]:
                copy.wait()
        base = m * chunk
        for i in range(chunk):
            acc_re = None
            acc_im = None
            for s in range(segments):
                a = own_f32[base + i : base + i + 1, s * NFFT : (s + 1) * NFFT]
                b = shifted[i, base : base + LAGS, s * NFFT : (s + 1) * NFFT]
                terms = product_terms(a, b)
                if acc_re is None:
                    acc_re, acc_im = terms
                else:
                    acc_re = [x + y for x, y in zip(acc_re, terms[0])]
                    acc_im = [x + y for x, y in zip(acc_im, terms[1])]
            store_row(buffers.at[slot], i, acc_re, acc_im, segments)
        group = []
        for p in range(parts):
            copy = pltpu.make_async_copy(
                buffers.at[slot, pl.ds(p * part, part)],
                out_hbm.at[pl.ds(base + p * part, part)],
                sems.at[slot, p],
            )
            copy.start()
            group.append(copy)
        copies.append(group)
    for group in copies[-slots:]:
        for copy in group:
            copy.wait()


def cross_spectra_pieces(pieces):
    width = pieces[0].shape[0]
    rows = sum(piece.shape[1] for piece in pieces) - LAGS
    segments = width // NFFT
    chunk = 8
    span = rows + LAGS - chunk
    return pl.pallas_call(
        functools.partial(cross_kernel_pieces, segments, rows, chunk),
        out_shape=jax.ShapeDtypeStruct((rows, LAGS, NFFT), jnp.bfloat16),
        in_specs=[pl.BlockSpec(memory_space=pltpu.VMEM)] * len(pieces),
        out_specs=pl.BlockSpec(memory_space=pl.ANY),
        scratch_shapes=[
            pltpu.VMEM((rows, width), jnp.float32),
            pltpu.VMEM((chunk, span, width), jnp.float32),
            pltpu.VMEM((4, chunk, LAGS, NFFT), jnp.bfloat16),
            pltpu.SemaphoreType.DMA((4, 4)),
        ],
        cost_estimate=pl.CostEstimate(
            flops=6 * rows * LAGS * NF * segments,
            transcendentals=0,
            bytes_accessed=rows * LAGS * NFFT * 2 + 2 * (rows + LAGS) * width,
        ),
    )(*pieces)


def fused_kernel(rows, chunk, taps_ref, samples_ref, table_ref, out_hbm, own_f32, shifted,
                 buffers, sems):
    tap_count = taps_ref.shape[0]
    outputs = NFFT // 2
    length, channels = samples_ref.shape
    blocks = length // (2 * outputs)
    lanes = 3 * NF
    lane = lax.broadcasted_iota(jnp.int32, (1, lanes), 1)
    row = jnp.zeros((1, lanes), jnp.float32)
    for k in range(tap_count):
        row = jnp.where(lane == tap_count - 1 - k, taps_ref[k], row)
    rolled = pltpu.roll(
        jnp.broadcast_to(row, (outputs, lanes)), 0, 1, stride=2, stride_axis=0
    )
    matrix = rolled[:, : 2 * outputs + tap_count]
    x = samples_ref[...].astype(jnp.float32)
    joined = jnp.concatenate(
        [
            jnp.zeros((tap_count, channels), jnp.float32),
            x,
            jnp.zeros((2 * outputs - tap_count, channels), jnp.float32),
        ],
        axis=0,
    )
    filtered = jnp.concatenate(
        [
            jnp.dot(
                matrix,
                joined[b * 2 * outputs : b * 2 * outputs + 2 * outputs + tap_count],
                precision=lax.Precision.HIGHEST,
                preferred_element_type=jnp.float32,
            )
            for b in range(blocks)
        ],
        axis=0,
    )
    filtered = filtered.astype(jnp.bfloat16).astype(jnp.float32)
    spectrum = jnp.dot(
        table_ref[...], filtered, precision=lax.Precision.HIGHEST, preferred_element_type=jnp.float32
    )
    real_part = spectrum[:NF]
    imag_part = spectrum[NF:]
    powers = real_part * real_part + imag_part * imag_part
    mean_power = jnp.mean(powers, axis=0, keepdims=True)
    whitening = 1.0 / jnp.sqrt(powers + mean_power + 1e-06)
    whitened = jnp.concatenate([real_part * whitening, imag_part * whitening], axis=0)
    extended = whitened.astype(jnp.bfloat16).astype(jnp.float32).T
    span = shifted.shape[1]
    own_f32[...] = extended[:rows]
    for i in range(chunk):
        shifted[i] = extended[i : i + span]
    slots, parts = buffers.shape[0], sems.shape[1]
    part = chunk // parts
    copies = []
    for m in range(rows // chunk):
        slot = m % slots
        if m >= slots:
            for copy in copies[m - slots]:
                copy.wait()
        base = m * chunk
        for i in range(chunk):
            a = own_f32[base + i : base + i + 1, :]
            b = shifted[i, base : base + LAGS, :]
            acc_re, acc_im = product_terms(a, b)
            store_row(buffers.at[slot], i, acc_re, acc_im, 1)
        group = []
        for p in range(parts):
            copy = pltpu.make_async_copy(
                buffers.at[slot, pl.ds(p * part, part)],
                out_hbm.at[pl.ds(base + p * part, part)],
                sems.at[slot, p],
            )
            copy.start()
            group.append(copy)
        copies.append(group)
    for group in copies[-slots:]:
        for copy in group:
            copy.wait()


def fused_spectra(samples, filter_taps, table_t, rows):
    length, channels = samples.shape
    chunk = 8
    span = channels - chunk
    return pl.pallas_call(
        functools.partial(fused_kernel, rows, chunk),
        out_shape=jax.ShapeDtypeStruct((rows, LAGS, NFFT), jnp.bfloat16),
        in_specs=[pl.BlockSpec(memory_space=pltpu.SMEM)] + [pl.BlockSpec(memory_space=pltpu.VMEM)] * 2,
        out_specs=pl.BlockSpec(memory_space=pl.ANY),
        scratch_shapes=[
            pltpu.VMEM((rows, NFFT), jnp.float32),
            pltpu.VMEM((chunk, span, NFFT), jnp.float32),
            pltpu.VMEM((4, chunk, LAGS, NFFT), jnp.bfloat16),
            pltpu.SemaphoreType.DMA((4, 4)),
        ],
        cost_estimate=pl.CostEstimate(
            flops=6 * rows * LAGS * NF + 12 * channels * (NF * 320 * length // 256 + NFFT * NFFT),
            transcendentals=2 * NF * channels,
            bytes_accessed=rows * LAGS * NFFT * 2 + 2 * samples.size + 4 * table_t.size,
        ),
    )(filter_taps, samples, table_t)


def cross_spectra(own, extended):
    rows, segments, columns = own.shape
    reach_rows = extended.shape[0]
    own_flat = own.reshape(rows, segments * columns)
    ext_flat = extended.reshape(reach_rows, segments * columns)
    rows_per_step = 8
    span = reach_rows - rows_per_step
    scratch_bytes = rows_per_step * span * segments * columns * 4
    cost = pl.CostEstimate(
        flops=6 * rows * LAGS * NF * segments,
        transcendentals=0,
        bytes_accessed=rows * LAGS * columns * 2 + 2 * segments * (rows + reach_rows) * columns,
    )
    common = dict(
        out_shape=jax.ShapeDtypeStruct((rows, LAGS, columns), jnp.bfloat16),
        grid=(rows // rows_per_step,),
        in_specs=[
            pl.BlockSpec((rows, segments * columns), lambda i: (0, 0)),
            pl.BlockSpec((reach_rows, segments * columns), lambda i: (0, 0)),
        ],
        out_specs=pl.BlockSpec((rows_per_step, LAGS, columns), lambda i: (i, 0, 0)),
        cost_estimate=cost,
    )
    if scratch_bytes <= 8 * 1024 * 1024:
        return pl.pallas_call(
            functools.partial(cross_kernel_shifted, segments, rows_per_step),
            scratch_shapes=[
                pltpu.VMEM((rows, segments * columns), jnp.float32),
                pltpu.VMEM((rows_per_step, span, segments * columns), jnp.float32),
            ],
            compiler_params=pltpu.CompilerParams(dimension_semantics=("arbitrary",)),
            **common,
        )(own_flat, ext_flat)
    return pl.pallas_call(
        functools.partial(cross_kernel, segments, rows_per_step), **common
    )(own_flat, ext_flat)


def body(strain, filter_taps):
    extent = lax.axis_size("ta")
    columns_n = lax.axis_size("col")
    section_rows, slab = strain.shape
    block_rows = section_rows // extent
    reach = LAGS // block_rows
    turned = strain.T
    route = [(c + 1, c) for c in range(columns_n - 1)]
    following = lax.ppermute(turned, "col", route)
    tail = following[:, : reach * block_rows]
    width = (reach + 1) * block_rows
    windows = channel_windows(turned, tail, extent, width, reach * block_rows)
    gathered = lax.all_to_all(windows, "ta", split_axis=0, concat_axis=0, tiled=True)
    samples = gathered.reshape(extent * slab, width)
    if extent * slab == 2 * NFFT:
        return fused_spectra(samples, filter_taps, fourier_table_t(), block_rows)[None]
    filtered = decimate_t(samples.astype(jnp.float32), filter_taps)
    whitened_t = whiten_t(filtered)
    segments, columns, _ = whitened_t.shape
    if segments * 8 * width * columns * 4 <= 8 * 1024 * 1024:
        flat = whitened_t.reshape(segments * columns, width)
        return cross_spectra_pieces([flat])[None]
    extended = whitened_t.transpose(2, 0, 1)
    return cross_spectra(extended[:block_rows], extended)[None]


def solution(mesh):
    return jax.shard_map(
        body,
        mesh=mesh,
        in_specs=(P("col", "ta"), P()),
        out_specs=P("col", "ta", None, None),
        check_vma=False,
    )
```

```python
import functools

import jax
import jax.numpy as jnp
from jax import lax
from jax.experimental import pallas as pl
from jax.experimental.pallas import tpu as pltpu
from jax.sharding import PartitionSpec as P

NFFT = 256
NF = 128
LAGS = 128


def tap_rows(filter_taps, outputs):
    tap_count = filter_taps.shape[0]
    window = 2 * outputs + tap_count
    flipped = filter_taps[::-1]
    period = jnp.concatenate([flipped, jnp.zeros((window + 2 - tap_count,), jnp.float32)])
    repeated = jnp.tile(period, outputs)[: outputs * window]
    return repeated.reshape(outputs, window)


def decimate_t(samples, filter_taps):
    length, channels = samples.shape
    tap_count = filter_taps.shape[0]
    outputs = min(length, NFFT) // 2
    blocks = length // (2 * outputs)
    joined = jnp.concatenate(
        [
            jnp.zeros((tap_count, channels), jnp.float32),
            samples,
            jnp.zeros((2 * outputs - tap_count, channels), jnp.float32),
        ],
        axis=0,
    )
    joined = joined.reshape(blocks + 1, 2 * outputs, channels)
    windows = jnp.concatenate([joined[:-1], joined[1:, :tap_count]], axis=1)
    matrix = tap_rows(filter_taps, outputs)
    result = jnp.einsum("tw,bwc->btc", matrix, windows, precision=lax.Precision.HIGHEST)
    return result.reshape(blocks * outputs, channels).astype(jnp.bfloat16)


def fourier_table():
    moment = lax.broadcasted_iota(jnp.int32, (NFFT, NF), 0)
    frequency = lax.broadcasted_iota(jnp.int32, (NFFT, NF), 1) + 1
    phase_index = moment * frequency % NFFT
    angles = phase_index.astype(jnp.float32) * (2.0 * jnp.pi / NFFT)
    window_taper = 0.5 - 0.5 * jnp.cos(moment.astype(jnp.float32) * (2.0 * jnp.pi / NFFT))
    return jnp.concatenate(
        [window_taper * jnp.cos(angles), -window_taper * jnp.sin(angles)], axis=1
    )


def fourier_table_t():
    moment = lax.broadcasted_iota(jnp.int32, (NFFT, NFFT), 1)
    frequency = lax.broadcasted_iota(jnp.int32, (NFFT, NFFT), 0) % NF + 1
    phase_index = moment * frequency % NFFT
    angles = phase_index.astype(jnp.float32) * (2.0 * jnp.pi / NFFT)
    window_taper = 0.5 - 0.5 * jnp.cos(moment.astype(jnp.float32) * (2.0 * jnp.pi / NFFT))
    real_rows = lax.broadcasted_iota(jnp.int32, (NFFT, NFFT), 0) < NF
    return jnp.where(real_rows, window_taper * jnp.cos(angles), -window_taper * jnp.sin(angles))


def whiten_t(filtered):
    length, channels = filtered.shape
    pieces = filtered.reshape(length // NF, NF, channels)
    segment_rows = jnp.concatenate([pieces[:-1], pieces[1:]], axis=1)
    spectrum = jnp.einsum(
        "nf,snc->sfc",
        fourier_table(),
        segment_rows.astype(jnp.float32),
        precision=lax.Precision.HIGHEST,
    )
    real_part = spectrum[:, :NF]
    imag_part = spectrum[:, NF:]
    powers = real_part * real_part + imag_part * imag_part
    mean_power = jnp.mean(powers, axis=1, keepdims=True)
    whitening = 1.0 / jnp.sqrt(powers + mean_power + 1e-06)
    return jnp.concatenate([real_part * whitening, imag_part * whitening], axis=1).astype(
        jnp.bfloat16
    )


def windows_kernel(width, tail_rows, x_ref, out_ref):
    x = x_ref[...].astype(jnp.float32)
    padded = jnp.concatenate([x, jnp.zeros((x.shape[0], tail_rows), jnp.float32)], axis=1)
    step = (padded.shape[1] - width) // (out_ref.shape[0] - 1)
    for j in range(out_ref.shape[0]):
        out_ref[j] = padded[:, j * step : j * step + width].astype(out_ref.dtype)


def tail_windows_kernel(width, count, x_ref, tail_ref, windows_hbm, out_hbm, fresh, sem):
    del windows_hbm
    x = x_ref[...].astype(jnp.float32)
    tail = tail_ref[...].astype(jnp.float32)
    extent = out_hbm.shape[0]
    rows = x.shape[1]
    step = (rows + tail.shape[1] - width) // (extent - 1)
    first = extent - count
    padded = jnp.concatenate([x[:, first * step :], tail], axis=1)
    for j in range(count):
        fresh[j] = padded[:, j * step : j * step + width].astype(fresh.dtype)
    copy = pltpu.make_async_copy(fresh, out_hbm.at[pl.ds(first, count)], sem)
    copy.start()
    copy.wait()


def channel_windows(turned, tail, extent, width, tail_rows):
    slab, rows = turned.shape
    windows = pl.pallas_call(
        functools.partial(windows_kernel, width, tail_rows),
        out_shape=jax.ShapeDtypeStruct((extent, slab, width), turned.dtype),
        cost_estimate=pl.CostEstimate(
            flops=0, transcendentals=0, bytes_accessed=2 * (slab * rows + extent * slab * width)
        ),
    )(turned)
    count = -(-tail_rows // ((rows + tail_rows - width) // (extent - 1)))
    return pl.pallas_call(
        functools.partial(tail_windows_kernel, width, count),
        out_shape=jax.ShapeDtypeStruct((extent, slab, width), turned.dtype),
        in_specs=[
            pl.BlockSpec(memory_space=pltpu.VMEM),
            pl.BlockSpec(memory_space=pltpu.VMEM),
            pl.BlockSpec(memory_space=pl.ANY),
        ],
        out_specs=pl.BlockSpec(memory_space=pl.ANY),
        scratch_shapes=[
            pltpu.VMEM((count, slab, width), turned.dtype),
            pltpu.SemaphoreType.DMA(()),
        ],
        input_output_aliases={2: 0},
        cost_estimate=pl.CostEstimate(
            flops=0, transcendentals=0, bytes_accessed=2 * (slab * rows + 2 * count * slab * width)
        ),
    )(turned, tail, windows)


def cross_kernel(segments, rows_per_step, own_ref, ext_ref, out_ref):
    step = pl.program_id(0)
    base = pl.multiple_of(step * rows_per_step, rows_per_step)
    for i in range(rows_per_step):
        acc_re = None
        acc_im = None
        for s in range(segments):
            a = own_ref[pl.ds(base, rows_per_step), pl.ds(s * NFFT, NFFT)]
            a = a.astype(jnp.float32)[i : i + 1]
            window = ext_ref[pl.ds(base, LAGS + rows_per_step), pl.ds(s * NFFT, NFFT)]
            b = window.astype(jnp.float32)[i : i + LAGS]
            terms = product_terms(a, b)
            if acc_re is None:
                acc_re, acc_im = terms
            else:
                acc_re = [x + y for x, y in zip(acc_re, terms[0])]
                acc_im = [x + y for x, y in zip(acc_im, terms[1])]
        store_row(out_ref, i, acc_re, acc_im, segments)


def product_terms(a, b):
    ar = a[:, :NF]
    ai = a[:, NF:]
    br = b[:, :NF]
    bi = b[:, NF:]
    return [ar * br, ai * bi], [ai * br, ar * bi]


def store_row(out_ref, i, acc_re, acc_im, segments):
    re = acc_re[0] + acc_re[1]
    im = acc_im[0] - acc_im[1]
    if segments > 1:
        re = re / segments
        im = im / segments
    out_ref[i, :, :NF] = re.astype(out_ref.dtype)
    out_ref[i, :, NF:] = im.astype(out_ref.dtype)


def cross_kernel_shifted(segments, rows_per_step, own_ref, ext_ref, out_ref, own_f32, shifted):
    step = pl.program_id(0)
    span = shifted.shape[1]

    @pl.when(step == 0)
    def _():
        own_f32[...] = own_ref[...].astype(jnp.float32)
        whole = ext_ref[...].astype(jnp.float32)
        for i in range(rows_per_step):
            shifted[i] = whole[i : i + span]

    base = pl.multiple_of(step * rows_per_step, rows_per_step)
    for i in range(rows_per_step):
        acc_re = None
        acc_im = None
        for s in range(segments):
            a = own_f32[pl.ds(base + i, 1), pl.ds(s * NFFT, NFFT)]
            b = shifted[i, pl.ds(base, LAGS), pl.ds(s * NFFT, NFFT)]
            terms = product_terms(a, b)
            if acc_re is None:
                acc_re, acc_im = terms
            else:
                acc_re = [x + y for x, y in zip(acc_re, terms[0])]
                acc_im = [x + y for x, y in zip(acc_im, terms[1])]
        store_row(out_ref, i, acc_re, acc_im, segments)


def cross_kernel_pieces(segments, rows, chunk, *refs):
    pieces = refs[:-5]
    out_hbm, own_f32, shifted, buffers, sems = refs[-5:]
    span = shifted.shape[1]
    extended = jnp.concatenate(
        [
            jnp.concatenate(
                [piece[s * NFFT : (s + 1) * NFFT, :].astype(jnp.float32).T for s in range(segments)],
                axis=1,
            )
            for piece in pieces
        ],
        axis=0,
    )
    own_f32[...] = extended[:rows]
    for i in range(chunk):
        shifted[i] = extended[i : i + span]
    slots, parts = buffers.shape[0], sems.shape[1]
    part = chunk // parts
    copies = []
    for m in range(rows // chunk):
        slot = m % slots
        if m >= slots:
            for copy in copies[m - slots]:
                copy.wait()
        base = m * chunk
        for i in range(chunk):
            acc_re = None
            acc_im = None
            for s in range(segments):
                a = own_f32[base + i : base + i + 1, s * NFFT : (s + 1) * NFFT]
                b = shifted[i, base : base + LAGS, s * NFFT : (s + 1) * NFFT]
                terms = product_terms(a, b)
                if acc_re is None:
                    acc_re, acc_im = terms
                else:
                    acc_re = [x + y for x, y in zip(acc_re, terms[0])]
                    acc_im = [x + y for x, y in zip(acc_im, terms[1])]
            store_row(buffers.at[slot], i, acc_re, acc_im, segments)
        group = []
        for p in range(parts):
            copy = pltpu.make_async_copy(
                buffers.at[slot, pl.ds(p * part, part)],
                out_hbm.at[pl.ds(base + p * part, part)],
                sems.at[slot, p],
            )
            copy.start()
            group.append(copy)
        copies.append(group)
    for group in copies[-slots:]:
        for copy in group:
            copy.wait()


def cross_spectra_pieces(pieces):
    width = pieces[0].shape[0]
    rows = sum(piece.shape[1] for piece in pieces) - LAGS
    segments = width // NFFT
    chunk = 8
    span = rows + LAGS - chunk
    return pl.pallas_call(
        functools.partial(cross_kernel_pieces, segments, rows, chunk),
        out_shape=jax.ShapeDtypeStruct((rows, LAGS, NFFT), jnp.bfloat16),
        in_specs=[pl.BlockSpec(memory_space=pltpu.VMEM)] * len(pieces),
        out_specs=pl.BlockSpec(memory_space=pl.ANY),
        scratch_shapes=[
            pltpu.VMEM((rows, width), jnp.float32),
            pltpu.VMEM((chunk, span, width), jnp.float32),
            pltpu.VMEM((4, chunk, LAGS, NFFT), jnp.bfloat16),
            pltpu.SemaphoreType.DMA((4, 4)),
        ],
        cost_estimate=pl.CostEstimate(
            flops=6 * rows * LAGS * NF * segments,
            transcendentals=0,
            bytes_accessed=rows * LAGS * NFFT * 2 + 2 * (rows + LAGS) * width,
        ),
    )(*pieces)


def split_three(values):
    high = values.astype(jnp.bfloat16)
    rest = values - high.astype(jnp.float32)
    middle = rest.astype(jnp.bfloat16)
    low = (rest - middle.astype(jnp.float32)).astype(jnp.bfloat16)
    return [high, middle, low]


def exact_dot(parts, operand):
    total = None
    for part in parts:
        term = jnp.dot(part, operand, preferred_element_type=jnp.float32)
        total = term if total is None else total + term
    return total


def fused_kernel(rows, chunk, taps_ref, samples_ref, table_ref, out_hbm, own_f32, shifted,
                 buffers, sems):
    tap_count = taps_ref.shape[0]
    outputs = NFFT // 2
    length, channels = samples_ref.shape
    blocks = length // (2 * outputs)
    lanes = 3 * NF
    lane = lax.broadcasted_iota(jnp.int32, (1, lanes), 1)
    row = jnp.zeros((1, lanes), jnp.float32)
    for k in range(tap_count):
        row = jnp.where(lane == tap_count - 1 - k, taps_ref[k], row)
    matrices = []
    for part in split_three(row):
        rolled = pltpu.roll(
            jnp.broadcast_to(part.astype(jnp.float32), (outputs, lanes)), 0, 1, stride=2, stride_axis=0
        )
        matrices.append(rolled[:, : 2 * outputs + tap_count].astype(jnp.bfloat16))
    x = samples_ref[...]
    joined = jnp.concatenate(
        [
            jnp.zeros((tap_count, channels), x.dtype),
            x,
            jnp.zeros((2 * outputs - tap_count, channels), x.dtype),
        ],
        axis=0,
    )
    filtered = jnp.concatenate(
        [
            exact_dot(matrices, joined[b * 2 * outputs : b * 2 * outputs + 2 * outputs + tap_count])
            for b in range(blocks)
        ],
        axis=0,
    )
    filtered = filtered.astype(jnp.bfloat16)
    spectrum = exact_dot([table_ref[p] for p in range(table_ref.shape[0])], filtered)
    real_part = spectrum[:NF]
    imag_part = spectrum[NF:]
    powers = real_part * real_part + imag_part * imag_part
    mean_power = jnp.mean(powers, axis=0, keepdims=True)
    whitening = 1.0 / jnp.sqrt(powers + mean_power + 1e-06)
    whitened = jnp.concatenate([real_part * whitening, imag_part * whitening], axis=0)
    extended = whitened.astype(jnp.bfloat16).astype(jnp.float32).T
    span = shifted.shape[1]
    own_f32[...] = extended[:rows]
    for i in range(chunk):
        shifted[i] = extended[i : i + span]
    slots, parts = buffers.shape[0], sems.shape[1]
    part = chunk // parts
    copies = []
    for m in range(rows // chunk):
        slot = m % slots
        if m >= slots:
            for copy in copies[m - slots]:
                copy.wait()
        base = m * chunk
        for i in range(chunk):
            a = own_f32[base + i : base + i + 1, :]
            b = shifted[i, base : base + LAGS, :]
            acc_re, acc_im = product_terms(a, b)
            store_row(buffers.at[slot], i, acc_re, acc_im, 1)
        group = []
        for p in range(parts):
            copy = pltpu.make_async_copy(
                buffers.at[slot, pl.ds(p * part, part)],
                out_hbm.at[pl.ds(base + p * part, part)],
                sems.at[slot, p],
            )
            copy.start()
            group.append(copy)
        copies.append(group)
    for group in copies[-slots:]:
        for copy in group:
            copy.wait()


def fused_spectra(samples, filter_taps, table_t, rows):
    length, channels = samples.shape
    chunk = 8
    span = channels - chunk
    return pl.pallas_call(
        functools.partial(fused_kernel, rows, chunk),
        out_shape=jax.ShapeDtypeStruct((rows, LAGS, NFFT), jnp.bfloat16),
        in_specs=[pl.BlockSpec(memory_space=pltpu.SMEM)] + [pl.BlockSpec(memory_space=pltpu.VMEM)] * 2,
        out_specs=pl.BlockSpec(memory_space=pl.ANY),
        scratch_shapes=[
            pltpu.VMEM((rows, NFFT), jnp.float32),
            pltpu.VMEM((chunk, span, NFFT), jnp.float32),
            pltpu.VMEM((4, chunk, LAGS, NFFT), jnp.bfloat16),
            pltpu.SemaphoreType.DMA((4, 4)),
        ],
        cost_estimate=pl.CostEstimate(
            flops=6 * rows * LAGS * NF + 12 * channels * (NF * 320 * length // 256 + NFFT * NFFT),
            transcendentals=2 * NF * channels,
            bytes_accessed=rows * LAGS * NFFT * 2 + 2 * samples.size + 2 * table_t.size,
        ),
    )(filter_taps, samples, table_t)


def cross_spectra(own, extended):
    rows, segments, columns = own.shape
    reach_rows = extended.shape[0]
    own_flat = own.reshape(rows, segments * columns)
    ext_flat = extended.reshape(reach_rows, segments * columns)
    rows_per_step = 8
    span = reach_rows - rows_per_step
    scratch_bytes = rows_per_step * span * segments * columns * 4
    cost = pl.CostEstimate(
        flops=6 * rows * LAGS * NF * segments,
        transcendentals=0,
        bytes_accessed=rows * LAGS * columns * 2 + 2 * segments * (rows + reach_rows) * columns,
    )
    common = dict(
        out_shape=jax.ShapeDtypeStruct((rows, LAGS, columns), jnp.bfloat16),
        grid=(rows // rows_per_step,),
        in_specs=[
            pl.BlockSpec((rows, segments * columns), lambda i: (0, 0)),
            pl.BlockSpec((reach_rows, segments * columns), lambda i: (0, 0)),
        ],
        out_specs=pl.BlockSpec((rows_per_step, LAGS, columns), lambda i: (i, 0, 0)),
        cost_estimate=cost,
    )
    if scratch_bytes <= 8 * 1024 * 1024:
        return pl.pallas_call(
            functools.partial(cross_kernel_shifted, segments, rows_per_step),
            scratch_shapes=[
                pltpu.VMEM((rows, segments * columns), jnp.float32),
                pltpu.VMEM((rows_per_step, span, segments * columns), jnp.float32),
            ],
            compiler_params=pltpu.CompilerParams(dimension_semantics=("arbitrary",)),
            **common,
        )(own_flat, ext_flat)
    return pl.pallas_call(
        functools.partial(cross_kernel, segments, rows_per_step), **common
    )(own_flat, ext_flat)


def body(strain, filter_taps):
    extent = lax.axis_size("ta")
    columns_n = lax.axis_size("col")
    section_rows, slab = strain.shape
    block_rows = section_rows // extent
    reach = LAGS // block_rows
    turned = strain.T
    route = [(c + 1, c) for c in range(columns_n - 1)]
    following = lax.ppermute(turned, "col", route)
    tail = following[:, : reach * block_rows]
    width = (reach + 1) * block_rows
    windows = channel_windows(turned, tail, extent, width, reach * block_rows)
    gathered = lax.all_to_all(windows, "ta", split_axis=0, concat_axis=0, tiled=True)
    samples = gathered.reshape(extent * slab, width)
    if extent * slab == 2 * NFFT:
        table_parts = jnp.stack(split_three(fourier_table_t()))
        return fused_spectra(samples, filter_taps, table_parts, block_rows)[None]
    filtered = decimate_t(samples.astype(jnp.float32), filter_taps)
    whitened_t = whiten_t(filtered)
    segments, columns, _ = whitened_t.shape
    if segments * 8 * width * columns * 4 <= 8 * 1024 * 1024:
        flat = whitened_t.reshape(segments * columns, width)
        return cross_spectra_pieces([flat])[None]
    extended = whitened_t.transpose(2, 0, 1)
    return cross_spectra(extended[:block_rows], extended)[None]


def solution(mesh):
    return jax.shard_map(
        body,
        mesh=mesh,
        in_specs=(P("col", "ta"), P()),
        out_specs=P("col", "ta", None, None),
        check_vma=False,
    )
```

```python
import functools

import jax
import jax.numpy as jnp
from jax import lax
from jax.experimental import pallas as pl
from jax.experimental.pallas import tpu as pltpu
from jax.sharding import PartitionSpec as P

NFFT = 256
NF = 128
LAGS = 128


def tap_rows(filter_taps, outputs):
    tap_count = filter_taps.shape[0]
    window = 2 * outputs + tap_count
    flipped = filter_taps[::-1]
    period = jnp.concatenate([flipped, jnp.zeros((window + 2 - tap_count,), jnp.float32)])
    repeated = jnp.tile(period, outputs)[: outputs * window]
    return repeated.reshape(outputs, window)


def decimate_t(samples, filter_taps):
    length, channels = samples.shape
    tap_count = filter_taps.shape[0]
    outputs = min(length, NFFT) // 2
    blocks = length // (2 * outputs)
    joined = jnp.concatenate(
        [
            jnp.zeros((tap_count, channels), jnp.float32),
            samples,
            jnp.zeros((2 * outputs - tap_count, channels), jnp.float32),
        ],
        axis=0,
    )
    joined = joined.reshape(blocks + 1, 2 * outputs, channels)
    windows = jnp.concatenate([joined[:-1], joined[1:, :tap_count]], axis=1)
    matrix = tap_rows(filter_taps, outputs)
    result = jnp.einsum("tw,bwc->btc", matrix, windows, precision=lax.Precision.HIGHEST)
    return result.reshape(blocks * outputs, channels).astype(jnp.bfloat16)


def fourier_table():
    moment = lax.broadcasted_iota(jnp.int32, (NFFT, NF), 0)
    frequency = lax.broadcasted_iota(jnp.int32, (NFFT, NF), 1) + 1
    phase_index = moment * frequency % NFFT
    angles = phase_index.astype(jnp.float32) * (2.0 * jnp.pi / NFFT)
    window_taper = 0.5 - 0.5 * jnp.cos(moment.astype(jnp.float32) * (2.0 * jnp.pi / NFFT))
    return jnp.concatenate(
        [window_taper * jnp.cos(angles), -window_taper * jnp.sin(angles)], axis=1
    )


def fourier_table_t():
    moment = lax.broadcasted_iota(jnp.int32, (NFFT, NFFT), 1)
    frequency = lax.broadcasted_iota(jnp.int32, (NFFT, NFFT), 0) % NF + 1
    phase_index = moment * frequency % NFFT
    angles = phase_index.astype(jnp.float32) * (2.0 * jnp.pi / NFFT)
    window_taper = 0.5 - 0.5 * jnp.cos(moment.astype(jnp.float32) * (2.0 * jnp.pi / NFFT))
    real_rows = lax.broadcasted_iota(jnp.int32, (NFFT, NFFT), 0) < NF
    return jnp.where(real_rows, window_taper * jnp.cos(angles), -window_taper * jnp.sin(angles))


def whiten_t(filtered):
    length, channels = filtered.shape
    pieces = filtered.reshape(length // NF, NF, channels)
    segment_rows = jnp.concatenate([pieces[:-1], pieces[1:]], axis=1)
    spectrum = jnp.einsum(
        "nf,snc->sfc",
        fourier_table(),
        segment_rows.astype(jnp.float32),
        precision=lax.Precision.HIGHEST,
    )
    real_part = spectrum[:, :NF]
    imag_part = spectrum[:, NF:]
    powers = real_part * real_part + imag_part * imag_part
    mean_power = jnp.mean(powers, axis=1, keepdims=True)
    whitening = 1.0 / jnp.sqrt(powers + mean_power + 1e-06)
    return jnp.concatenate([real_part * whitening, imag_part * whitening], axis=1).astype(
        jnp.bfloat16
    )


def windows_kernel(width, tail_rows, x_ref, out_ref):
    x = x_ref[...].astype(jnp.float32)
    padded = jnp.concatenate([x, jnp.zeros((x.shape[0], tail_rows), jnp.float32)], axis=1)
    step = (padded.shape[1] - width) // (out_ref.shape[0] - 1)
    for j in range(out_ref.shape[0]):
        out_ref[j] = padded[:, j * step : j * step + width].astype(out_ref.dtype)


def tail_windows_kernel(width, count, x_ref, tail_ref, windows_hbm, out_hbm, fresh, sem):
    del windows_hbm
    x = x_ref[...].astype(jnp.float32)
    tail = tail_ref[...].astype(jnp.float32)
    extent = out_hbm.shape[0]
    rows = x.shape[1]
    step = (rows + tail.shape[1] - width) // (extent - 1)
    first = extent - count
    padded = jnp.concatenate([x[:, first * step :], tail], axis=1)
    for j in range(count):
        fresh[j] = padded[:, j * step : j * step + width].astype(fresh.dtype)
    copy = pltpu.make_async_copy(fresh, out_hbm.at[pl.ds(first, count)], sem)
    copy.start()
    copy.wait()


def channel_windows(turned, tail, extent, width, tail_rows):
    slab, rows = turned.shape
    windows = pl.pallas_call(
        functools.partial(windows_kernel, width, tail_rows),
        out_shape=jax.ShapeDtypeStruct((extent, slab, width), turned.dtype),
        cost_estimate=pl.CostEstimate(
            flops=0, transcendentals=0, bytes_accessed=2 * (slab * rows + extent * slab * width)
        ),
    )(turned)
    count = -(-tail_rows // ((rows + tail_rows - width) // (extent - 1)))
    return pl.pallas_call(
        functools.partial(tail_windows_kernel, width, count),
        out_shape=jax.ShapeDtypeStruct((extent, slab, width), turned.dtype),
        in_specs=[
            pl.BlockSpec(memory_space=pltpu.VMEM),
            pl.BlockSpec(memory_space=pltpu.VMEM),
            pl.BlockSpec(memory_space=pl.ANY),
        ],
        out_specs=pl.BlockSpec(memory_space=pl.ANY),
        scratch_shapes=[
            pltpu.VMEM((count, slab, width), turned.dtype),
            pltpu.SemaphoreType.DMA(()),
        ],
        input_output_aliases={2: 0},
        cost_estimate=pl.CostEstimate(
            flops=0, transcendentals=0, bytes_accessed=2 * (slab * rows + 2 * count * slab * width)
        ),
    )(turned, tail, windows)


def cross_kernel(segments, rows_per_step, own_ref, ext_ref, out_ref):
    step = pl.program_id(0)
    base = pl.multiple_of(step * rows_per_step, rows_per_step)
    for i in range(rows_per_step):
        acc_re = None
        acc_im = None
        for s in range(segments):
            a = own_ref[pl.ds(base, rows_per_step), pl.ds(s * NFFT, NFFT)]
            a = a.astype(jnp.float32)[i : i + 1]
            window = ext_ref[pl.ds(base, LAGS + rows_per_step), pl.ds(s * NFFT, NFFT)]
            b = window.astype(jnp.float32)[i : i + LAGS]
            terms = product_terms(a, b)
            if acc_re is None:
                acc_re, acc_im = terms
            else:
                acc_re = [x + y for x, y in zip(acc_re, terms[0])]
                acc_im = [x + y for x, y in zip(acc_im, terms[1])]
        store_row(out_ref, i, acc_re, acc_im, segments)


def product_terms(a, b):
    ar = a[:, :NF]
    ai = a[:, NF:]
    br = b[:, :NF]
    bi = b[:, NF:]
    return [ar * br, ai * bi], [ai * br, ar * bi]


def store_row(out_ref, i, acc_re, acc_im, segments):
    re = acc_re[0] + acc_re[1]
    im = acc_im[0] - acc_im[1]
    if segments > 1:
        re = re / segments
        im = im / segments
    out_ref[i, :, :NF] = re.astype(out_ref.dtype)
    out_ref[i, :, NF:] = im.astype(out_ref.dtype)


def cross_kernel_shifted(segments, rows_per_step, own_ref, ext_ref, out_ref, own_f32, shifted):
    step = pl.program_id(0)
    span = shifted.shape[1]

    @pl.when(step == 0)
    def _():
        own_f32[...] = own_ref[...].astype(jnp.float32)
        whole = ext_ref[...].astype(jnp.float32)
        for i in range(rows_per_step):
            shifted[i] = whole[i : i + span]

    base = pl.multiple_of(step * rows_per_step, rows_per_step)
    for i in range(rows_per_step):
        acc_re = None
        acc_im = None
        for s in range(segments):
            a = own_f32[pl.ds(base + i, 1), pl.ds(s * NFFT, NFFT)]
            b = shifted[i, pl.ds(base, LAGS), pl.ds(s * NFFT, NFFT)]
            terms = product_terms(a, b)
            if acc_re is None:
                acc_re, acc_im = terms
            else:
                acc_re = [x + y for x, y in zip(acc_re, terms[0])]
                acc_im = [x + y for x, y in zip(acc_im, terms[1])]
        store_row(out_ref, i, acc_re, acc_im, segments)


def cross_kernel_pieces(segments, rows, chunk, *refs):
    pieces = refs[:-5]
    out_hbm, own_f32, shifted, buffers, sems = refs[-5:]
    span = shifted.shape[1]
    extended = jnp.concatenate(
        [
            jnp.concatenate(
                [piece[s * NFFT : (s + 1) * NFFT, :].astype(jnp.float32).T for s in range(segments)],
                axis=1,
            )
            for piece in pieces
        ],
        axis=0,
    )
    own_f32[...] = extended[:rows]
    for i in range(chunk):
        shifted[i] = extended[i : i + span]
    slots, parts = buffers.shape[0], sems.shape[1]
    part = chunk // parts
    copies = []
    for m in range(rows // chunk):
        slot = m % slots
        if m >= slots:
            for copy in copies[m - slots]:
                copy.wait()
        base = m * chunk
        for i in range(chunk):
            acc_re = None
            acc_im = None
            for s in range(segments):
                a = own_f32[base + i : base + i + 1, s * NFFT : (s + 1) * NFFT]
                b = shifted[i, base : base + LAGS, s * NFFT : (s + 1) * NFFT]
                terms = product_terms(a, b)
                if acc_re is None:
                    acc_re, acc_im = terms
                else:
                    acc_re = [x + y for x, y in zip(acc_re, terms[0])]
                    acc_im = [x + y for x, y in zip(acc_im, terms[1])]
            store_row(buffers.at[slot], i, acc_re, acc_im, segments)
        group = []
        for p in range(parts):
            copy = pltpu.make_async_copy(
                buffers.at[slot, pl.ds(p * part, part)],
                out_hbm.at[pl.ds(base + p * part, part)],
                sems.at[slot, p],
            )
            copy.start()
            group.append(copy)
        copies.append(group)
    for group in copies[-slots:]:
        for copy in group:
            copy.wait()


def cross_spectra_pieces(pieces):
    width = pieces[0].shape[0]
    rows = sum(piece.shape[1] for piece in pieces) - LAGS
    segments = width // NFFT
    chunk = 8
    span = rows + LAGS - chunk
    return pl.pallas_call(
        functools.partial(cross_kernel_pieces, segments, rows, chunk),
        out_shape=jax.ShapeDtypeStruct((rows, LAGS, NFFT), jnp.bfloat16),
        in_specs=[pl.BlockSpec(memory_space=pltpu.VMEM)] * len(pieces),
        out_specs=pl.BlockSpec(memory_space=pl.ANY),
        scratch_shapes=[
            pltpu.VMEM((rows, width), jnp.float32),
            pltpu.VMEM((chunk, span, width), jnp.float32),
            pltpu.VMEM((4, chunk, LAGS, NFFT), jnp.bfloat16),
            pltpu.SemaphoreType.DMA((4, 4)),
        ],
        cost_estimate=pl.CostEstimate(
            flops=6 * rows * LAGS * NF * segments,
            transcendentals=0,
            bytes_accessed=rows * LAGS * NFFT * 2 + 2 * (rows + LAGS) * width,
        ),
    )(*pieces)


def split_three(values):
    high = values.astype(jnp.bfloat16)
    rest = values - high.astype(jnp.float32)
    middle = rest.astype(jnp.bfloat16)
    low = (rest - middle.astype(jnp.float32)).astype(jnp.bfloat16)
    return [high, middle, low]


def split_three_kept(values):
    high = lax.reduce_precision(values, exponent_bits=8, mantissa_bits=7)
    rest = values - high
    middle = lax.reduce_precision(rest, exponent_bits=8, mantissa_bits=7)
    low = rest - middle
    return [part.astype(jnp.bfloat16) for part in (high, middle, low)]


def exact_dot(parts, operand):
    total = None
    for part in parts:
        term = jnp.dot(part, operand, preferred_element_type=jnp.float32)
        total = term if total is None else total + term
    return total


def fused_kernel(rows, chunk, taps_ref, samples_ref, table_ref, out_hbm, own_f32, shifted,
                 buffers, sems):
    tap_count = taps_ref.shape[0]
    outputs = NFFT // 2
    length, channels = samples_ref.shape
    blocks = length // (2 * outputs)
    lanes = 3 * NF
    lane = lax.broadcasted_iota(jnp.int32, (1, lanes), 1)
    row = jnp.zeros((1, lanes), jnp.float32)
    for k in range(tap_count):
        row = jnp.where(lane == tap_count - 1 - k, taps_ref[k], row)
    matrices = []
    for part in split_three(row):
        rolled = pltpu.roll(
            jnp.broadcast_to(part.astype(jnp.float32), (outputs, lanes)), 0, 1, stride=2, stride_axis=0
        )
        matrices.append(rolled[:, : 2 * outputs + tap_count].astype(jnp.bfloat16))
    x = samples_ref[...]
    joined = jnp.concatenate(
        [
            jnp.zeros((tap_count, channels), x.dtype),
            x,
            jnp.zeros((2 * outputs - tap_count, channels), x.dtype),
        ],
        axis=0,
    )
    filtered = jnp.concatenate(
        [
            exact_dot(matrices, joined[b * 2 * outputs : b * 2 * outputs + 2 * outputs + tap_count])
            for b in range(blocks)
        ],
        axis=0,
    )
    filtered = filtered.astype(jnp.bfloat16)
    spectrum = exact_dot([table_ref[p] for p in range(table_ref.shape[0])], filtered)
    real_part = spectrum[:NF]
    imag_part = spectrum[NF:]
    powers = real_part * real_part + imag_part * imag_part
    mean_power = jnp.mean(powers, axis=0, keepdims=True)
    whitening = 1.0 / jnp.sqrt(powers + mean_power + 1e-06)
    whitened = jnp.concatenate([real_part * whitening, imag_part * whitening], axis=0)
    extended = whitened.astype(jnp.bfloat16).astype(jnp.float32).T
    span = shifted.shape[1]
    own_f32[...] = extended[:rows]
    for i in range(chunk):
        shifted[i] = extended[i : i + span]
    slots, parts = buffers.shape[0], sems.shape[1]
    part = chunk // parts
    copies = []
    for m in range(rows // chunk):
        slot = m % slots
        if m >= slots:
            for copy in copies[m - slots]:
                copy.wait()
        base = m * chunk
        for i in range(chunk):
            a = own_f32[base + i : base + i + 1, :]
            b = shifted[i, base : base + LAGS, :]
            acc_re, acc_im = product_terms(a, b)
            store_row(buffers.at[slot], i, acc_re, acc_im, 1)
        group = []
        for p in range(parts):
            copy = pltpu.make_async_copy(
                buffers.at[slot, pl.ds(p * part, part)],
                out_hbm.at[pl.ds(base + p * part, part)],
                sems.at[slot, p],
            )
            copy.start()
            group.append(copy)
        copies.append(group)
    for group in copies[-slots:]:
        for copy in group:
            copy.wait()


def fused_spectra(samples, filter_taps, table_t, rows):
    length, channels = samples.shape
    chunk = 8
    span = channels - chunk
    return pl.pallas_call(
        functools.partial(fused_kernel, rows, chunk),
        out_shape=jax.ShapeDtypeStruct((rows, LAGS, NFFT), jnp.bfloat16),
        in_specs=[pl.BlockSpec(memory_space=pltpu.SMEM)] + [pl.BlockSpec(memory_space=pltpu.VMEM)] * 2,
        out_specs=pl.BlockSpec(memory_space=pl.ANY),
        scratch_shapes=[
            pltpu.VMEM((rows, NFFT), jnp.float32),
            pltpu.VMEM((chunk, span, NFFT), jnp.float32),
            pltpu.VMEM((4, chunk, LAGS, NFFT), jnp.bfloat16),
            pltpu.SemaphoreType.DMA((4, 4)),
        ],
        cost_estimate=pl.CostEstimate(
            flops=6 * rows * LAGS * NF + 12 * channels * (NF * 320 * length // 256 + NFFT * NFFT),
            transcendentals=2 * NF * channels,
            bytes_accessed=rows * LAGS * NFFT * 2 + 2 * samples.size + 2 * table_t.size,
        ),
    )(filter_taps, samples, table_t)


def cross_spectra(own, extended):
    rows, segments, columns = own.shape
    reach_rows = extended.shape[0]
    own_flat = own.reshape(rows, segments * columns)
    ext_flat = extended.reshape(reach_rows, segments * columns)
    rows_per_step = 8
    span = reach_rows - rows_per_step
    scratch_bytes = rows_per_step * span * segments * columns * 4
    cost = pl.CostEstimate(
        flops=6 * rows * LAGS * NF * segments,
        transcendentals=0,
        bytes_accessed=rows * LAGS * columns * 2 + 2 * segments * (rows + reach_rows) * columns,
    )
    common = dict(
        out_shape=jax.ShapeDtypeStruct((rows, LAGS, columns), jnp.bfloat16),
        grid=(rows // rows_per_step,),
        in_specs=[
            pl.BlockSpec((rows, segments * columns), lambda i: (0, 0)),
            pl.BlockSpec((reach_rows, segments * columns), lambda i: (0, 0)),
        ],
        out_specs=pl.BlockSpec((rows_per_step, LAGS, columns), lambda i: (i, 0, 0)),
        cost_estimate=cost,
    )
    if scratch_bytes <= 8 * 1024 * 1024:
        return pl.pallas_call(
            functools.partial(cross_kernel_shifted, segments, rows_per_step),
            scratch_shapes=[
                pltpu.VMEM((rows, segments * columns), jnp.float32),
                pltpu.VMEM((rows_per_step, span, segments * columns), jnp.float32),
            ],
            compiler_params=pltpu.CompilerParams(dimension_semantics=("arbitrary",)),
            **common,
        )(own_flat, ext_flat)
    return pl.pallas_call(
        functools.partial(cross_kernel, segments, rows_per_step), **common
    )(own_flat, ext_flat)


def body(strain, filter_taps):
    extent = lax.axis_size("ta")
    columns_n = lax.axis_size("col")
    section_rows, slab = strain.shape
    block_rows = section_rows // extent
    reach = LAGS // block_rows
    turned = strain.T
    route = [(c + 1, c) for c in range(columns_n - 1)]
    following = lax.ppermute(turned, "col", route)
    tail = following[:, : reach * block_rows]
    width = (reach + 1) * block_rows
    windows = channel_windows(turned, tail, extent, width, reach * block_rows)
    gathered = lax.all_to_all(windows, "ta", split_axis=0, concat_axis=0, tiled=True)
    samples = gathered.reshape(extent * slab, width)
    if extent * slab == 2 * NFFT:
        table_parts = jnp.stack(split_three_kept(fourier_table_t()))
        return fused_spectra(samples, filter_taps, table_parts, block_rows)[None]
    filtered = decimate_t(samples.astype(jnp.float32), filter_taps)
    whitened_t = whiten_t(filtered)
    segments, columns, _ = whitened_t.shape
    if segments * 8 * width * columns * 4 <= 8 * 1024 * 1024:
        flat = whitened_t.reshape(segments * columns, width)
        return cross_spectra_pieces([flat])[None]
    extended = whitened_t.transpose(2, 0, 1)
    return cross_spectra(extended[:block_rows], extended)[None]


def solution(mesh):
    return jax.shard_map(
        body,
        mesh=mesh,
        in_specs=(P("col", "ta"), P()),
        out_specs=P("col", "ta", None, None),
        check_vma=False,
    )
```

```python
import functools

import jax
import jax.numpy as jnp
from jax import lax
from jax.experimental import pallas as pl
from jax.experimental.pallas import tpu as pltpu
from jax.sharding import PartitionSpec as P

NFFT = 256
NF = 128
LAGS = 128


def tap_rows(filter_taps, outputs):
    tap_count = filter_taps.shape[0]
    window = 2 * outputs + tap_count
    flipped = filter_taps[::-1]
    period = jnp.concatenate([flipped, jnp.zeros((window + 2 - tap_count,), jnp.float32)])
    repeated = jnp.tile(period, outputs)[: outputs * window]
    return repeated.reshape(outputs, window)


def decimate_t(samples, filter_taps):
    length, channels = samples.shape
    tap_count = filter_taps.shape[0]
    outputs = min(length, NFFT) // 2
    blocks = length // (2 * outputs)
    joined = jnp.concatenate(
        [
            jnp.zeros((tap_count, channels), jnp.float32),
            samples,
            jnp.zeros((2 * outputs - tap_count, channels), jnp.float32),
        ],
        axis=0,
    )
    joined = joined.reshape(blocks + 1, 2 * outputs, channels)
    windows = jnp.concatenate([joined[:-1], joined[1:, :tap_count]], axis=1)
    matrix = tap_rows(filter_taps, outputs)
    result = jnp.einsum("tw,bwc->btc", matrix, windows, precision=lax.Precision.HIGHEST)
    return result.reshape(blocks * outputs, channels).astype(jnp.bfloat16)


def fourier_table():
    moment = lax.broadcasted_iota(jnp.int32, (NFFT, NF), 0)
    frequency = lax.broadcasted_iota(jnp.int32, (NFFT, NF), 1) + 1
    phase_index = moment * frequency % NFFT
    angles = phase_index.astype(jnp.float32) * (2.0 * jnp.pi / NFFT)
    window_taper = 0.5 - 0.5 * jnp.cos(moment.astype(jnp.float32) * (2.0 * jnp.pi / NFFT))
    return jnp.concatenate(
        [window_taper * jnp.cos(angles), -window_taper * jnp.sin(angles)], axis=1
    )


def fourier_table_t():
    moment = lax.broadcasted_iota(jnp.int32, (NFFT, NFFT), 1)
    frequency = lax.broadcasted_iota(jnp.int32, (NFFT, NFFT), 0) % NF + 1
    phase_index = moment * frequency % NFFT
    angles = phase_index.astype(jnp.float32) * (2.0 * jnp.pi / NFFT)
    window_taper = 0.5 - 0.5 * jnp.cos(moment.astype(jnp.float32) * (2.0 * jnp.pi / NFFT))
    real_rows = lax.broadcasted_iota(jnp.int32, (NFFT, NFFT), 0) < NF
    return jnp.where(real_rows, window_taper * jnp.cos(angles), -window_taper * jnp.sin(angles))


def whiten_t(filtered):
    length, channels = filtered.shape
    pieces = filtered.reshape(length // NF, NF, channels)
    segment_rows = jnp.concatenate([pieces[:-1], pieces[1:]], axis=1)
    spectrum = jnp.einsum(
        "nf,snc->sfc",
        fourier_table(),
        segment_rows.astype(jnp.float32),
        precision=lax.Precision.HIGHEST,
    )
    real_part = spectrum[:, :NF]
    imag_part = spectrum[:, NF:]
    powers = real_part * real_part + imag_part * imag_part
    mean_power = jnp.mean(powers, axis=1, keepdims=True)
    whitening = 1.0 / jnp.sqrt(powers + mean_power + 1e-06)
    return jnp.concatenate([real_part * whitening, imag_part * whitening], axis=1).astype(
        jnp.bfloat16
    )


def windows_kernel(width, tail_rows, x_ref, out_ref):
    x = x_ref[...].astype(jnp.float32)
    padded = jnp.concatenate([x, jnp.zeros((x.shape[0], tail_rows), jnp.float32)], axis=1)
    step = (padded.shape[1] - width) // (out_ref.shape[0] - 1)
    for j in range(out_ref.shape[0]):
        out_ref[j] = padded[:, j * step : j * step + width].astype(out_ref.dtype)


def tail_windows_kernel(width, count, x_ref, tail_ref, windows_hbm, out_hbm, fresh, sem):
    del windows_hbm
    x = x_ref[...].astype(jnp.float32)
    tail = tail_ref[...].astype(jnp.float32)
    extent = out_hbm.shape[0]
    rows = x.shape[1]
    step = (rows + tail.shape[1] - width) // (extent - 1)
    first = extent - count
    padded = jnp.concatenate([x[:, first * step :], tail], axis=1)
    for j in range(count):
        fresh[j] = padded[:, j * step : j * step + width].astype(fresh.dtype)
    copy = pltpu.make_async_copy(fresh, out_hbm.at[pl.ds(first, count)], sem)
    copy.start()
    copy.wait()


def channel_windows(turned, tail, extent, width, tail_rows):
    slab, rows = turned.shape
    windows = pl.pallas_call(
        functools.partial(windows_kernel, width, tail_rows),
        out_shape=jax.ShapeDtypeStruct((extent, slab, width), turned.dtype),
        cost_estimate=pl.CostEstimate(
            flops=0, transcendentals=0, bytes_accessed=2 * (slab * rows + extent * slab * width)
        ),
    )(turned)
    count = -(-tail_rows // ((rows + tail_rows - width) // (extent - 1)))
    return pl.pallas_call(
        functools.partial(tail_windows_kernel, width, count),
        out_shape=jax.ShapeDtypeStruct((extent, slab, width), turned.dtype),
        in_specs=[
            pl.BlockSpec(memory_space=pltpu.VMEM),
            pl.BlockSpec(memory_space=pltpu.VMEM),
            pl.BlockSpec(memory_space=pl.ANY),
        ],
        out_specs=pl.BlockSpec(memory_space=pl.ANY),
        scratch_shapes=[
            pltpu.VMEM((count, slab, width), turned.dtype),
            pltpu.SemaphoreType.DMA(()),
        ],
        input_output_aliases={2: 0},
        cost_estimate=pl.CostEstimate(
            flops=0, transcendentals=0, bytes_accessed=2 * (slab * rows + 2 * count * slab * width)
        ),
    )(turned, tail, windows)


def cross_kernel(segments, rows_per_step, own_ref, ext_ref, out_ref):
    step = pl.program_id(0)
    base = pl.multiple_of(step * rows_per_step, rows_per_step)
    for i in range(rows_per_step):
        acc_re = None
        acc_im = None
        for s in range(segments):
            a = own_ref[pl.ds(base, rows_per_step), pl.ds(s * NFFT, NFFT)]
            a = a.astype(jnp.float32)[i : i + 1]
            window = ext_ref[pl.ds(base, LAGS + rows_per_step), pl.ds(s * NFFT, NFFT)]
            b = window.astype(jnp.float32)[i : i + LAGS]
            terms = product_terms(a, b)
            if acc_re is None:
                acc_re, acc_im = terms
            else:
                acc_re = [x + y for x, y in zip(acc_re, terms[0])]
                acc_im = [x + y for x, y in zip(acc_im, terms[1])]
        store_row(out_ref, i, acc_re, acc_im, segments)


def product_terms(a, b):
    ar = a[:, :NF]
    ai = a[:, NF:]
    br = b[:, :NF]
    bi = b[:, NF:]
    return [ar * br, ai * bi], [ai * br, ar * bi]


def store_row(out_ref, i, acc_re, acc_im, segments):
    re = acc_re[0] + acc_re[1]
    im = acc_im[0] - acc_im[1]
    if segments > 1:
        re = re / segments
        im = im / segments
    out_ref[i, :, :NF] = re.astype(out_ref.dtype)
    out_ref[i, :, NF:] = im.astype(out_ref.dtype)


def cross_kernel_shifted(segments, rows_per_step, own_ref, ext_ref, out_ref, own_f32, shifted):
    step = pl.program_id(0)
    span = shifted.shape[1]

    @pl.when(step == 0)
    def _():
        own_f32[...] = own_ref[...].astype(jnp.float32)
        whole = ext_ref[...].astype(jnp.float32)
        for i in range(rows_per_step):
            shifted[i] = whole[i : i + span]

    base = pl.multiple_of(step * rows_per_step, rows_per_step)
    for i in range(rows_per_step):
        acc_re = None
        acc_im = None
        for s in range(segments):
            a = own_f32[pl.ds(base + i, 1), pl.ds(s * NFFT, NFFT)]
            b = shifted[i, pl.ds(base, LAGS), pl.ds(s * NFFT, NFFT)]
            terms = product_terms(a, b)
            if acc_re is None:
                acc_re, acc_im = terms
            else:
                acc_re = [x + y for x, y in zip(acc_re, terms[0])]
                acc_im = [x + y for x, y in zip(acc_im, terms[1])]
        store_row(out_ref, i, acc_re, acc_im, segments)


def cross_kernel_pieces(segments, rows, chunk, *refs):
    pieces = refs[:-5]
    out_hbm, own_f32, shifted, buffers, sems = refs[-5:]
    span = shifted.shape[1]
    extended = jnp.concatenate(
        [
            jnp.concatenate(
                [piece[s * NFFT : (s + 1) * NFFT, :].astype(jnp.float32).T for s in range(segments)],
                axis=1,
            )
            for piece in pieces
        ],
        axis=0,
    )
    own_f32[...] = extended[:rows]
    for i in range(chunk):
        shifted[i] = extended[i : i + span]
    slots, parts = buffers.shape[0], sems.shape[1]
    part = chunk // parts
    copies = []
    for m in range(rows // chunk):
        slot = m % slots
        if m >= slots:
            for copy in copies[m - slots]:
                copy.wait()
        base = m * chunk
        for i in range(chunk):
            acc_re = None
            acc_im = None
            for s in range(segments):
                a = own_f32[base + i : base + i + 1, s * NFFT : (s + 1) * NFFT]
                b = shifted[i, base : base + LAGS, s * NFFT : (s + 1) * NFFT]
                terms = product_terms(a, b)
                if acc_re is None:
                    acc_re, acc_im = terms
                else:
                    acc_re = [x + y for x, y in zip(acc_re, terms[0])]
                    acc_im = [x + y for x, y in zip(acc_im, terms[1])]
            store_row(buffers.at[slot], i, acc_re, acc_im, segments)
        group = []
        for p in range(parts):
            copy = pltpu.make_async_copy(
                buffers.at[slot, pl.ds(p * part, part)],
                out_hbm.at[pl.ds(base + p * part, part)],
                sems.at[slot, p],
            )
            copy.start()
            group.append(copy)
        copies.append(group)
    for group in copies[-slots:]:
        for copy in group:
            copy.wait()


def cross_spectra_pieces(pieces):
    width = pieces[0].shape[0]
    rows = sum(piece.shape[1] for piece in pieces) - LAGS
    segments = width // NFFT
    chunk = 8
    span = rows + LAGS - chunk
    return pl.pallas_call(
        functools.partial(cross_kernel_pieces, segments, rows, chunk),
        out_shape=jax.ShapeDtypeStruct((rows, LAGS, NFFT), jnp.bfloat16),
        in_specs=[pl.BlockSpec(memory_space=pltpu.VMEM)] * len(pieces),
        out_specs=pl.BlockSpec(memory_space=pl.ANY),
        scratch_shapes=[
            pltpu.VMEM((rows, width), jnp.float32),
            pltpu.VMEM((chunk, span, width), jnp.float32),
            pltpu.VMEM((4, chunk, LAGS, NFFT), jnp.bfloat16),
            pltpu.SemaphoreType.DMA((4, 4)),
        ],
        cost_estimate=pl.CostEstimate(
            flops=6 * rows * LAGS * NF * segments,
            transcendentals=0,
            bytes_accessed=rows * LAGS * NFFT * 2 + 2 * (rows + LAGS) * width,
        ),
    )(*pieces)


def split_three(values):
    high = values.astype(jnp.bfloat16)
    rest = values - high.astype(jnp.float32)
    middle = rest.astype(jnp.bfloat16)
    low = (rest - middle.astype(jnp.float32)).astype(jnp.bfloat16)
    return [high, middle, low]


def split_three_kept(values):
    high = lax.reduce_precision(values, exponent_bits=8, mantissa_bits=7)
    rest = values - high
    middle = lax.reduce_precision(rest, exponent_bits=8, mantissa_bits=7)
    low = rest - middle
    return [part.astype(jnp.bfloat16) for part in (high, middle, low)]


def exact_dot(parts, operand):
    total = None
    for part in parts:
        term = jnp.dot(part, operand, preferred_element_type=jnp.float32)
        total = term if total is None else total + term
    return total


def fused_kernel(rows, chunk, taps_ref, samples_ref, table_ref, out_hbm, own_f32, shifted,
                 buffers, sems):
    tap_count = taps_ref.shape[0]
    outputs = NFFT // 2
    length, channels = samples_ref.shape
    blocks = length // (2 * outputs)
    lanes = 3 * NF
    lane = lax.broadcasted_iota(jnp.int32, (1, lanes), 1)
    row = jnp.zeros((1, lanes), jnp.float32)
    for k in range(tap_count):
        row = jnp.where(lane == tap_count - 1 - k, taps_ref[k], row)
    matrices = []
    for part in split_three(row):
        rolled = pltpu.roll(
            jnp.broadcast_to(part.astype(jnp.float32), (outputs, lanes)), 0, 1, stride=2, stride_axis=0
        )
        matrices.append(rolled[:, : 2 * outputs + tap_count].astype(jnp.bfloat16))
    x = samples_ref[...]
    joined = jnp.concatenate(
        [
            jnp.zeros((tap_count, channels), x.dtype),
            x,
            jnp.zeros((2 * outputs - tap_count, channels), x.dtype),
        ],
        axis=0,
    )
    filtered = jnp.concatenate(
        [
            exact_dot(matrices, joined[b * 2 * outputs : b * 2 * outputs + 2 * outputs + tap_count])
            for b in range(blocks)
        ],
        axis=0,
    )
    filtered = filtered.astype(jnp.bfloat16)
    spectrum = exact_dot([table_ref[p] for p in range(table_ref.shape[0])], filtered)
    real_part = spectrum[:NF]
    imag_part = spectrum[NF:]
    powers = real_part * real_part + imag_part * imag_part
    mean_power = jnp.mean(powers, axis=0, keepdims=True)
    whitening = 1.0 / jnp.sqrt(powers + mean_power + 1e-06)
    whitened = jnp.concatenate([real_part * whitening, imag_part * whitening], axis=0)
    extended = whitened.astype(jnp.bfloat16).astype(jnp.float32).T
    span = shifted.shape[1]
    own_f32[...] = extended[:rows]
    for i in range(chunk):
        shifted[i] = extended[i : i + span]
    slots, parts = buffers.shape[0], sems.shape[1]
    part = chunk // parts
    copies = []
    for m in range(rows // chunk):
        slot = m % slots
        if m >= slots:
            for copy in copies[m - slots]:
                copy.wait()
        base = m * chunk
        for i in range(chunk):
            a = own_f32[base + i : base + i + 1, :]
            b = shifted[i, base : base + LAGS, :]
            acc_re, acc_im = product_terms(a, b)
            store_row(buffers.at[slot], i, acc_re, acc_im, 1)
        group = []
        for p in range(parts):
            copy = pltpu.make_async_copy(
                buffers.at[slot, pl.ds(p * part, part)],
                out_hbm.at[pl.ds(base + p * part, part)],
                sems.at[slot, p],
            )
            copy.start()
            group.append(copy)
        copies.append(group)
    for group in copies[-slots:]:
        for copy in group:
            copy.wait()


def fused_spectra(samples, filter_taps, table_t, rows):
    length, channels = samples.shape
    chunk = 8
    span = channels - chunk
    return pl.pallas_call(
        functools.partial(fused_kernel, rows, chunk),
        out_shape=jax.ShapeDtypeStruct((rows, LAGS, NFFT), jnp.bfloat16),
        in_specs=[pl.BlockSpec(memory_space=pltpu.SMEM)] + [pl.BlockSpec(memory_space=pltpu.VMEM)] * 2,
        out_specs=pl.BlockSpec(memory_space=pl.ANY),
        scratch_shapes=[
            pltpu.VMEM((rows, NFFT), jnp.float32),
            pltpu.VMEM((chunk, span, NFFT), jnp.float32),
            pltpu.VMEM((4, chunk, LAGS, NFFT), jnp.bfloat16),
            pltpu.SemaphoreType.DMA((4, 8)),
        ],
        cost_estimate=pl.CostEstimate(
            flops=6 * rows * LAGS * NF + 12 * channels * (NF * 320 * length // 256 + NFFT * NFFT),
            transcendentals=2 * NF * channels,
            bytes_accessed=rows * LAGS * NFFT * 2 + 2 * samples.size + 2 * table_t.size,
        ),
    )(filter_taps, samples, table_t)


def cross_spectra(own, extended):
    rows, segments, columns = own.shape
    reach_rows = extended.shape[0]
    own_flat = own.reshape(rows, segments * columns)
    ext_flat = extended.reshape(reach_rows, segments * columns)
    rows_per_step = 8
    span = reach_rows - rows_per_step
    scratch_bytes = rows_per_step * span * segments * columns * 4
    cost = pl.CostEstimate(
        flops=6 * rows * LAGS * NF * segments,
        transcendentals=0,
        bytes_accessed=rows * LAGS * columns * 2 + 2 * segments * (rows + reach_rows) * columns,
    )
    common = dict(
        out_shape=jax.ShapeDtypeStruct((rows, LAGS, columns), jnp.bfloat16),
        grid=(rows // rows_per_step,),
        in_specs=[
            pl.BlockSpec((rows, segments * columns), lambda i: (0, 0)),
            pl.BlockSpec((reach_rows, segments * columns), lambda i: (0, 0)),
        ],
        out_specs=pl.BlockSpec((rows_per_step, LAGS, columns), lambda i: (i, 0, 0)),
        cost_estimate=cost,
    )
    if scratch_bytes <= 8 * 1024 * 1024:
        return pl.pallas_call(
            functools.partial(cross_kernel_shifted, segments, rows_per_step),
            scratch_shapes=[
                pltpu.VMEM((rows, segments * columns), jnp.float32),
                pltpu.VMEM((rows_per_step, span, segments * columns), jnp.float32),
            ],
            compiler_params=pltpu.CompilerParams(dimension_semantics=("arbitrary",)),
            **common,
        )(own_flat, ext_flat)
    return pl.pallas_call(
        functools.partial(cross_kernel, segments, rows_per_step), **common
    )(own_flat, ext_flat)


def body(strain, filter_taps):
    extent = lax.axis_size("ta")
    columns_n = lax.axis_size("col")
    section_rows, slab = strain.shape
    block_rows = section_rows // extent
    reach = LAGS // block_rows
    turned = strain.T
    route = [(c + 1, c) for c in range(columns_n - 1)]
    following = lax.ppermute(turned, "col", route)
    tail = following[:, : reach * block_rows]
    width = (reach + 1) * block_rows
    windows = channel_windows(turned, tail, extent, width, reach * block_rows)
    gathered = lax.all_to_all(windows, "ta", split_axis=0, concat_axis=0, tiled=True)
    samples = gathered.reshape(extent * slab, width)
    if extent * slab == 2 * NFFT:
        table_parts = jnp.stack(split_three_kept(fourier_table_t()))
        return fused_spectra(samples, filter_taps, table_parts, block_rows)[None]
    filtered = decimate_t(samples.astype(jnp.float32), filter_taps)
    whitened_t = whiten_t(filtered)
    segments, columns, _ = whitened_t.shape
    if segments * 8 * width * columns * 4 <= 8 * 1024 * 1024:
        flat = whitened_t.reshape(segments * columns, width)
        return cross_spectra_pieces([flat])[None]
    extended = whitened_t.transpose(2, 0, 1)
    return cross_spectra(extended[:block_rows], extended)[None]


def solution(mesh):
    return jax.shard_map(
        body,
        mesh=mesh,
        in_specs=(P("col", "ta"), P()),
        out_specs=P("col", "ta", None, None),
        check_vma=False,
    )
```

```python
import functools

import jax
import jax.numpy as jnp
from jax import lax
from jax.experimental import pallas as pl
from jax.experimental.pallas import tpu as pltpu
from jax.sharding import PartitionSpec as P

NFFT = 256
NF = 128
LAGS = 128


def tap_rows(filter_taps, outputs):
    tap_count = filter_taps.shape[0]
    window = 2 * outputs + tap_count
    flipped = filter_taps[::-1]
    period = jnp.concatenate([flipped, jnp.zeros((window + 2 - tap_count,), jnp.float32)])
    repeated = jnp.tile(period, outputs)[: outputs * window]
    return repeated.reshape(outputs, window)


def decimate_t(samples, filter_taps):
    length, channels = samples.shape
    tap_count = filter_taps.shape[0]
    outputs = min(length, NFFT) // 2
    blocks = length // (2 * outputs)
    joined = jnp.concatenate(
        [
            jnp.zeros((tap_count, channels), jnp.float32),
            samples,
            jnp.zeros((2 * outputs - tap_count, channels), jnp.float32),
        ],
        axis=0,
    )
    joined = joined.reshape(blocks + 1, 2 * outputs, channels)
    windows = jnp.concatenate([joined[:-1], joined[1:, :tap_count]], axis=1)
    matrix = tap_rows(filter_taps, outputs)
    result = jnp.einsum("tw,bwc->btc", matrix, windows, precision=lax.Precision.HIGHEST)
    return result.reshape(blocks * outputs, channels).astype(jnp.bfloat16)


def fourier_table():
    moment = lax.broadcasted_iota(jnp.int32, (NFFT, NF), 0)
    frequency = lax.broadcasted_iota(jnp.int32, (NFFT, NF), 1) + 1
    phase_index = moment * frequency % NFFT
    angles = phase_index.astype(jnp.float32) * (2.0 * jnp.pi / NFFT)
    window_taper = 0.5 - 0.5 * jnp.cos(moment.astype(jnp.float32) * (2.0 * jnp.pi / NFFT))
    return jnp.concatenate(
        [window_taper * jnp.cos(angles), -window_taper * jnp.sin(angles)], axis=1
    )


def fourier_table_t():
    moment = lax.broadcasted_iota(jnp.int32, (NFFT, NFFT), 1)
    frequency = lax.broadcasted_iota(jnp.int32, (NFFT, NFFT), 0) % NF + 1
    phase_index = moment * frequency % NFFT
    angles = phase_index.astype(jnp.float32) * (2.0 * jnp.pi / NFFT)
    window_taper = 0.5 - 0.5 * jnp.cos(moment.astype(jnp.float32) * (2.0 * jnp.pi / NFFT))
    real_rows = lax.broadcasted_iota(jnp.int32, (NFFT, NFFT), 0) < NF
    return jnp.where(real_rows, window_taper * jnp.cos(angles), -window_taper * jnp.sin(angles))


def whiten_t(filtered):
    length, channels = filtered.shape
    pieces = filtered.reshape(length // NF, NF, channels)
    segment_rows = jnp.concatenate([pieces[:-1], pieces[1:]], axis=1)
    spectrum = jnp.einsum(
        "nf,snc->sfc",
        fourier_table(),
        segment_rows.astype(jnp.float32),
        precision=lax.Precision.HIGHEST,
    )
    real_part = spectrum[:, :NF]
    imag_part = spectrum[:, NF:]
    powers = real_part * real_part + imag_part * imag_part
    mean_power = jnp.mean(powers, axis=1, keepdims=True)
    whitening = 1.0 / jnp.sqrt(powers + mean_power + 1e-06)
    return jnp.concatenate([real_part * whitening, imag_part * whitening], axis=1).astype(
        jnp.bfloat16
    )


def windows_kernel(width, tail_rows, x_ref, out_ref):
    x = x_ref[...].astype(jnp.float32)
    padded = jnp.concatenate([x, jnp.zeros((x.shape[0], tail_rows), jnp.float32)], axis=1)
    step = (padded.shape[1] - width) // (out_ref.shape[0] - 1)
    for j in range(out_ref.shape[0]):
        out_ref[j] = padded[:, j * step : j * step + width].astype(out_ref.dtype)


def channel_windows(turned, tail, extent, width, tail_rows):
    slab, rows = turned.shape
    windows = pl.pallas_call(
        functools.partial(windows_kernel, width, tail_rows),
        out_shape=jax.ShapeDtypeStruct((extent, slab, width), turned.dtype),
        cost_estimate=pl.CostEstimate(
            flops=0, transcendentals=0, bytes_accessed=2 * (slab * rows + extent * slab * width)
        ),
    )(turned)
    step = (rows + tail_rows - width) // (extent - 1)
    count = -(-tail_rows // step)
    first = extent - count
    padded = jnp.concatenate([turned[:, first * step :], tail], axis=1)
    patch = jnp.stack([padded[:, j * step : j * step + width] for j in range(count)])
    return lax.dynamic_update_slice(windows, patch, (first, 0, 0))


def cross_kernel(segments, rows_per_step, own_ref, ext_ref, out_ref):
    step = pl.program_id(0)
    base = pl.multiple_of(step * rows_per_step, rows_per_step)
    for i in range(rows_per_step):
        acc_re = None
        acc_im = None
        for s in range(segments):
            a = own_ref[pl.ds(base, rows_per_step), pl.ds(s * NFFT, NFFT)]
            a = a.astype(jnp.float32)[i : i + 1]
            window = ext_ref[pl.ds(base, LAGS + rows_per_step), pl.ds(s * NFFT, NFFT)]
            b = window.astype(jnp.float32)[i : i + LAGS]
            terms = product_terms(a, b)
            if acc_re is None:
                acc_re, acc_im = terms
            else:
                acc_re = [x + y for x, y in zip(acc_re, terms[0])]
                acc_im = [x + y for x, y in zip(acc_im, terms[1])]
        store_row(out_ref, i, acc_re, acc_im, segments)


def product_terms(a, b):
    ar = a[:, :NF]
    ai = a[:, NF:]
    br = b[:, :NF]
    bi = b[:, NF:]
    return [ar * br, ai * bi], [ai * br, ar * bi]


def store_row(out_ref, i, acc_re, acc_im, segments):
    re = acc_re[0] + acc_re[1]
    im = acc_im[0] - acc_im[1]
    if segments > 1:
        re = re / segments
        im = im / segments
    out_ref[i, :, :NF] = re.astype(out_ref.dtype)
    out_ref[i, :, NF:] = im.astype(out_ref.dtype)


def cross_kernel_shifted(segments, rows_per_step, own_ref, ext_ref, out_ref, own_f32, shifted):
    step = pl.program_id(0)
    span = shifted.shape[1]

    @pl.when(step == 0)
    def _():
        own_f32[...] = own_ref[...].astype(jnp.float32)
        whole = ext_ref[...].astype(jnp.float32)
        for i in range(rows_per_step):
            shifted[i] = whole[i : i + span]

    base = pl.multiple_of(step * rows_per_step, rows_per_step)
    for i in range(rows_per_step):
        acc_re = None
        acc_im = None
        for s in range(segments):
            a = own_f32[pl.ds(base + i, 1), pl.ds(s * NFFT, NFFT)]
            b = shifted[i, pl.ds(base, LAGS), pl.ds(s * NFFT, NFFT)]
            terms = product_terms(a, b)
            if acc_re is None:
                acc_re, acc_im = terms
            else:
                acc_re = [x + y for x, y in zip(acc_re, terms[0])]
                acc_im = [x + y for x, y in zip(acc_im, terms[1])]
        store_row(out_ref, i, acc_re, acc_im, segments)


def cross_kernel_pieces(segments, rows, chunk, *refs):
    pieces = refs[:-5]
    out_hbm, own_f32, shifted, buffers, sems = refs[-5:]
    span = shifted.shape[1]
    extended = jnp.concatenate(
        [
            jnp.concatenate(
                [piece[s * NFFT : (s + 1) * NFFT, :].astype(jnp.float32).T for s in range(segments)],
                axis=1,
            )
            for piece in pieces
        ],
        axis=0,
    )
    own_f32[...] = extended[:rows]
    for i in range(chunk):
        shifted[i] = extended[i : i + span]
    slots, parts = buffers.shape[0], sems.shape[1]
    part = chunk // parts
    copies = []
    for m in range(rows // chunk):
        slot = m % slots
        if m >= slots:
            for copy in copies[m - slots]:
                copy.wait()
        base = m * chunk
        for i in range(chunk):
            acc_re = None
            acc_im = None
            for s in range(segments):
                a = own_f32[base + i : base + i + 1, s * NFFT : (s + 1) * NFFT]
                b = shifted[i, base : base + LAGS, s * NFFT : (s + 1) * NFFT]
                terms = product_terms(a, b)
                if acc_re is None:
                    acc_re, acc_im = terms
                else:
                    acc_re = [x + y for x, y in zip(acc_re, terms[0])]
                    acc_im = [x + y for x, y in zip(acc_im, terms[1])]
            store_row(buffers.at[slot], i, acc_re, acc_im, segments)
        group = []
        for p in range(parts):
            copy = pltpu.make_async_copy(
                buffers.at[slot, pl.ds(p * part, part)],
                out_hbm.at[pl.ds(base + p * part, part)],
                sems.at[slot, p],
            )
            copy.start()
            group.append(copy)
        copies.append(group)
    for group in copies[-slots:]:
        for copy in group:
            copy.wait()


def cross_spectra_pieces(pieces):
    width = pieces[0].shape[0]
    rows = sum(piece.shape[1] for piece in pieces) - LAGS
    segments = width // NFFT
    chunk = 8
    span = rows + LAGS - chunk
    return pl.pallas_call(
        functools.partial(cross_kernel_pieces, segments, rows, chunk),
        out_shape=jax.ShapeDtypeStruct((rows, LAGS, NFFT), jnp.bfloat16),
        in_specs=[pl.BlockSpec(memory_space=pltpu.VMEM)] * len(pieces),
        out_specs=pl.BlockSpec(memory_space=pl.ANY),
        scratch_shapes=[
            pltpu.VMEM((rows, width), jnp.float32),
            pltpu.VMEM((chunk, span, width), jnp.float32),
            pltpu.VMEM((4, chunk, LAGS, NFFT), jnp.bfloat16),
            pltpu.SemaphoreType.DMA((4, 4)),
        ],
        cost_estimate=pl.CostEstimate(
            flops=6 * rows * LAGS * NF * segments,
            transcendentals=0,
            bytes_accessed=rows * LAGS * NFFT * 2 + 2 * (rows + LAGS) * width,
        ),
    )(*pieces)


def split_three(values):
    high = values.astype(jnp.bfloat16)
    rest = values - high.astype(jnp.float32)
    middle = rest.astype(jnp.bfloat16)
    low = (rest - middle.astype(jnp.float32)).astype(jnp.bfloat16)
    return [high, middle, low]


def split_three_kept(values):
    high = lax.reduce_precision(values, exponent_bits=8, mantissa_bits=7)
    rest = values - high
    middle = lax.reduce_precision(rest, exponent_bits=8, mantissa_bits=7)
    low = rest - middle
    return [part.astype(jnp.bfloat16) for part in (high, middle, low)]


def exact_dot(parts, operand):
    total = None
    for part in parts:
        term = jnp.dot(part, operand, preferred_element_type=jnp.float32)
        total = term if total is None else total + term
    return total


def fused_kernel(rows, chunk, taps_ref, samples_ref, table_ref, out_hbm, own_f32, shifted,
                 buffers, sems):
    tap_count = taps_ref.shape[0]
    outputs = NFFT // 2
    length, channels = samples_ref.shape
    blocks = length // (2 * outputs)
    lanes = 3 * NF
    lane = lax.broadcasted_iota(jnp.int32, (1, lanes), 1)
    row = jnp.zeros((1, lanes), jnp.float32)
    for k in range(tap_count):
        row = jnp.where(lane == tap_count - 1 - k, taps_ref[k], row)
    matrices = []
    for part in split_three(row):
        rolled = pltpu.roll(
            jnp.broadcast_to(part.astype(jnp.float32), (outputs, lanes)), 0, 1, stride=2, stride_axis=0
        )
        matrices.append(rolled[:, : 2 * outputs + tap_count].astype(jnp.bfloat16))
    x = samples_ref[...]
    joined = jnp.concatenate(
        [
            jnp.zeros((tap_count, channels), x.dtype),
            x,
            jnp.zeros((2 * outputs - tap_count, channels), x.dtype),
        ],
        axis=0,
    )
    filtered = jnp.concatenate(
        [
            exact_dot(matrices, joined[b * 2 * outputs : b * 2 * outputs + 2 * outputs + tap_count])
            for b in range(blocks)
        ],
        axis=0,
    )
    filtered = filtered.astype(jnp.bfloat16)
    spectrum = exact_dot([table_ref[p] for p in range(table_ref.shape[0])], filtered)
    real_part = spectrum[:NF]
    imag_part = spectrum[NF:]
    powers = real_part * real_part + imag_part * imag_part
    mean_power = jnp.mean(powers, axis=0, keepdims=True)
    whitening = 1.0 / jnp.sqrt(powers + mean_power + 1e-06)
    whitened = jnp.concatenate([real_part * whitening, imag_part * whitening], axis=0)
    extended = whitened.astype(jnp.bfloat16).astype(jnp.float32).T
    span = shifted.shape[1]
    own_f32[...] = extended[:rows]
    for i in range(chunk):
        shifted[i] = extended[i : i + span]
    slots, parts = buffers.shape[0], sems.shape[1]
    part = chunk // parts
    copies = []
    for m in range(rows // chunk):
        slot = m % slots
        if m >= slots:
            for copy in copies[m - slots]:
                copy.wait()
        base = m * chunk
        for i in range(chunk):
            a = own_f32[base + i : base + i + 1, :]
            b = shifted[i, base : base + LAGS, :]
            acc_re, acc_im = product_terms(a, b)
            store_row(buffers.at[slot], i, acc_re, acc_im, 1)
        group = []
        for p in range(parts):
            copy = pltpu.make_async_copy(
                buffers.at[slot, pl.ds(p * part, part)],
                out_hbm.at[pl.ds(base + p * part, part)],
                sems.at[slot, p],
            )
            copy.start()
            group.append(copy)
        copies.append(group)
    for group in copies[-slots:]:
        for copy in group:
            copy.wait()


def fused_spectra(samples, filter_taps, table_t, rows):
    length, channels = samples.shape
    chunk = 8
    span = channels - chunk
    return pl.pallas_call(
        functools.partial(fused_kernel, rows, chunk),
        out_shape=jax.ShapeDtypeStruct((rows, LAGS, NFFT), jnp.bfloat16),
        in_specs=[pl.BlockSpec(memory_space=pltpu.SMEM)] + [pl.BlockSpec(memory_space=pltpu.VMEM)] * 2,
        out_specs=pl.BlockSpec(memory_space=pl.ANY),
        scratch_shapes=[
            pltpu.VMEM((rows, NFFT), jnp.float32),
            pltpu.VMEM((chunk, span, NFFT), jnp.float32),
            pltpu.VMEM((4, chunk, LAGS, NFFT), jnp.bfloat16),
            pltpu.SemaphoreType.DMA((4, 4)),
        ],
        cost_estimate=pl.CostEstimate(
            flops=6 * rows * LAGS * NF + 12 * channels * (NF * 320 * length // 256 + NFFT * NFFT),
            transcendentals=2 * NF * channels,
            bytes_accessed=rows * LAGS * NFFT * 2 + 2 * samples.size + 2 * table_t.size,
        ),
    )(filter_taps, samples, table_t)


def cross_spectra(own, extended):
    rows, segments, columns = own.shape
    reach_rows = extended.shape[0]
    own_flat = own.reshape(rows, segments * columns)
    ext_flat = extended.reshape(reach_rows, segments * columns)
    rows_per_step = 8
    span = reach_rows - rows_per_step
    scratch_bytes = rows_per_step * span * segments * columns * 4
    cost = pl.CostEstimate(
        flops=6 * rows * LAGS * NF * segments,
        transcendentals=0,
        bytes_accessed=rows * LAGS * columns * 2 + 2 * segments * (rows + reach_rows) * columns,
    )
    common = dict(
        out_shape=jax.ShapeDtypeStruct((rows, LAGS, columns), jnp.bfloat16),
        grid=(rows // rows_per_step,),
        in_specs=[
            pl.BlockSpec((rows, segments * columns), lambda i: (0, 0)),
            pl.BlockSpec((reach_rows, segments * columns), lambda i: (0, 0)),
        ],
        out_specs=pl.BlockSpec((rows_per_step, LAGS, columns), lambda i: (i, 0, 0)),
        cost_estimate=cost,
    )
    if scratch_bytes <= 8 * 1024 * 1024:
        return pl.pallas_call(
            functools.partial(cross_kernel_shifted, segments, rows_per_step),
            scratch_shapes=[
                pltpu.VMEM((rows, segments * columns), jnp.float32),
                pltpu.VMEM((rows_per_step, span, segments * columns), jnp.float32),
            ],
            compiler_params=pltpu.CompilerParams(dimension_semantics=("arbitrary",)),
            **common,
        )(own_flat, ext_flat)
    return pl.pallas_call(
        functools.partial(cross_kernel, segments, rows_per_step), **common
    )(own_flat, ext_flat)


def body(strain, filter_taps):
    extent = lax.axis_size("ta")
    columns_n = lax.axis_size("col")
    section_rows, slab = strain.shape
    block_rows = section_rows // extent
    reach = LAGS // block_rows
    turned = strain.T
    route = [(c + 1, c) for c in range(columns_n - 1)]
    following = lax.ppermute(turned, "col", route)
    tail = following[:, : reach * block_rows]
    width = (reach + 1) * block_rows
    windows = channel_windows(turned, tail, extent, width, reach * block_rows)
    gathered = lax.all_to_all(windows, "ta", split_axis=0, concat_axis=0, tiled=True)
    samples = gathered.reshape(extent * slab, width)
    if extent * slab == 2 * NFFT:
        table_parts = jnp.stack(split_three_kept(fourier_table_t()))
        return fused_spectra(samples, filter_taps, table_parts, block_rows)[None]
    filtered = decimate_t(samples.astype(jnp.float32), filter_taps)
    whitened_t = whiten_t(filtered)
    segments, columns, _ = whitened_t.shape
    if segments * 8 * width * columns * 4 <= 8 * 1024 * 1024:
        flat = whitened_t.reshape(segments * columns, width)
        return cross_spectra_pieces([flat])[None]
    extended = whitened_t.transpose(2, 0, 1)
    return cross_spectra(extended[:block_rows], extended)[None]


def solution(mesh):
    return jax.shard_map(
        body,
        mesh=mesh,
        in_specs=(P("col", "ta"), P()),
        out_specs=P("col", "ta", None, None),
        check_vma=False,
    )
```

```python
import functools

import jax
import jax.numpy as jnp
from jax import lax
from jax.experimental import pallas as pl
from jax.experimental.pallas import tpu as pltpu
from jax.sharding import PartitionSpec as P

NFFT = 256
NF = 128
LAGS = 128


def tap_rows(filter_taps, outputs):
    tap_count = filter_taps.shape[0]
    window = 2 * outputs + tap_count
    flipped = filter_taps[::-1]
    period = jnp.concatenate([flipped, jnp.zeros((window + 2 - tap_count,), jnp.float32)])
    repeated = jnp.tile(period, outputs)[: outputs * window]
    return repeated.reshape(outputs, window)


def decimate_t(samples, filter_taps):
    length, channels = samples.shape
    tap_count = filter_taps.shape[0]
    outputs = min(length, NFFT) // 2
    blocks = length // (2 * outputs)
    joined = jnp.concatenate(
        [
            jnp.zeros((tap_count, channels), jnp.float32),
            samples,
            jnp.zeros((2 * outputs - tap_count, channels), jnp.float32),
        ],
        axis=0,
    )
    joined = joined.reshape(blocks + 1, 2 * outputs, channels)
    windows = jnp.concatenate([joined[:-1], joined[1:, :tap_count]], axis=1)
    matrix = tap_rows(filter_taps, outputs)
    result = jnp.einsum("tw,bwc->btc", matrix, windows, precision=lax.Precision.HIGHEST)
    return result.reshape(blocks * outputs, channels).astype(jnp.bfloat16)


def fourier_table():
    moment = lax.broadcasted_iota(jnp.int32, (NFFT, NF), 0)
    frequency = lax.broadcasted_iota(jnp.int32, (NFFT, NF), 1) + 1
    phase_index = moment * frequency % NFFT
    angles = phase_index.astype(jnp.float32) * (2.0 * jnp.pi / NFFT)
    window_taper = 0.5 - 0.5 * jnp.cos(moment.astype(jnp.float32) * (2.0 * jnp.pi / NFFT))
    return jnp.concatenate(
        [window_taper * jnp.cos(angles), -window_taper * jnp.sin(angles)], axis=1
    )


def fourier_table_t():
    moment = lax.broadcasted_iota(jnp.int32, (NFFT, NFFT), 1)
    frequency = lax.broadcasted_iota(jnp.int32, (NFFT, NFFT), 0) % NF + 1
    phase_index = moment * frequency % NFFT
    angles = phase_index.astype(jnp.float32) * (2.0 * jnp.pi / NFFT)
    window_taper = 0.5 - 0.5 * jnp.cos(moment.astype(jnp.float32) * (2.0 * jnp.pi / NFFT))
    real_rows = lax.broadcasted_iota(jnp.int32, (NFFT, NFFT), 0) < NF
    return jnp.where(real_rows, window_taper * jnp.cos(angles), -window_taper * jnp.sin(angles))


def whiten_t(filtered):
    length, channels = filtered.shape
    pieces = filtered.reshape(length // NF, NF, channels)
    segment_rows = jnp.concatenate([pieces[:-1], pieces[1:]], axis=1)
    spectrum = jnp.einsum(
        "nf,snc->sfc",
        fourier_table(),
        segment_rows.astype(jnp.float32),
        precision=lax.Precision.HIGHEST,
    )
    real_part = spectrum[:, :NF]
    imag_part = spectrum[:, NF:]
    powers = real_part * real_part + imag_part * imag_part
    mean_power = jnp.mean(powers, axis=1, keepdims=True)
    whitening = 1.0 / jnp.sqrt(powers + mean_power + 1e-06)
    return jnp.concatenate([real_part * whitening, imag_part * whitening], axis=1).astype(
        jnp.bfloat16
    )


def windows_kernel(width, tail_rows, x_ref, out_ref):
    x = x_ref[...].astype(jnp.float32)
    padded = jnp.concatenate([x, jnp.zeros((x.shape[0], tail_rows), jnp.float32)], axis=1)
    step = (padded.shape[1] - width) // (out_ref.shape[0] - 1)
    for j in range(out_ref.shape[0]):
        out_ref[j] = padded[:, j * step : j * step + width].astype(out_ref.dtype)


def channel_windows(turned, tail, extent, width, tail_rows):
    slab, rows = turned.shape
    windows = pl.pallas_call(
        functools.partial(windows_kernel, width, tail_rows),
        out_shape=jax.ShapeDtypeStruct((extent, slab, width), turned.dtype),
        cost_estimate=pl.CostEstimate(
            flops=0, transcendentals=0, bytes_accessed=2 * (slab * rows + extent * slab * width)
        ),
    )(turned)
    step = (rows + tail_rows - width) // (extent - 1)
    count = -(-tail_rows // step)
    first = extent - count
    for j in range(first, extent):
        offset = rows - j * step
        windows = lax.dynamic_update_slice(windows, tail[None, :, : width - offset], (j, 0, offset))
    return windows


def cross_kernel(segments, rows_per_step, own_ref, ext_ref, out_ref):
    step = pl.program_id(0)
    base = pl.multiple_of(step * rows_per_step, rows_per_step)
    for i in range(rows_per_step):
        acc_re = None
        acc_im = None
        for s in range(segments):
            a = own_ref[pl.ds(base, rows_per_step), pl.ds(s * NFFT, NFFT)]
            a = a.astype(jnp.float32)[i : i + 1]
            window = ext_ref[pl.ds(base, LAGS + rows_per_step), pl.ds(s * NFFT, NFFT)]
            b = window.astype(jnp.float32)[i : i + LAGS]
            terms = product_terms(a, b)
            if acc_re is None:
                acc_re, acc_im = terms
            else:
                acc_re = [x + y for x, y in zip(acc_re, terms[0])]
                acc_im = [x + y for x, y in zip(acc_im, terms[1])]
        store_row(out_ref, i, acc_re, acc_im, segments)


def product_terms(a, b):
    ar = a[:, :NF]
    ai = a[:, NF:]
    br = b[:, :NF]
    bi = b[:, NF:]
    return [ar * br, ai * bi], [ai * br, ar * bi]


def store_row(out_ref, i, acc_re, acc_im, segments):
    re = acc_re[0] + acc_re[1]
    im = acc_im[0] - acc_im[1]
    if segments > 1:
        re = re / segments
        im = im / segments
    out_ref[i, :, :NF] = re.astype(out_ref.dtype)
    out_ref[i, :, NF:] = im.astype(out_ref.dtype)


def cross_kernel_shifted(segments, rows_per_step, own_ref, ext_ref, out_ref, own_f32, shifted):
    step = pl.program_id(0)
    span = shifted.shape[1]

    @pl.when(step == 0)
    def _():
        own_f32[...] = own_ref[...].astype(jnp.float32)
        whole = ext_ref[...].astype(jnp.float32)
        for i in range(rows_per_step):
            shifted[i] = whole[i : i + span]

    base = pl.multiple_of(step * rows_per_step, rows_per_step)
    for i in range(rows_per_step):
        acc_re = None
        acc_im = None
        for s in range(segments):
            a = own_f32[pl.ds(base + i, 1), pl.ds(s * NFFT, NFFT)]
            b = shifted[i, pl.ds(base, LAGS), pl.ds(s * NFFT, NFFT)]
            terms = product_terms(a, b)
            if acc_re is None:
                acc_re, acc_im = terms
            else:
                acc_re = [x + y for x, y in zip(acc_re, terms[0])]
                acc_im = [x + y for x, y in zip(acc_im, terms[1])]
        store_row(out_ref, i, acc_re, acc_im, segments)


def cross_kernel_pieces(segments, rows, chunk, *refs):
    pieces = refs[:-5]
    out_hbm, own_f32, shifted, buffers, sems = refs[-5:]
    span = shifted.shape[1]
    extended = jnp.concatenate(
        [
            jnp.concatenate(
                [piece[s * NFFT : (s + 1) * NFFT, :].astype(jnp.float32).T for s in range(segments)],
                axis=1,
            )
            for piece in pieces
        ],
        axis=0,
    )
    own_f32[...] = extended[:rows]
    for i in range(chunk):
        shifted[i] = extended[i : i + span]
    slots, parts = buffers.shape[0], sems.shape[1]
    part = chunk // parts
    copies = []
    for m in range(rows // chunk):
        slot = m % slots
        if m >= slots:
            for copy in copies[m - slots]:
                copy.wait()
        base = m * chunk
        for i in range(chunk):
            acc_re = None
            acc_im = None
            for s in range(segments):
                a = own_f32[base + i : base + i + 1, s * NFFT : (s + 1) * NFFT]
                b = shifted[i, base : base + LAGS, s * NFFT : (s + 1) * NFFT]
                terms = product_terms(a, b)
                if acc_re is None:
                    acc_re, acc_im = terms
                else:
                    acc_re = [x + y for x, y in zip(acc_re, terms[0])]
                    acc_im = [x + y for x, y in zip(acc_im, terms[1])]
            store_row(buffers.at[slot], i, acc_re, acc_im, segments)
        group = []
        for p in range(parts):
            copy = pltpu.make_async_copy(
                buffers.at[slot, pl.ds(p * part, part)],
                out_hbm.at[pl.ds(base + p * part, part)],
                sems.at[slot, p],
            )
            copy.start()
            group.append(copy)
        copies.append(group)
    for group in copies[-slots:]:
        for copy in group:
            copy.wait()


def cross_spectra_pieces(pieces):
    width = pieces[0].shape[0]
    rows = sum(piece.shape[1] for piece in pieces) - LAGS
    segments = width // NFFT
    chunk = 8
    span = rows + LAGS - chunk
    return pl.pallas_call(
        functools.partial(cross_kernel_pieces, segments, rows, chunk),
        out_shape=jax.ShapeDtypeStruct((rows, LAGS, NFFT), jnp.bfloat16),
        in_specs=[pl.BlockSpec(memory_space=pltpu.VMEM)] * len(pieces),
        out_specs=pl.BlockSpec(memory_space=pl.ANY),
        scratch_shapes=[
            pltpu.VMEM((rows, width), jnp.float32),
            pltpu.VMEM((chunk, span, width), jnp.float32),
            pltpu.VMEM((4, chunk, LAGS, NFFT), jnp.bfloat16),
            pltpu.SemaphoreType.DMA((4, 4)),
        ],
        cost_estimate=pl.CostEstimate(
            flops=6 * rows * LAGS * NF * segments,
            transcendentals=0,
            bytes_accessed=rows * LAGS * NFFT * 2 + 2 * (rows + LAGS) * width,
        ),
    )(*pieces)


def split_three(values):
    high = values.astype(jnp.bfloat16)
    rest = values - high.astype(jnp.float32)
    middle = rest.astype(jnp.bfloat16)
    low = (rest - middle.astype(jnp.float32)).astype(jnp.bfloat16)
    return [high, middle, low]


def split_three_kept(values):
    high = lax.reduce_precision(values, exponent_bits=8, mantissa_bits=7)
    rest = values - high
    middle = lax.reduce_precision(rest, exponent_bits=8, mantissa_bits=7)
    low = rest - middle
    return [part.astype(jnp.bfloat16) for part in (high, middle, low)]


def exact_dot(parts, operand):
    total = None
    for part in parts:
        term = jnp.dot(part, operand, preferred_element_type=jnp.float32)
        total = term if total is None else total + term
    return total


def fused_kernel(rows, chunk, taps_ref, samples_ref, table_ref, out_hbm, own_f32, shifted,
                 buffers, sems):
    tap_count = taps_ref.shape[0]
    outputs = NFFT // 2
    length, channels = samples_ref.shape
    blocks = length // (2 * outputs)
    lanes = 3 * NF
    lane = lax.broadcasted_iota(jnp.int32, (1, lanes), 1)
    row = jnp.zeros((1, lanes), jnp.float32)
    for k in range(tap_count):
        row = jnp.where(lane == tap_count - 1 - k, taps_ref[k], row)
    matrices = []
    for part in split_three(row):
        rolled = pltpu.roll(
            jnp.broadcast_to(part.astype(jnp.float32), (outputs, lanes)), 0, 1, stride=2, stride_axis=0
        )
        matrices.append(rolled[:, : 2 * outputs + tap_count].astype(jnp.bfloat16))
    x = samples_ref[...]
    joined = jnp.concatenate(
        [
            jnp.zeros((tap_count, channels), x.dtype),
            x,
            jnp.zeros((2 * outputs - tap_count, channels), x.dtype),
        ],
        axis=0,
    )
    filtered = jnp.concatenate(
        [
            exact_dot(matrices, joined[b * 2 * outputs : b * 2 * outputs + 2 * outputs + tap_count])
            for b in range(blocks)
        ],
        axis=0,
    )
    filtered = filtered.astype(jnp.bfloat16)
    spectrum = exact_dot([table_ref[p] for p in range(table_ref.shape[0])], filtered)
    real_part = spectrum[:NF]
    imag_part = spectrum[NF:]
    powers = real_part * real_part + imag_part * imag_part
    mean_power = jnp.mean(powers, axis=0, keepdims=True)
    whitening = 1.0 / jnp.sqrt(powers + mean_power + 1e-06)
    whitened = jnp.concatenate([real_part * whitening, imag_part * whitening], axis=0)
    extended = whitened.astype(jnp.bfloat16).astype(jnp.float32).T
    span = shifted.shape[1]
    own_f32[...] = extended[:rows]
    for i in range(chunk):
        shifted[i] = extended[i : i + span]
    slots, parts = buffers.shape[0], sems.shape[1]
    part = chunk // parts
    copies = []
    for m in range(rows // chunk):
        slot = m % slots
        if m >= slots:
            for copy in copies[m - slots]:
                copy.wait()
        base = m * chunk
        for i in range(chunk):
            a = own_f32[base + i : base + i + 1, :]
            b = shifted[i, base : base + LAGS, :]
            acc_re, acc_im = product_terms(a, b)
            store_row(buffers.at[slot], i, acc_re, acc_im, 1)
        group = []
        for p in range(parts):
            copy = pltpu.make_async_copy(
                buffers.at[slot, pl.ds(p * part, part)],
                out_hbm.at[pl.ds(base + p * part, part)],
                sems.at[slot, p],
            )
            copy.start()
            group.append(copy)
        copies.append(group)
    for group in copies[-slots:]:
        for copy in group:
            copy.wait()


def fused_spectra(samples, filter_taps, table_t, rows):
    length, channels = samples.shape
    chunk = 8
    span = channels - chunk
    return pl.pallas_call(
        functools.partial(fused_kernel, rows, chunk),
        out_shape=jax.ShapeDtypeStruct((rows, LAGS, NFFT), jnp.bfloat16),
        in_specs=[pl.BlockSpec(memory_space=pltpu.SMEM)] + [pl.BlockSpec(memory_space=pltpu.VMEM)] * 2,
        out_specs=pl.BlockSpec(memory_space=pl.ANY),
        scratch_shapes=[
            pltpu.VMEM((rows, NFFT), jnp.float32),
            pltpu.VMEM((chunk, span, NFFT), jnp.float32),
            pltpu.VMEM((4, chunk, LAGS, NFFT), jnp.bfloat16),
            pltpu.SemaphoreType.DMA((4, 4)),
        ],
        cost_estimate=pl.CostEstimate(
            flops=6 * rows * LAGS * NF + 12 * channels * (NF * 320 * length // 256 + NFFT * NFFT),
            transcendentals=2 * NF * channels,
            bytes_accessed=rows * LAGS * NFFT * 2 + 2 * samples.size + 2 * table_t.size,
        ),
    )(filter_taps, samples, table_t)


def cross_spectra(own, extended):
    rows, segments, columns = own.shape
    reach_rows = extended.shape[0]
    own_flat = own.reshape(rows, segments * columns)
    ext_flat = extended.reshape(reach_rows, segments * columns)
    rows_per_step = 8
    span = reach_rows - rows_per_step
    scratch_bytes = rows_per_step * span * segments * columns * 4
    cost = pl.CostEstimate(
        flops=6 * rows * LAGS * NF * segments,
        transcendentals=0,
        bytes_accessed=rows * LAGS * columns * 2 + 2 * segments * (rows + reach_rows) * columns,
    )
    common = dict(
        out_shape=jax.ShapeDtypeStruct((rows, LAGS, columns), jnp.bfloat16),
        grid=(rows // rows_per_step,),
        in_specs=[
            pl.BlockSpec((rows, segments * columns), lambda i: (0, 0)),
            pl.BlockSpec((reach_rows, segments * columns), lambda i: (0, 0)),
        ],
        out_specs=pl.BlockSpec((rows_per_step, LAGS, columns), lambda i: (i, 0, 0)),
        cost_estimate=cost,
    )
    if scratch_bytes <= 8 * 1024 * 1024:
        return pl.pallas_call(
            functools.partial(cross_kernel_shifted, segments, rows_per_step),
            scratch_shapes=[
                pltpu.VMEM((rows, segments * columns), jnp.float32),
                pltpu.VMEM((rows_per_step, span, segments * columns), jnp.float32),
            ],
            compiler_params=pltpu.CompilerParams(dimension_semantics=("arbitrary",)),
            **common,
        )(own_flat, ext_flat)
    return pl.pallas_call(
        functools.partial(cross_kernel, segments, rows_per_step), **common
    )(own_flat, ext_flat)


def body(strain, filter_taps):
    extent = lax.axis_size("ta")
    columns_n = lax.axis_size("col")
    section_rows, slab = strain.shape
    block_rows = section_rows // extent
    reach = LAGS // block_rows
    turned = strain.T
    route = [(c + 1, c) for c in range(columns_n - 1)]
    following = lax.ppermute(turned, "col", route)
    tail = following[:, : reach * block_rows]
    width = (reach + 1) * block_rows
    windows = channel_windows(turned, tail, extent, width, reach * block_rows)
    gathered = lax.all_to_all(windows, "ta", split_axis=0, concat_axis=0, tiled=True)
    samples = gathered.reshape(extent * slab, width)
    if extent * slab == 2 * NFFT:
        table_parts = jnp.stack(split_three_kept(fourier_table_t()))
        return fused_spectra(samples, filter_taps, table_parts, block_rows)[None]
    filtered = decimate_t(samples.astype(jnp.float32), filter_taps)
    whitened_t = whiten_t(filtered)
    segments, columns, _ = whitened_t.shape
    if segments * 8 * width * columns * 4 <= 8 * 1024 * 1024:
        flat = whitened_t.reshape(segments * columns, width)
        return cross_spectra_pieces([flat])[None]
    extended = whitened_t.transpose(2, 0, 1)
    return cross_spectra(extended[:block_rows], extended)[None]


def solution(mesh):
    return jax.shard_map(
        body,
        mesh=mesh,
        in_specs=(P("col", "ta"), P()),
        out_specs=P("col", "ta", None, None),
        check_vma=False,
    )
```

```python
import functools

import jax
import jax.numpy as jnp
from jax import lax
from jax.experimental import pallas as pl
from jax.experimental.pallas import tpu as pltpu
from jax.sharding import PartitionSpec as P

NFFT = 256
NF = 128
LAGS = 128


def tap_rows(filter_taps, outputs):
    tap_count = filter_taps.shape[0]
    window = 2 * outputs + tap_count
    flipped = filter_taps[::-1]
    period = jnp.concatenate([flipped, jnp.zeros((window + 2 - tap_count,), jnp.float32)])
    repeated = jnp.tile(period, outputs)[: outputs * window]
    return repeated.reshape(outputs, window)


def decimate_t(samples, filter_taps):
    length, channels = samples.shape
    tap_count = filter_taps.shape[0]
    outputs = min(length, NFFT) // 2
    blocks = length // (2 * outputs)
    joined = jnp.concatenate(
        [
            jnp.zeros((tap_count, channels), jnp.float32),
            samples,
            jnp.zeros((2 * outputs - tap_count, channels), jnp.float32),
        ],
        axis=0,
    )
    joined = joined.reshape(blocks + 1, 2 * outputs, channels)
    windows = jnp.concatenate([joined[:-1], joined[1:, :tap_count]], axis=1)
    matrix = tap_rows(filter_taps, outputs)
    result = jnp.einsum("tw,bwc->btc", matrix, windows, precision=lax.Precision.HIGHEST)
    return result.reshape(blocks * outputs, channels).astype(jnp.bfloat16)


def fourier_table():
    moment = lax.broadcasted_iota(jnp.int32, (NFFT, NF), 0)
    frequency = lax.broadcasted_iota(jnp.int32, (NFFT, NF), 1) + 1
    phase_index = moment * frequency % NFFT
    angles = phase_index.astype(jnp.float32) * (2.0 * jnp.pi / NFFT)
    window_taper = 0.5 - 0.5 * jnp.cos(moment.astype(jnp.float32) * (2.0 * jnp.pi / NFFT))
    return jnp.concatenate(
        [window_taper * jnp.cos(angles), -window_taper * jnp.sin(angles)], axis=1
    )


def fourier_table_t():
    moment = lax.broadcasted_iota(jnp.int32, (NFFT, NFFT), 1)
    frequency = lax.broadcasted_iota(jnp.int32, (NFFT, NFFT), 0) % NF + 1
    phase_index = moment * frequency % NFFT
    angles = phase_index.astype(jnp.float32) * (2.0 * jnp.pi / NFFT)
    window_taper = 0.5 - 0.5 * jnp.cos(moment.astype(jnp.float32) * (2.0 * jnp.pi / NFFT))
    real_rows = lax.broadcasted_iota(jnp.int32, (NFFT, NFFT), 0) < NF
    return jnp.where(real_rows, window_taper * jnp.cos(angles), -window_taper * jnp.sin(angles))


def whiten_t(filtered):
    length, channels = filtered.shape
    pieces = filtered.reshape(length // NF, NF, channels)
    segment_rows = jnp.concatenate([pieces[:-1], pieces[1:]], axis=1)
    spectrum = jnp.einsum(
        "nf,snc->sfc",
        fourier_table(),
        segment_rows.astype(jnp.float32),
        precision=lax.Precision.HIGHEST,
    )
    real_part = spectrum[:, :NF]
    imag_part = spectrum[:, NF:]
    powers = real_part * real_part + imag_part * imag_part
    mean_power = jnp.mean(powers, axis=1, keepdims=True)
    whitening = 1.0 / jnp.sqrt(powers + mean_power + 1e-06)
    return jnp.concatenate([real_part * whitening, imag_part * whitening], axis=1).astype(
        jnp.bfloat16
    )


def windows_kernel(width, tail_rows, x_ref, out_ref, last_ref):
    x = x_ref[...].astype(jnp.float32)
    padded = jnp.concatenate([x, jnp.zeros((x.shape[0], tail_rows), jnp.float32)], axis=1)
    step = (padded.shape[1] - width) // (out_ref.shape[0] - 1)
    for j in range(out_ref.shape[0]):
        out_ref[j] = padded[:, j * step : j * step + width].astype(out_ref.dtype)
    last_ref[...] = x[:, x.shape[1] - last_ref.shape[1] :].astype(last_ref.dtype)


def channel_windows(turned, tail, extent, width, tail_rows):
    slab, rows = turned.shape
    step = (rows + tail_rows - width) // (extent - 1)
    count = -(-tail_rows // step)
    first = extent - count
    windows, last = pl.pallas_call(
        functools.partial(windows_kernel, width, tail_rows),
        out_shape=(
            jax.ShapeDtypeStruct((extent, slab, width), turned.dtype),
            jax.ShapeDtypeStruct((slab, rows - first * step), turned.dtype),
        ),
        cost_estimate=pl.CostEstimate(
            flops=0, transcendentals=0, bytes_accessed=2 * (slab * rows + extent * slab * width)
        ),
    )(turned)
    padded = jnp.concatenate([last, tail], axis=1)
    patch = jnp.stack([padded[:, j * step : j * step + width] for j in range(count)])
    return lax.dynamic_update_slice(windows, patch, (first, 0, 0))


def cross_kernel(segments, rows_per_step, own_ref, ext_ref, out_ref):
    step = pl.program_id(0)
    base = pl.multiple_of(step * rows_per_step, rows_per_step)
    for i in range(rows_per_step):
        acc_re = None
        acc_im = None
        for s in range(segments):
            a = own_ref[pl.ds(base, rows_per_step), pl.ds(s * NFFT, NFFT)]
            a = a.astype(jnp.float32)[i : i + 1]
            window = ext_ref[pl.ds(base, LAGS + rows_per_step), pl.ds(s * NFFT, NFFT)]
            b = window.astype(jnp.float32)[i : i + LAGS]
            terms = product_terms(a, b)
            if acc_re is None:
                acc_re, acc_im = terms
            else:
                acc_re = [x + y for x, y in zip(acc_re, terms[0])]
                acc_im = [x + y for x, y in zip(acc_im, terms[1])]
        store_row(out_ref, i, acc_re, acc_im, segments)


def product_terms(a, b):
    ar = a[:, :NF]
    ai = a[:, NF:]
    br = b[:, :NF]
    bi = b[:, NF:]
    return [ar * br, ai * bi], [ai * br, ar * bi]


def store_row(out_ref, i, acc_re, acc_im, segments):
    re = acc_re[0] + acc_re[1]
    im = acc_im[0] - acc_im[1]
    if segments > 1:
        re = re / segments
        im = im / segments
    out_ref[i, :, :NF] = re.astype(out_ref.dtype)
    out_ref[i, :, NF:] = im.astype(out_ref.dtype)


def cross_kernel_shifted(segments, rows_per_step, own_ref, ext_ref, out_ref, own_f32, shifted):
    step = pl.program_id(0)
    span = shifted.shape[1]

    @pl.when(step == 0)
    def _():
        own_f32[...] = own_ref[...].astype(jnp.float32)
        whole = ext_ref[...].astype(jnp.float32)
        for i in range(rows_per_step):
            shifted[i] = whole[i : i + span]

    base = pl.multiple_of(step * rows_per_step, rows_per_step)
    for i in range(rows_per_step):
        acc_re = None
        acc_im = None
        for s in range(segments):
            a = own_f32[pl.ds(base + i, 1), pl.ds(s * NFFT, NFFT)]
            b = shifted[i, pl.ds(base, LAGS), pl.ds(s * NFFT, NFFT)]
            terms = product_terms(a, b)
            if acc_re is None:
                acc_re, acc_im = terms
            else:
                acc_re = [x + y for x, y in zip(acc_re, terms[0])]
                acc_im = [x + y for x, y in zip(acc_im, terms[1])]
        store_row(out_ref, i, acc_re, acc_im, segments)


def cross_kernel_pieces(segments, rows, chunk, *refs):
    pieces = refs[:-5]
    out_hbm, own_f32, shifted, buffers, sems = refs[-5:]
    span = shifted.shape[1]
    extended = jnp.concatenate(
        [
            jnp.concatenate(
                [piece[s * NFFT : (s + 1) * NFFT, :].astype(jnp.float32).T for s in range(segments)],
                axis=1,
            )
            for piece in pieces
        ],
        axis=0,
    )
    own_f32[...] = extended[:rows]
    for i in range(chunk):
        shifted[i] = extended[i : i + span]
    slots, parts = buffers.shape[0], sems.shape[1]
    part = chunk // parts
    copies = []
    for m in range(rows // chunk):
        slot = m % slots
        if m >= slots:
            for copy in copies[m - slots]:
                copy.wait()
        base = m * chunk
        for i in range(chunk):
            acc_re = None
            acc_im = None
            for s in range(segments):
                a = own_f32[base + i : base + i + 1, s * NFFT : (s + 1) * NFFT]
                b = shifted[i, base : base + LAGS, s * NFFT : (s + 1) * NFFT]
                terms = product_terms(a, b)
                if acc_re is None:
                    acc_re, acc_im = terms
                else:
                    acc_re = [x + y for x, y in zip(acc_re, terms[0])]
                    acc_im = [x + y for x, y in zip(acc_im, terms[1])]
            store_row(buffers.at[slot], i, acc_re, acc_im, segments)
        group = []
        for p in range(parts):
            copy = pltpu.make_async_copy(
                buffers.at[slot, pl.ds(p * part, part)],
                out_hbm.at[pl.ds(base + p * part, part)],
                sems.at[slot, p],
            )
            copy.start()
            group.append(copy)
        copies.append(group)
    for group in copies[-slots:]:
        for copy in group:
            copy.wait()


def cross_spectra_pieces(pieces):
    width = pieces[0].shape[0]
    rows = sum(piece.shape[1] for piece in pieces) - LAGS
    segments = width // NFFT
    chunk = 8
    span = rows + LAGS - chunk
    return pl.pallas_call(
        functools.partial(cross_kernel_pieces, segments, rows, chunk),
        out_shape=jax.ShapeDtypeStruct((rows, LAGS, NFFT), jnp.bfloat16),
        in_specs=[pl.BlockSpec(memory_space=pltpu.VMEM)] * len(pieces),
        out_specs=pl.BlockSpec(memory_space=pl.ANY),
        scratch_shapes=[
            pltpu.VMEM((rows, width), jnp.float32),
            pltpu.VMEM((chunk, span, width), jnp.float32),
            pltpu.VMEM((4, chunk, LAGS, NFFT), jnp.bfloat16),
            pltpu.SemaphoreType.DMA((4, 4)),
        ],
        cost_estimate=pl.CostEstimate(
            flops=6 * rows * LAGS * NF * segments,
            transcendentals=0,
            bytes_accessed=rows * LAGS * NFFT * 2 + 2 * (rows + LAGS) * width,
        ),
    )(*pieces)


def split_three(values):
    high = values.astype(jnp.bfloat16)
    rest = values - high.astype(jnp.float32)
    middle = rest.astype(jnp.bfloat16)
    low = (rest - middle.astype(jnp.float32)).astype(jnp.bfloat16)
    return [high, middle, low]


def split_three_kept(values):
    high = lax.reduce_precision(values, exponent_bits=8, mantissa_bits=7)
    rest = values - high
    middle = lax.reduce_precision(rest, exponent_bits=8, mantissa_bits=7)
    low = rest - middle
    return [part.astype(jnp.bfloat16) for part in (high, middle, low)]


def exact_dot(parts, operand):
    total = None
    for part in parts:
        term = jnp.dot(part, operand, preferred_element_type=jnp.float32)
        total = term if total is None else total + term
    return total


def fused_kernel(rows, chunk, taps_ref, samples_ref, table_ref, out_hbm, own_f32, shifted,
                 buffers, sems):
    tap_count = taps_ref.shape[0]
    outputs = NFFT // 2
    length, channels = samples_ref.shape
    blocks = length // (2 * outputs)
    lanes = 3 * NF
    lane = lax.broadcasted_iota(jnp.int32, (1, lanes), 1)
    row = jnp.zeros((1, lanes), jnp.float32)
    for k in range(tap_count):
        row = jnp.where(lane == tap_count - 1 - k, taps_ref[k], row)
    matrices = []
    for part in split_three(row):
        rolled = pltpu.roll(
            jnp.broadcast_to(part.astype(jnp.float32), (outputs, lanes)), 0, 1, stride=2, stride_axis=0
        )
        matrices.append(rolled[:, : 2 * outputs + tap_count].astype(jnp.bfloat16))
    x = samples_ref[...]
    joined = jnp.concatenate(
        [
            jnp.zeros((tap_count, channels), x.dtype),
            x,
            jnp.zeros((2 * outputs - tap_count, channels), x.dtype),
        ],
        axis=0,
    )
    filtered = jnp.concatenate(
        [
            exact_dot(matrices, joined[b * 2 * outputs : b * 2 * outputs + 2 * outputs + tap_count])
            for b in range(blocks)
        ],
        axis=0,
    )
    filtered = filtered.astype(jnp.bfloat16)
    spectrum = exact_dot([table_ref[p] for p in range(table_ref.shape[0])], filtered)
    real_part = spectrum[:NF]
    imag_part = spectrum[NF:]
    powers = real_part * real_part + imag_part * imag_part
    mean_power = jnp.mean(powers, axis=0, keepdims=True)
    whitening = 1.0 / jnp.sqrt(powers + mean_power + 1e-06)
    whitened = jnp.concatenate([real_part * whitening, imag_part * whitening], axis=0)
    extended = whitened.astype(jnp.bfloat16).astype(jnp.float32).T
    span = shifted.shape[1]
    own_f32[...] = extended[:rows]
    for i in range(chunk):
        shifted[i] = extended[i : i + span]
    slots, parts = buffers.shape[0], sems.shape[1]
    part = chunk // parts
    copies = []
    for m in range(rows // chunk):
        slot = m % slots
        if m >= slots:
            for copy in copies[m - slots]:
                copy.wait()
        base = m * chunk
        for i in range(chunk):
            a = own_f32[base + i : base + i + 1, :]
            b = shifted[i, base : base + LAGS, :]
            acc_re, acc_im = product_terms(a, b)
            store_row(buffers.at[slot], i, acc_re, acc_im, 1)
        group = []
        for p in range(parts):
            copy = pltpu.make_async_copy(
                buffers.at[slot, pl.ds(p * part, part)],
                out_hbm.at[pl.ds(base + p * part, part)],
                sems.at[slot, p],
            )
            copy.start()
            group.append(copy)
        copies.append(group)
    for group in copies[-slots:]:
        for copy in group:
            copy.wait()


def fused_spectra(samples, filter_taps, table_t, rows):
    length, channels = samples.shape
    chunk = 8
    span = channels - chunk
    return pl.pallas_call(
        functools.partial(fused_kernel, rows, chunk),
        out_shape=jax.ShapeDtypeStruct((rows, LAGS, NFFT), jnp.bfloat16),
        in_specs=[pl.BlockSpec(memory_space=pltpu.SMEM)] + [pl.BlockSpec(memory_space=pltpu.VMEM)] * 2,
        out_specs=pl.BlockSpec(memory_space=pl.ANY),
        scratch_shapes=[
            pltpu.VMEM((rows, NFFT), jnp.float32),
            pltpu.VMEM((chunk, span, NFFT), jnp.float32),
            pltpu.VMEM((4, chunk, LAGS, NFFT), jnp.bfloat16),
            pltpu.SemaphoreType.DMA((4, 4)),
        ],
        cost_estimate=pl.CostEstimate(
            flops=6 * rows * LAGS * NF + 12 * channels * (NF * 320 * length // 256 + NFFT * NFFT),
            transcendentals=2 * NF * channels,
            bytes_accessed=rows * LAGS * NFFT * 2 + 2 * samples.size + 2 * table_t.size,
        ),
    )(filter_taps, samples, table_t)


def cross_spectra(own, extended):
    rows, segments, columns = own.shape
    reach_rows = extended.shape[0]
    own_flat = own.reshape(rows, segments * columns)
    ext_flat = extended.reshape(reach_rows, segments * columns)
    rows_per_step = 8
    span = reach_rows - rows_per_step
    scratch_bytes = rows_per_step * span * segments * columns * 4
    cost = pl.CostEstimate(
        flops=6 * rows * LAGS * NF * segments,
        transcendentals=0,
        bytes_accessed=rows * LAGS * columns * 2 + 2 * segments * (rows + reach_rows) * columns,
    )
    common = dict(
        out_shape=jax.ShapeDtypeStruct((rows, LAGS, columns), jnp.bfloat16),
        grid=(rows // rows_per_step,),
        in_specs=[
            pl.BlockSpec((rows, segments * columns), lambda i: (0, 0)),
            pl.BlockSpec((reach_rows, segments * columns), lambda i: (0, 0)),
        ],
        out_specs=pl.BlockSpec((rows_per_step, LAGS, columns), lambda i: (i, 0, 0)),
        cost_estimate=cost,
    )
    if scratch_bytes <= 8 * 1024 * 1024:
        return pl.pallas_call(
            functools.partial(cross_kernel_shifted, segments, rows_per_step),
            scratch_shapes=[
                pltpu.VMEM((rows, segments * columns), jnp.float32),
                pltpu.VMEM((rows_per_step, span, segments * columns), jnp.float32),
            ],
            compiler_params=pltpu.CompilerParams(dimension_semantics=("arbitrary",)),
            **common,
        )(own_flat, ext_flat)
    return pl.pallas_call(
        functools.partial(cross_kernel, segments, rows_per_step), **common
    )(own_flat, ext_flat)


def body(strain, filter_taps):
    extent = lax.axis_size("ta")
    columns_n = lax.axis_size("col")
    section_rows, slab = strain.shape
    block_rows = section_rows // extent
    reach = LAGS // block_rows
    turned = strain.T
    route = [(c + 1, c) for c in range(columns_n - 1)]
    following = lax.ppermute(turned, "col", route)
    tail = following[:, : reach * block_rows]
    width = (reach + 1) * block_rows
    windows = channel_windows(turned, tail, extent, width, reach * block_rows)
    gathered = lax.all_to_all(windows, "ta", split_axis=0, concat_axis=0, tiled=True)
    samples = gathered.reshape(extent * slab, width)
    if extent * slab == 2 * NFFT:
        table_parts = jnp.stack(split_three_kept(fourier_table_t()))
        return fused_spectra(samples, filter_taps, table_parts, block_rows)[None]
    filtered = decimate_t(samples.astype(jnp.float32), filter_taps)
    whitened_t = whiten_t(filtered)
    segments, columns, _ = whitened_t.shape
    if segments * 8 * width * columns * 4 <= 8 * 1024 * 1024:
        flat = whitened_t.reshape(segments * columns, width)
        return cross_spectra_pieces([flat])[None]
    extended = whitened_t.transpose(2, 0, 1)
    return cross_spectra(extended[:block_rows], extended)[None]


def solution(mesh):
    return jax.shard_map(
        body,
        mesh=mesh,
        in_specs=(P("col", "ta"), P()),
        out_specs=P("col", "ta", None, None),
        check_vma=False,
    )
```

```python
import functools

import jax
import jax.numpy as jnp
from jax import lax
from jax.experimental import pallas as pl
from jax.experimental.pallas import tpu as pltpu
from jax.sharding import PartitionSpec as P

NFFT = 256
NF = 128
LAGS = 128


def tap_rows(filter_taps, outputs):
    tap_count = filter_taps.shape[0]
    window = 2 * outputs + tap_count
    flipped = filter_taps[::-1]
    period = jnp.concatenate([flipped, jnp.zeros((window + 2 - tap_count,), jnp.float32)])
    repeated = jnp.tile(period, outputs)[: outputs * window]
    return repeated.reshape(outputs, window)


def decimate_t(samples, filter_taps):
    length, channels = samples.shape
    tap_count = filter_taps.shape[0]
    outputs = min(length, NFFT) // 2
    blocks = length // (2 * outputs)
    joined = jnp.concatenate(
        [
            jnp.zeros((tap_count, channels), jnp.float32),
            samples,
            jnp.zeros((2 * outputs - tap_count, channels), jnp.float32),
        ],
        axis=0,
    )
    joined = joined.reshape(blocks + 1, 2 * outputs, channels)
    windows = jnp.concatenate([joined[:-1], joined[1:, :tap_count]], axis=1)
    matrix = tap_rows(filter_taps, outputs)
    result = jnp.einsum("tw,bwc->btc", matrix, windows, precision=lax.Precision.HIGHEST)
    return result.reshape(blocks * outputs, channels).astype(jnp.bfloat16)


def fourier_table():
    moment = lax.broadcasted_iota(jnp.int32, (NFFT, NF), 0)
    frequency = lax.broadcasted_iota(jnp.int32, (NFFT, NF), 1) + 1
    phase_index = moment * frequency % NFFT
    angles = phase_index.astype(jnp.float32) * (2.0 * jnp.pi / NFFT)
    window_taper = 0.5 - 0.5 * jnp.cos(moment.astype(jnp.float32) * (2.0 * jnp.pi / NFFT))
    return jnp.concatenate(
        [window_taper * jnp.cos(angles), -window_taper * jnp.sin(angles)], axis=1
    )


def fourier_table_t():
    moment = lax.broadcasted_iota(jnp.int32, (NFFT, NFFT), 1)
    frequency = lax.broadcasted_iota(jnp.int32, (NFFT, NFFT), 0) % NF + 1
    phase_index = moment * frequency % NFFT
    angles = phase_index.astype(jnp.float32) * (2.0 * jnp.pi / NFFT)
    window_taper = 0.5 - 0.5 * jnp.cos(moment.astype(jnp.float32) * (2.0 * jnp.pi / NFFT))
    real_rows = lax.broadcasted_iota(jnp.int32, (NFFT, NFFT), 0) < NF
    return jnp.where(real_rows, window_taper * jnp.cos(angles), -window_taper * jnp.sin(angles))


def whiten_t(filtered):
    length, channels = filtered.shape
    pieces = filtered.reshape(length // NF, NF, channels)
    segment_rows = jnp.concatenate([pieces[:-1], pieces[1:]], axis=1)
    spectrum = jnp.einsum(
        "nf,snc->sfc",
        fourier_table(),
        segment_rows.astype(jnp.float32),
        precision=lax.Precision.HIGHEST,
    )
    real_part = spectrum[:, :NF]
    imag_part = spectrum[:, NF:]
    powers = real_part * real_part + imag_part * imag_part
    mean_power = jnp.mean(powers, axis=1, keepdims=True)
    whitening = 1.0 / jnp.sqrt(powers + mean_power + 1e-06)
    return jnp.concatenate([real_part * whitening, imag_part * whitening], axis=1).astype(
        jnp.bfloat16
    )


def windows_kernel(width, tail_rows, x_ref, out_ref):
    x = x_ref[...].astype(jnp.float32)
    padded = jnp.concatenate([x, jnp.zeros((x.shape[0], tail_rows), jnp.float32)], axis=1)
    step = (padded.shape[1] - width) // (out_ref.shape[0] - 1)
    for j in range(out_ref.shape[0]):
        out_ref[j] = padded[:, j * step : j * step + width].astype(out_ref.dtype)


def channel_windows(turned, tail, extent, width, tail_rows):
    slab, rows = turned.shape
    windows = pl.pallas_call(
        functools.partial(windows_kernel, width, tail_rows),
        out_shape=jax.ShapeDtypeStruct((extent, slab, width), turned.dtype),
        cost_estimate=pl.CostEstimate(
            flops=0, transcendentals=0, bytes_accessed=2 * (slab * rows + extent * slab * width)
        ),
    )(turned)
    step = (rows + tail_rows - width) // (extent - 1)
    count = -(-tail_rows // step)
    first = extent - count
    padded = jnp.concatenate([turned[:, first * step :], tail], axis=1)
    patch = jnp.stack([padded[:, j * step : j * step + width] for j in range(count)])
    return lax.dynamic_update_slice(windows, patch, (first, 0, 0))


def cross_kernel(segments, rows_per_step, own_ref, ext_ref, out_ref):
    step = pl.program_id(0)
    base = pl.multiple_of(step * rows_per_step, rows_per_step)
    for i in range(rows_per_step):
        acc_re = None
        acc_im = None
        for s in range(segments):
            a = own_ref[pl.ds(base, rows_per_step), pl.ds(s * NFFT, NFFT)]
            a = a.astype(jnp.float32)[i : i + 1]
            window = ext_ref[pl.ds(base, LAGS + rows_per_step), pl.ds(s * NFFT, NFFT)]
            b = window.astype(jnp.float32)[i : i + LAGS]
            terms = product_terms(a, b)
            if acc_re is None:
                acc_re, acc_im = terms
            else:
                acc_re = [x + y for x, y in zip(acc_re, terms[0])]
                acc_im = [x + y for x, y in zip(acc_im, terms[1])]
        store_row(out_ref, i, acc_re, acc_im, segments)


def product_terms(a, b):
    ar = a[:, :NF]
    ai = a[:, NF:]
    br = b[:, :NF]
    bi = b[:, NF:]
    return [ar * br, ai * bi], [ai * br, ar * bi]


def store_row(out_ref, i, acc_re, acc_im, segments):
    re = acc_re[0] + acc_re[1]
    im = acc_im[0] - acc_im[1]
    if segments > 1:
        re = re / segments
        im = im / segments
    out_ref[i, :, :NF] = re.astype(out_ref.dtype)
    out_ref[i, :, NF:] = im.astype(out_ref.dtype)


def cross_kernel_shifted(segments, rows_per_step, own_ref, ext_ref, out_ref, own_f32, shifted):
    step = pl.program_id(0)
    span = shifted.shape[1]

    @pl.when(step == 0)
    def _():
        own_f32[...] = own_ref[...].astype(jnp.float32)
        whole = ext_ref[...].astype(jnp.float32)
        for i in range(rows_per_step):
            shifted[i] = whole[i : i + span]

    base = pl.multiple_of(step * rows_per_step, rows_per_step)
    for i in range(rows_per_step):
        acc_re = None
        acc_im = None
        for s in range(segments):
            a = own_f32[pl.ds(base + i, 1), pl.ds(s * NFFT, NFFT)]
            b = shifted[i, pl.ds(base, LAGS), pl.ds(s * NFFT, NFFT)]
            terms = product_terms(a, b)
            if acc_re is None:
                acc_re, acc_im = terms
            else:
                acc_re = [x + y for x, y in zip(acc_re, terms[0])]
                acc_im = [x + y for x, y in zip(acc_im, terms[1])]
        store_row(out_ref, i, acc_re, acc_im, segments)


def cross_kernel_pieces(segments, rows, chunk, *refs):
    pieces = refs[:-5]
    out_hbm, own_f32, shifted, buffers, sems = refs[-5:]
    span = shifted.shape[1]
    extended = jnp.concatenate(
        [
            jnp.concatenate(
                [piece[s * NFFT : (s + 1) * NFFT, :].astype(jnp.float32).T for s in range(segments)],
                axis=1,
            )
            for piece in pieces
        ],
        axis=0,
    )
    own_f32[...] = extended[:rows]
    for i in range(chunk):
        shifted[i] = extended[i : i + span]
    slots, parts = buffers.shape[0], sems.shape[1]
    part = chunk // parts
    copies = []
    for m in range(rows // chunk):
        slot = m % slots
        if m >= slots:
            for copy in copies[m - slots]:
                copy.wait()
        base = m * chunk
        for i in range(chunk):
            acc_re = None
            acc_im = None
            for s in range(segments):
                a = own_f32[base + i : base + i + 1, s * NFFT : (s + 1) * NFFT]
                b = shifted[i, base : base + LAGS, s * NFFT : (s + 1) * NFFT]
                terms = product_terms(a, b)
                if acc_re is None:
                    acc_re, acc_im = terms
                else:
                    acc_re = [x + y for x, y in zip(acc_re, terms[0])]
                    acc_im = [x + y for x, y in zip(acc_im, terms[1])]
            store_row(buffers.at[slot], i, acc_re, acc_im, segments)
        group = []
        for p in range(parts):
            copy = pltpu.make_async_copy(
                buffers.at[slot, pl.ds(p * part, part)],
                out_hbm.at[pl.ds(base + p * part, part)],
                sems.at[slot, p],
            )
            copy.start()
            group.append(copy)
        copies.append(group)
    for group in copies[-slots:]:
        for copy in group:
            copy.wait()


def cross_spectra_pieces(pieces):
    width = pieces[0].shape[0]
    rows = sum(piece.shape[1] for piece in pieces) - LAGS
    segments = width // NFFT
    chunk = 8
    span = rows + LAGS - chunk
    return pl.pallas_call(
        functools.partial(cross_kernel_pieces, segments, rows, chunk),
        out_shape=jax.ShapeDtypeStruct((rows, LAGS, NFFT), jnp.bfloat16),
        in_specs=[pl.BlockSpec(memory_space=pltpu.VMEM)] * len(pieces),
        out_specs=pl.BlockSpec(memory_space=pl.ANY),
        scratch_shapes=[
            pltpu.VMEM((rows, width), jnp.float32),
            pltpu.VMEM((chunk, span, width), jnp.float32),
            pltpu.VMEM((4, chunk, LAGS, NFFT), jnp.bfloat16),
            pltpu.SemaphoreType.DMA((4, 4)),
        ],
        cost_estimate=pl.CostEstimate(
            flops=6 * rows * LAGS * NF * segments,
            transcendentals=0,
            bytes_accessed=rows * LAGS * NFFT * 2 + 2 * (rows + LAGS) * width,
        ),
    )(*pieces)


def split_three(values):
    high = values.astype(jnp.bfloat16)
    rest = values - high.astype(jnp.float32)
    middle = rest.astype(jnp.bfloat16)
    low = (rest - middle.astype(jnp.float32)).astype(jnp.bfloat16)
    return [high, middle, low]


def split_three_kept(values):
    high = lax.reduce_precision(values, exponent_bits=8, mantissa_bits=7)
    rest = values - high
    middle = lax.reduce_precision(rest, exponent_bits=8, mantissa_bits=7)
    low = rest - middle
    return [part.astype(jnp.bfloat16) for part in (high, middle, low)]


def exact_dot(parts, operand):
    total = None
    for part in parts:
        term = jnp.dot(part, operand, preferred_element_type=jnp.float32)
        total = term if total is None else total + term
    return total


def fused_kernel(rows, chunk, taps_ref, samples_hbm, table_hbm, out_hbm, own_f32, shifted,
                 buffers, sems, samples_ref, table_ref, in_sems):
    fetch_samples = pltpu.make_async_copy(samples_hbm, samples_ref, in_sems.at[0])
    fetch_table = pltpu.make_async_copy(table_hbm, table_ref, in_sems.at[1])
    fetch_samples.start()
    fetch_table.start()
    tap_count = taps_ref.shape[0]
    outputs = NFFT // 2
    length, channels = samples_ref.shape
    blocks = length // (2 * outputs)
    lanes = 3 * NF
    lane = lax.broadcasted_iota(jnp.int32, (1, lanes), 1)
    row = jnp.zeros((1, lanes), jnp.float32)
    for k in range(tap_count):
        row = jnp.where(lane == tap_count - 1 - k, taps_ref[k], row)
    matrices = []
    for part in split_three(row):
        rolled = pltpu.roll(
            jnp.broadcast_to(part.astype(jnp.float32), (outputs, lanes)), 0, 1, stride=2, stride_axis=0
        )
        matrices.append(rolled[:, : 2 * outputs + tap_count].astype(jnp.bfloat16))
    fetch_samples.wait()
    x = samples_ref[...]
    joined = jnp.concatenate(
        [
            jnp.zeros((tap_count, channels), x.dtype),
            x,
            jnp.zeros((2 * outputs - tap_count, channels), x.dtype),
        ],
        axis=0,
    )
    filtered = jnp.concatenate(
        [
            exact_dot(matrices, joined[b * 2 * outputs : b * 2 * outputs + 2 * outputs + tap_count])
            for b in range(blocks)
        ],
        axis=0,
    )
    filtered = filtered.astype(jnp.bfloat16)
    fetch_table.wait()
    spectrum = exact_dot([table_ref[p] for p in range(table_ref.shape[0])], filtered)
    real_part = spectrum[:NF]
    imag_part = spectrum[NF:]
    powers = real_part * real_part + imag_part * imag_part
    mean_power = jnp.mean(powers, axis=0, keepdims=True)
    whitening = 1.0 / jnp.sqrt(powers + mean_power + 1e-06)
    whitened = jnp.concatenate([real_part * whitening, imag_part * whitening], axis=0)
    extended = whitened.astype(jnp.bfloat16).astype(jnp.float32).T
    span = shifted.shape[1]
    own_f32[...] = extended[:rows]
    for i in range(chunk):
        shifted[i] = extended[i : i + span]
    slots, parts = buffers.shape[0], sems.shape[1]
    part = chunk // parts
    copies = []
    for m in range(rows // chunk):
        slot = m % slots
        if m >= slots:
            for copy in copies[m - slots]:
                copy.wait()
        base = m * chunk
        for i in range(chunk):
            a = own_f32[base + i : base + i + 1, :]
            b = shifted[i, base : base + LAGS, :]
            acc_re, acc_im = product_terms(a, b)
            store_row(buffers.at[slot], i, acc_re, acc_im, 1)
        group = []
        for p in range(parts):
            copy = pltpu.make_async_copy(
                buffers.at[slot, pl.ds(p * part, part)],
                out_hbm.at[pl.ds(base + p * part, part)],
                sems.at[slot, p],
            )
            copy.start()
            group.append(copy)
        copies.append(group)
    for group in copies[-slots:]:
        for copy in group:
            copy.wait()


def fused_spectra(samples, filter_taps, table_t, rows):
    length, channels = samples.shape
    chunk = 8
    span = channels - chunk
    return pl.pallas_call(
        functools.partial(fused_kernel, rows, chunk),
        out_shape=jax.ShapeDtypeStruct((rows, LAGS, NFFT), jnp.bfloat16),
        in_specs=[pl.BlockSpec(memory_space=pltpu.SMEM)] + [pl.BlockSpec(memory_space=pl.ANY)] * 2,
        out_specs=pl.BlockSpec(memory_space=pl.ANY),
        scratch_shapes=[
            pltpu.VMEM((rows, NFFT), jnp.float32),
            pltpu.VMEM((chunk, span, NFFT), jnp.float32),
            pltpu.VMEM((4, chunk, LAGS, NFFT), jnp.bfloat16),
            pltpu.SemaphoreType.DMA((4, 4)),
            pltpu.VMEM(samples.shape, samples.dtype),
            pltpu.VMEM(table_t.shape, table_t.dtype),
            pltpu.SemaphoreType.DMA((2,)),
        ],
        cost_estimate=pl.CostEstimate(
            flops=6 * rows * LAGS * NF + 12 * channels * (NF * 320 * length // 256 + NFFT * NFFT),
            transcendentals=2 * NF * channels,
            bytes_accessed=rows * LAGS * NFFT * 2 + 2 * samples.size + 2 * table_t.size,
        ),
    )(filter_taps, samples, table_t)


def cross_spectra(own, extended):
    rows, segments, columns = own.shape
    reach_rows = extended.shape[0]
    own_flat = own.reshape(rows, segments * columns)
    ext_flat = extended.reshape(reach_rows, segments * columns)
    rows_per_step = 8
    span = reach_rows - rows_per_step
    scratch_bytes = rows_per_step * span * segments * columns * 4
    cost = pl.CostEstimate(
        flops=6 * rows * LAGS * NF * segments,
        transcendentals=0,
        bytes_accessed=rows * LAGS * columns * 2 + 2 * segments * (rows + reach_rows) * columns,
    )
    common = dict(
        out_shape=jax.ShapeDtypeStruct((rows, LAGS, columns), jnp.bfloat16),
        grid=(rows // rows_per_step,),
        in_specs=[
            pl.BlockSpec((rows, segments * columns), lambda i: (0, 0)),
            pl.BlockSpec((reach_rows, segments * columns), lambda i: (0, 0)),
        ],
        out_specs=pl.BlockSpec((rows_per_step, LAGS, columns), lambda i: (i, 0, 0)),
        cost_estimate=cost,
    )
    if scratch_bytes <= 8 * 1024 * 1024:
        return pl.pallas_call(
            functools.partial(cross_kernel_shifted, segments, rows_per_step),
            scratch_shapes=[
                pltpu.VMEM((rows, segments * columns), jnp.float32),
                pltpu.VMEM((rows_per_step, span, segments * columns), jnp.float32),
            ],
            compiler_params=pltpu.CompilerParams(dimension_semantics=("arbitrary",)),
            **common,
        )(own_flat, ext_flat)
    return pl.pallas_call(
        functools.partial(cross_kernel, segments, rows_per_step), **common
    )(own_flat, ext_flat)


def body(strain, filter_taps):
    extent = lax.axis_size("ta")
    columns_n = lax.axis_size("col")
    section_rows, slab = strain.shape
    block_rows = section_rows // extent
    reach = LAGS // block_rows
    turned = strain.T
    route = [(c + 1, c) for c in range(columns_n - 1)]
    following = lax.ppermute(turned, "col", route)
    tail = following[:, : reach * block_rows]
    width = (reach + 1) * block_rows
    windows = channel_windows(turned, tail, extent, width, reach * block_rows)
    gathered = lax.all_to_all(windows, "ta", split_axis=0, concat_axis=0, tiled=True)
    samples = gathered.reshape(extent * slab, width)
    if extent * slab == 2 * NFFT:
        table_parts = jnp.stack(split_three_kept(fourier_table_t()))
        return fused_spectra(samples, filter_taps, table_parts, block_rows)[None]
    filtered = decimate_t(samples.astype(jnp.float32), filter_taps)
    whitened_t = whiten_t(filtered)
    segments, columns, _ = whitened_t.shape
    if segments * 8 * width * columns * 4 <= 8 * 1024 * 1024:
        flat = whitened_t.reshape(segments * columns, width)
        return cross_spectra_pieces([flat])[None]
    extended = whitened_t.transpose(2, 0, 1)
    return cross_spectra(extended[:block_rows], extended)[None]


def solution(mesh):
    return jax.shard_map(
        body,
        mesh=mesh,
        in_specs=(P("col", "ta"), P()),
        out_specs=P("col", "ta", None, None),
        check_vma=False,
    )
```

```python
import functools

import jax
import jax.numpy as jnp
from jax import lax
from jax.experimental import pallas as pl
from jax.experimental.pallas import tpu as pltpu
from jax.sharding import PartitionSpec as P

NFFT = 256
NF = 128
LAGS = 128


def tap_rows(filter_taps, outputs):
    tap_count = filter_taps.shape[0]
    window = 2 * outputs + tap_count
    flipped = filter_taps[::-1]
    period = jnp.concatenate([flipped, jnp.zeros((window + 2 - tap_count,), jnp.float32)])
    repeated = jnp.tile(period, outputs)[: outputs * window]
    return repeated.reshape(outputs, window)


def decimate_t(samples, filter_taps):
    length, channels = samples.shape
    tap_count = filter_taps.shape[0]
    outputs = min(length, NFFT) // 2
    blocks = length // (2 * outputs)
    joined = jnp.concatenate(
        [
            jnp.zeros((tap_count, channels), jnp.float32),
            samples,
            jnp.zeros((2 * outputs - tap_count, channels), jnp.float32),
        ],
        axis=0,
    )
    joined = joined.reshape(blocks + 1, 2 * outputs, channels)
    windows = jnp.concatenate([joined[:-1], joined[1:, :tap_count]], axis=1)
    matrix = tap_rows(filter_taps, outputs)
    result = jnp.einsum("tw,bwc->btc", matrix, windows, precision=lax.Precision.HIGHEST)
    return result.reshape(blocks * outputs, channels).astype(jnp.bfloat16)


def fourier_table():
    moment = lax.broadcasted_iota(jnp.int32, (NFFT, NF), 0)
    frequency = lax.broadcasted_iota(jnp.int32, (NFFT, NF), 1) + 1
    phase_index = moment * frequency % NFFT
    angles = phase_index.astype(jnp.float32) * (2.0 * jnp.pi / NFFT)
    window_taper = 0.5 - 0.5 * jnp.cos(moment.astype(jnp.float32) * (2.0 * jnp.pi / NFFT))
    return jnp.concatenate(
        [window_taper * jnp.cos(angles), -window_taper * jnp.sin(angles)], axis=1
    )


def fourier_table_t():
    moment = lax.broadcasted_iota(jnp.int32, (NFFT, NFFT), 1)
    frequency = lax.broadcasted_iota(jnp.int32, (NFFT, NFFT), 0) % NF + 1
    phase_index = moment * frequency % NFFT
    angles = phase_index.astype(jnp.float32) * (2.0 * jnp.pi / NFFT)
    window_taper = 0.5 - 0.5 * jnp.cos(moment.astype(jnp.float32) * (2.0 * jnp.pi / NFFT))
    real_rows = lax.broadcasted_iota(jnp.int32, (NFFT, NFFT), 0) < NF
    return jnp.where(real_rows, window_taper * jnp.cos(angles), -window_taper * jnp.sin(angles))


def whiten_t(filtered):
    length, channels = filtered.shape
    pieces = filtered.reshape(length // NF, NF, channels)
    segment_rows = jnp.concatenate([pieces[:-1], pieces[1:]], axis=1)
    spectrum = jnp.einsum(
        "nf,snc->sfc",
        fourier_table(),
        segment_rows.astype(jnp.float32),
        precision=lax.Precision.HIGHEST,
    )
    real_part = spectrum[:, :NF]
    imag_part = spectrum[:, NF:]
    powers = real_part * real_part + imag_part * imag_part
    mean_power = jnp.mean(powers, axis=1, keepdims=True)
    whitening = 1.0 / jnp.sqrt(powers + mean_power + 1e-06)
    return jnp.concatenate([real_part * whitening, imag_part * whitening], axis=1).astype(
        jnp.bfloat16
    )


def windows_kernel(width, tail_rows, x_ref, out_ref):
    x = x_ref[...].astype(jnp.float32)
    padded = jnp.concatenate([x, jnp.zeros((x.shape[0], tail_rows), jnp.float32)], axis=1)
    step = (padded.shape[1] - width) // (out_ref.shape[0] - 1)
    for j in range(out_ref.shape[0]):
        out_ref[j] = padded[:, j * step : j * step + width].astype(out_ref.dtype)


def channel_windows(turned, tail, extent, width, tail_rows):
    slab, rows = turned.shape
    windows = pl.pallas_call(
        functools.partial(windows_kernel, width, tail_rows),
        out_shape=jax.ShapeDtypeStruct((extent, slab, width), turned.dtype),
        cost_estimate=pl.CostEstimate(
            flops=0, transcendentals=0, bytes_accessed=2 * (slab * rows + extent * slab * width)
        ),
    )(turned)
    step = (rows + tail_rows - width) // (extent - 1)
    count = -(-tail_rows // step)
    first = extent - count
    padded = jnp.concatenate([turned[:, first * step :], tail], axis=1)
    patch = jnp.stack([padded[:, j * step : j * step + width] for j in range(count)])
    return lax.dynamic_update_slice(windows, patch, (first, 0, 0))


def cross_kernel(segments, rows_per_step, own_ref, ext_ref, out_ref):
    step = pl.program_id(0)
    base = pl.multiple_of(step * rows_per_step, rows_per_step)
    for i in range(rows_per_step):
        acc_re = None
        acc_im = None
        for s in range(segments):
            a = own_ref[pl.ds(base, rows_per_step), pl.ds(s * NFFT, NFFT)]
            a = a.astype(jnp.float32)[i : i + 1]
            window = ext_ref[pl.ds(base, LAGS + rows_per_step), pl.ds(s * NFFT, NFFT)]
            b = window.astype(jnp.float32)[i : i + LAGS]
            terms = product_terms(a, b)
            if acc_re is None:
                acc_re, acc_im = terms
            else:
                acc_re = [x + y for x, y in zip(acc_re, terms[0])]
                acc_im = [x + y for x, y in zip(acc_im, terms[1])]
        store_row(out_ref, i, acc_re, acc_im, segments)


def product_terms(a, b):
    ar = a[:, :NF]
    ai = a[:, NF:]
    br = b[:, :NF]
    bi = b[:, NF:]
    return [ar * br, ai * bi], [ai * br, ar * bi]


def store_row(out_ref, i, acc_re, acc_im, segments):
    re = acc_re[0] + acc_re[1]
    im = acc_im[0] - acc_im[1]
    if segments > 1:
        re = re / segments
        im = im / segments
    out_ref[i, :, :NF] = re.astype(out_ref.dtype)
    out_ref[i, :, NF:] = im.astype(out_ref.dtype)


def cross_kernel_shifted(segments, rows_per_step, own_ref, ext_ref, out_ref, own_f32, shifted):
    step = pl.program_id(0)
    span = shifted.shape[1]

    @pl.when(step == 0)
    def _():
        own_f32[...] = own_ref[...].astype(jnp.float32)
        whole = ext_ref[...].astype(jnp.float32)
        for i in range(rows_per_step):
            shifted[i] = whole[i : i + span]

    base = pl.multiple_of(step * rows_per_step, rows_per_step)
    for i in range(rows_per_step):
        acc_re = None
        acc_im = None
        for s in range(segments):
            a = own_f32[pl.ds(base + i, 1), pl.ds(s * NFFT, NFFT)]
            b = shifted[i, pl.ds(base, LAGS), pl.ds(s * NFFT, NFFT)]
            terms = product_terms(a, b)
            if acc_re is None:
                acc_re, acc_im = terms
            else:
                acc_re = [x + y for x, y in zip(acc_re, terms[0])]
                acc_im = [x + y for x, y in zip(acc_im, terms[1])]
        store_row(out_ref, i, acc_re, acc_im, segments)


def cross_kernel_pieces(segments, rows, chunk, *refs):
    pieces = refs[:-5]
    out_hbm, own_f32, shifted, buffers, sems = refs[-5:]
    span = shifted.shape[1]
    extended = jnp.concatenate(
        [
            jnp.concatenate(
                [piece[s * NFFT : (s + 1) * NFFT, :].astype(jnp.float32).T for s in range(segments)],
                axis=1,
            )
            for piece in pieces
        ],
        axis=0,
    )
    own_f32[...] = extended[:rows]
    for i in range(chunk):
        shifted[i] = extended[i : i + span]
    slots, parts = buffers.shape[0], sems.shape[1]
    part = chunk // parts
    copies = []
    for m in range(rows // chunk):
        slot = m % slots
        if m >= slots:
            for copy in copies[m - slots]:
                copy.wait()
        base = m * chunk
        for i in range(chunk):
            acc_re = None
            acc_im = None
            for s in range(segments):
                a = own_f32[base + i : base + i + 1, s * NFFT : (s + 1) * NFFT]
                b = shifted[i, base : base + LAGS, s * NFFT : (s + 1) * NFFT]
                terms = product_terms(a, b)
                if acc_re is None:
                    acc_re, acc_im = terms
                else:
                    acc_re = [x + y for x, y in zip(acc_re, terms[0])]
                    acc_im = [x + y for x, y in zip(acc_im, terms[1])]
            store_row(buffers.at[slot], i, acc_re, acc_im, segments)
        group = []
        for p in range(parts):
            copy = pltpu.make_async_copy(
                buffers.at[slot, pl.ds(p * part, part)],
                out_hbm.at[pl.ds(base + p * part, part)],
                sems.at[slot, p],
            )
            copy.start()
            group.append(copy)
        copies.append(group)
    for group in copies[-slots:]:
        for copy in group:
            copy.wait()


def cross_spectra_pieces(pieces):
    width = pieces[0].shape[0]
    rows = sum(piece.shape[1] for piece in pieces) - LAGS
    segments = width // NFFT
    chunk = 8
    span = rows + LAGS - chunk
    return pl.pallas_call(
        functools.partial(cross_kernel_pieces, segments, rows, chunk),
        out_shape=jax.ShapeDtypeStruct((rows, LAGS, NFFT), jnp.bfloat16),
        in_specs=[pl.BlockSpec(memory_space=pltpu.VMEM)] * len(pieces),
        out_specs=pl.BlockSpec(memory_space=pl.ANY),
        scratch_shapes=[
            pltpu.VMEM((rows, width), jnp.float32),
            pltpu.VMEM((chunk, span, width), jnp.float32),
            pltpu.VMEM((4, chunk, LAGS, NFFT), jnp.bfloat16),
            pltpu.SemaphoreType.DMA((4, 4)),
        ],
        cost_estimate=pl.CostEstimate(
            flops=6 * rows * LAGS * NF * segments,
            transcendentals=0,
            bytes_accessed=rows * LAGS * NFFT * 2 + 2 * (rows + LAGS) * width,
        ),
    )(*pieces)


def split_three(values):
    high = values.astype(jnp.bfloat16)
    rest = values - high.astype(jnp.float32)
    middle = rest.astype(jnp.bfloat16)
    low = (rest - middle.astype(jnp.float32)).astype(jnp.bfloat16)
    return [high, middle, low]


def split_three_kept(values):
    high = lax.reduce_precision(values, exponent_bits=8, mantissa_bits=7)
    rest = values - high
    middle = lax.reduce_precision(rest, exponent_bits=8, mantissa_bits=7)
    low = rest - middle
    return [part.astype(jnp.bfloat16) for part in (high, middle, low)]


def exact_dot(parts, operand):
    total = None
    for part in parts:
        term = jnp.dot(part, operand, preferred_element_type=jnp.float32)
        total = term if total is None else total + term
    return total


def fused_kernel(rows, chunk, taps_ref, samples_ref, table_ref, out_hbm, own_f32, shifted,
                 buffers, sems):
    tap_count = taps_ref.shape[0]
    outputs = NFFT // 2
    length, channels = samples_ref.shape
    blocks = length // (2 * outputs)
    lanes = 3 * NF
    lane = lax.broadcasted_iota(jnp.int32, (1, lanes), 1)
    row = jnp.zeros((1, lanes), jnp.float32)
    for k in range(tap_count):
        row = jnp.where(lane == tap_count - 1 - k, taps_ref[k], row)
    matrices = []
    for part in split_three(row):
        rolled = pltpu.roll(
            jnp.broadcast_to(part.astype(jnp.float32), (outputs, lanes)), 0, 1, stride=2, stride_axis=0
        )
        matrices.append(rolled[:, : 2 * outputs + tap_count].astype(jnp.bfloat16))
    x = samples_ref[...]
    joined = jnp.concatenate(
        [
            jnp.zeros((tap_count, channels), x.dtype),
            x,
            jnp.zeros((2 * outputs - tap_count, channels), x.dtype),
        ],
        axis=0,
    )
    filtered = jnp.concatenate(
        [
            exact_dot(matrices, joined[b * 2 * outputs : b * 2 * outputs + 2 * outputs + tap_count])
            for b in range(blocks)
        ],
        axis=0,
    )
    filtered = filtered.astype(jnp.bfloat16)
    spectrum = exact_dot([table_ref[p] for p in range(table_ref.shape[0])], filtered)
    real_part = spectrum[:NF]
    imag_part = spectrum[NF:]
    powers = real_part * real_part + imag_part * imag_part
    mean_power = jnp.mean(powers, axis=0, keepdims=True)
    whitening = 1.0 / jnp.sqrt(powers + mean_power + 1e-06)
    whitened = jnp.concatenate([real_part * whitening, imag_part * whitening], axis=0)
    extended = whitened.astype(jnp.bfloat16).astype(jnp.float32).T
    span = shifted.shape[1]
    own_f32[...] = extended[:rows]
    narrow = extended.astype(jnp.bfloat16)
    offset = lax.broadcasted_iota(jnp.int32, (span, channels), 1) - lax.broadcasted_iota(
        jnp.int32, (span, channels), 0
    )
    for i in range(chunk):
        pick = (offset == i).astype(jnp.bfloat16)
        shifted[i] = jnp.dot(pick, narrow, preferred_element_type=jnp.float32)
    slots, parts = buffers.shape[0], sems.shape[1]
    part = chunk // parts
    copies = []
    for m in range(rows // chunk):
        slot = m % slots
        if m >= slots:
            for copy in copies[m - slots]:
                copy.wait()
        base = m * chunk
        for i in range(chunk):
            a = own_f32[base + i : base + i + 1, :]
            b = shifted[i, base : base + LAGS, :]
            acc_re, acc_im = product_terms(a, b)
            store_row(buffers.at[slot], i, acc_re, acc_im, 1)
        group = []
        for p in range(parts):
            copy = pltpu.make_async_copy(
                buffers.at[slot, pl.ds(p * part, part)],
                out_hbm.at[pl.ds(base + p * part, part)],
                sems.at[slot, p],
            )
            copy.start()
            group.append(copy)
        copies.append(group)
    for group in copies[-slots:]:
        for copy in group:
            copy.wait()


def fused_spectra(samples, filter_taps, table_t, rows):
    length, channels = samples.shape
    chunk = 8
    span = channels - chunk
    return pl.pallas_call(
        functools.partial(fused_kernel, rows, chunk),
        out_shape=jax.ShapeDtypeStruct((rows, LAGS, NFFT), jnp.bfloat16),
        in_specs=[pl.BlockSpec(memory_space=pltpu.SMEM)] + [pl.BlockSpec(memory_space=pltpu.VMEM)] * 2,
        out_specs=pl.BlockSpec(memory_space=pl.ANY),
        scratch_shapes=[
            pltpu.VMEM((rows, NFFT), jnp.float32),
            pltpu.VMEM((chunk, span, NFFT), jnp.float32),
            pltpu.VMEM((4, chunk, LAGS, NFFT), jnp.bfloat16),
            pltpu.SemaphoreType.DMA((4, 4)),
        ],
        cost_estimate=pl.CostEstimate(
            flops=6 * rows * LAGS * NF + 12 * channels * (NF * 320 * length // 256 + NFFT * NFFT),
            transcendentals=2 * NF * channels,
            bytes_accessed=rows * LAGS * NFFT * 2 + 2 * samples.size + 2 * table_t.size,
        ),
    )(filter_taps, samples, table_t)


def cross_spectra(own, extended):
    rows, segments, columns = own.shape
    reach_rows = extended.shape[0]
    own_flat = own.reshape(rows, segments * columns)
    ext_flat = extended.reshape(reach_rows, segments * columns)
    rows_per_step = 8
    span = reach_rows - rows_per_step
    scratch_bytes = rows_per_step * span * segments * columns * 4
    cost = pl.CostEstimate(
        flops=6 * rows * LAGS * NF * segments,
        transcendentals=0,
        bytes_accessed=rows * LAGS * columns * 2 + 2 * segments * (rows + reach_rows) * columns,
    )
    common = dict(
        out_shape=jax.ShapeDtypeStruct((rows, LAGS, columns), jnp.bfloat16),
        grid=(rows // rows_per_step,),
        in_specs=[
            pl.BlockSpec((rows, segments * columns), lambda i: (0, 0)),
            pl.BlockSpec((reach_rows, segments * columns), lambda i: (0, 0)),
        ],
        out_specs=pl.BlockSpec((rows_per_step, LAGS, columns), lambda i: (i, 0, 0)),
        cost_estimate=cost,
    )
    if scratch_bytes <= 8 * 1024 * 1024:
        return pl.pallas_call(
            functools.partial(cross_kernel_shifted, segments, rows_per_step),
            scratch_shapes=[
                pltpu.VMEM((rows, segments * columns), jnp.float32),
                pltpu.VMEM((rows_per_step, span, segments * columns), jnp.float32),
            ],
            compiler_params=pltpu.CompilerParams(dimension_semantics=("arbitrary",)),
            **common,
        )(own_flat, ext_flat)
    return pl.pallas_call(
        functools.partial(cross_kernel, segments, rows_per_step), **common
    )(own_flat, ext_flat)


def body(strain, filter_taps):
    extent = lax.axis_size("ta")
    columns_n = lax.axis_size("col")
    section_rows, slab = strain.shape
    block_rows = section_rows // extent
    reach = LAGS // block_rows
    turned = strain.T
    route = [(c + 1, c) for c in range(columns_n - 1)]
    following = lax.ppermute(turned, "col", route)
    tail = following[:, : reach * block_rows]
    width = (reach + 1) * block_rows
    windows = channel_windows(turned, tail, extent, width, reach * block_rows)
    gathered = lax.all_to_all(windows, "ta", split_axis=0, concat_axis=0, tiled=True)
    samples = gathered.reshape(extent * slab, width)
    if extent * slab == 2 * NFFT:
        table_parts = jnp.stack(split_three_kept(fourier_table_t()))
        return fused_spectra(samples, filter_taps, table_parts, block_rows)[None]
    filtered = decimate_t(samples.astype(jnp.float32), filter_taps)
    whitened_t = whiten_t(filtered)
    segments, columns, _ = whitened_t.shape
    if segments * 8 * width * columns * 4 <= 8 * 1024 * 1024:
        flat = whitened_t.reshape(segments * columns, width)
        return cross_spectra_pieces([flat])[None]
    extended = whitened_t.transpose(2, 0, 1)
    return cross_spectra(extended[:block_rows], extended)[None]


def solution(mesh):
    return jax.shard_map(
        body,
        mesh=mesh,
        in_specs=(P("col", "ta"), P()),
        out_specs=P("col", "ta", None, None),
        check_vma=False,
    )
```

```python
import functools

import jax
import jax.numpy as jnp
from jax import lax
from jax.experimental import pallas as pl
from jax.experimental.pallas import tpu as pltpu
from jax.sharding import PartitionSpec as P

NFFT = 256
NF = 128
LAGS = 128


def tap_rows(filter_taps, outputs):
    tap_count = filter_taps.shape[0]
    window = 2 * outputs + tap_count
    flipped = filter_taps[::-1]
    period = jnp.concatenate([flipped, jnp.zeros((window + 2 - tap_count,), jnp.float32)])
    repeated = jnp.tile(period, outputs)[: outputs * window]
    return repeated.reshape(outputs, window)


def decimate_t(samples, filter_taps):
    length, channels = samples.shape
    tap_count = filter_taps.shape[0]
    outputs = min(length, NFFT) // 2
    blocks = length // (2 * outputs)
    joined = jnp.concatenate(
        [
            jnp.zeros((tap_count, channels), jnp.float32),
            samples,
            jnp.zeros((2 * outputs - tap_count, channels), jnp.float32),
        ],
        axis=0,
    )
    joined = joined.reshape(blocks + 1, 2 * outputs, channels)
    windows = jnp.concatenate([joined[:-1], joined[1:, :tap_count]], axis=1)
    matrix = tap_rows(filter_taps, outputs)
    result = jnp.einsum("tw,bwc->btc", matrix, windows, precision=lax.Precision.HIGHEST)
    return result.reshape(blocks * outputs, channels).astype(jnp.bfloat16)


def fourier_table():
    moment = lax.broadcasted_iota(jnp.int32, (NFFT, NF), 0)
    frequency = lax.broadcasted_iota(jnp.int32, (NFFT, NF), 1) + 1
    phase_index = moment * frequency % NFFT
    angles = phase_index.astype(jnp.float32) * (2.0 * jnp.pi / NFFT)
    window_taper = 0.5 - 0.5 * jnp.cos(moment.astype(jnp.float32) * (2.0 * jnp.pi / NFFT))
    return jnp.concatenate(
        [window_taper * jnp.cos(angles), -window_taper * jnp.sin(angles)], axis=1
    )


def fourier_table_t():
    moment = lax.broadcasted_iota(jnp.int32, (NFFT, NFFT), 1)
    frequency = lax.broadcasted_iota(jnp.int32, (NFFT, NFFT), 0) % NF + 1
    phase_index = moment * frequency % NFFT
    angles = phase_index.astype(jnp.float32) * (2.0 * jnp.pi / NFFT)
    window_taper = 0.5 - 0.5 * jnp.cos(moment.astype(jnp.float32) * (2.0 * jnp.pi / NFFT))
    real_rows = lax.broadcasted_iota(jnp.int32, (NFFT, NFFT), 0) < NF
    return jnp.where(real_rows, window_taper * jnp.cos(angles), -window_taper * jnp.sin(angles))


def whiten_t(filtered):
    length, channels = filtered.shape
    pieces = filtered.reshape(length // NF, NF, channels)
    segment_rows = jnp.concatenate([pieces[:-1], pieces[1:]], axis=1)
    spectrum = jnp.einsum(
        "nf,snc->sfc",
        fourier_table(),
        segment_rows.astype(jnp.float32),
        precision=lax.Precision.HIGHEST,
    )
    real_part = spectrum[:, :NF]
    imag_part = spectrum[:, NF:]
    powers = real_part * real_part + imag_part * imag_part
    mean_power = jnp.mean(powers, axis=1, keepdims=True)
    whitening = 1.0 / jnp.sqrt(powers + mean_power + 1e-06)
    return jnp.concatenate([real_part * whitening, imag_part * whitening], axis=1).astype(
        jnp.bfloat16
    )


def windows_kernel(width, tail_rows, x_ref, out_ref):
    x = x_ref[...].astype(jnp.float32)
    padded = jnp.concatenate([x, jnp.zeros((x.shape[0], tail_rows), jnp.float32)], axis=1)
    step = (padded.shape[1] - width) // (out_ref.shape[0] - 1)
    for j in range(out_ref.shape[0]):
        out_ref[j] = padded[:, j * step : j * step + width].astype(out_ref.dtype)


def channel_windows(turned, tail, extent, width, tail_rows):
    slab, rows = turned.shape
    windows = pl.pallas_call(
        functools.partial(windows_kernel, width, tail_rows),
        out_shape=jax.ShapeDtypeStruct((extent, slab, width), turned.dtype),
        cost_estimate=pl.CostEstimate(
            flops=0, transcendentals=0, bytes_accessed=2 * (slab * rows + extent * slab * width)
        ),
    )(turned)
    step = (rows + tail_rows - width) // (extent - 1)
    count = -(-tail_rows // step)
    first = extent - count
    padded = jnp.concatenate([turned[:, first * step :], tail], axis=1)
    patch = jnp.stack([padded[:, j * step : j * step + width] for j in range(count)])
    return lax.dynamic_update_slice(windows, patch, (first, 0, 0))


def cross_kernel(segments, rows_per_step, own_ref, ext_ref, out_ref):
    step = pl.program_id(0)
    base = pl.multiple_of(step * rows_per_step, rows_per_step)
    for i in range(rows_per_step):
        acc_re = None
        acc_im = None
        for s in range(segments):
            a = own_ref[pl.ds(base, rows_per_step), pl.ds(s * NFFT, NFFT)]
            a = a.astype(jnp.float32)[i : i + 1]
            window = ext_ref[pl.ds(base, LAGS + rows_per_step), pl.ds(s * NFFT, NFFT)]
            b = window.astype(jnp.float32)[i : i + LAGS]
            terms = product_terms(a, b)
            if acc_re is None:
                acc_re, acc_im = terms
            else:
                acc_re = [x + y for x, y in zip(acc_re, terms[0])]
                acc_im = [x + y for x, y in zip(acc_im, terms[1])]
        store_row(out_ref, i, acc_re, acc_im, segments)


def product_terms(a, b):
    ar = a[:, :NF]
    ai = a[:, NF:]
    br = b[:, :NF]
    bi = b[:, NF:]
    return [ar * br, ai * bi], [ai * br, ar * bi]


def store_row(out_ref, i, acc_re, acc_im, segments):
    re = acc_re[0] + acc_re[1]
    im = acc_im[0] - acc_im[1]
    if segments > 1:
        re = re / segments
        im = im / segments
    out_ref[i, :, :NF] = re.astype(out_ref.dtype)
    out_ref[i, :, NF:] = im.astype(out_ref.dtype)


def cross_kernel_shifted(segments, rows_per_step, own_ref, ext_ref, out_ref, own_f32, shifted):
    step = pl.program_id(0)
    span = shifted.shape[1]

    @pl.when(step == 0)
    def _():
        own_f32[...] = own_ref[...].astype(jnp.float32)
        whole = ext_ref[...].astype(jnp.float32)
        for i in range(rows_per_step):
            shifted[i] = whole[i : i + span]

    base = pl.multiple_of(step * rows_per_step, rows_per_step)
    for i in range(rows_per_step):
        acc_re = None
        acc_im = None
        for s in range(segments):
            a = own_f32[pl.ds(base + i, 1), pl.ds(s * NFFT, NFFT)]
            b = shifted[i, pl.ds(base, LAGS), pl.ds(s * NFFT, NFFT)]
            terms = product_terms(a, b)
            if acc_re is None:
                acc_re, acc_im = terms
            else:
                acc_re = [x + y for x, y in zip(acc_re, terms[0])]
                acc_im = [x + y for x, y in zip(acc_im, terms[1])]
        store_row(out_ref, i, acc_re, acc_im, segments)


def cross_kernel_pieces(segments, rows, chunk, *refs):
    pieces = refs[:-5]
    out_hbm, own_f32, shifted, buffers, sems = refs[-5:]
    span = shifted.shape[1]
    extended = jnp.concatenate(
        [
            jnp.concatenate(
                [piece[s * NFFT : (s + 1) * NFFT, :].astype(jnp.float32).T for s in range(segments)],
                axis=1,
            )
            for piece in pieces
        ],
        axis=0,
    )
    own_f32[...] = extended[:rows]
    for i in range(chunk):
        shifted[i] = extended[i : i + span]
    slots, parts = buffers.shape[0], sems.shape[1]
    part = chunk // parts
    copies = []
    for m in range(rows // chunk):
        slot = m % slots
        if m >= slots:
            for copy in copies[m - slots]:
                copy.wait()
        base = m * chunk
        for i in range(chunk):
            acc_re = None
            acc_im = None
            for s in range(segments):
                a = own_f32[base + i : base + i + 1, s * NFFT : (s + 1) * NFFT]
                b = shifted[i, base : base + LAGS, s * NFFT : (s + 1) * NFFT]
                terms = product_terms(a, b)
                if acc_re is None:
                    acc_re, acc_im = terms
                else:
                    acc_re = [x + y for x, y in zip(acc_re, terms[0])]
                    acc_im = [x + y for x, y in zip(acc_im, terms[1])]
            store_row(buffers.at[slot], i, acc_re, acc_im, segments)
        group = []
        for p in range(parts):
            copy = pltpu.make_async_copy(
                buffers.at[slot, pl.ds(p * part, part)],
                out_hbm.at[pl.ds(base + p * part, part)],
                sems.at[slot, p],
            )
            copy.start()
            group.append(copy)
        copies.append(group)
    for group in copies[-slots:]:
        for copy in group:
            copy.wait()


def cross_spectra_pieces(pieces):
    width = pieces[0].shape[0]
    rows = sum(piece.shape[1] for piece in pieces) - LAGS
    segments = width // NFFT
    chunk = 8
    span = rows + LAGS - chunk
    return pl.pallas_call(
        functools.partial(cross_kernel_pieces, segments, rows, chunk),
        out_shape=jax.ShapeDtypeStruct((rows, LAGS, NFFT), jnp.bfloat16),
        in_specs=[pl.BlockSpec(memory_space=pltpu.VMEM)] * len(pieces),
        out_specs=pl.BlockSpec(memory_space=pl.ANY),
        scratch_shapes=[
            pltpu.VMEM((rows, width), jnp.float32),
            pltpu.VMEM((chunk, span, width), jnp.float32),
            pltpu.VMEM((4, chunk, LAGS, NFFT), jnp.bfloat16),
            pltpu.SemaphoreType.DMA((4, 4)),
        ],
        cost_estimate=pl.CostEstimate(
            flops=6 * rows * LAGS * NF * segments,
            transcendentals=0,
            bytes_accessed=rows * LAGS * NFFT * 2 + 2 * (rows + LAGS) * width,
        ),
    )(*pieces)


def split_three(values):
    high = values.astype(jnp.bfloat16)
    rest = values - high.astype(jnp.float32)
    middle = rest.astype(jnp.bfloat16)
    low = (rest - middle.astype(jnp.float32)).astype(jnp.bfloat16)
    return [high, middle, low]


def split_three_kept(values):
    high = lax.reduce_precision(values, exponent_bits=8, mantissa_bits=7)
    rest = values - high
    middle = lax.reduce_precision(rest, exponent_bits=8, mantissa_bits=7)
    low = rest - middle
    return [part.astype(jnp.bfloat16) for part in (high, middle, low)]


def exact_dot(parts, operand):
    total = None
    for part in parts:
        term = jnp.dot(part, operand, preferred_element_type=jnp.float32)
        total = term if total is None else total + term
    return total


def fused_kernel(rows, chunk, taps_ref, samples_ref, table_ref, out_hbm, own_f32, shifted,
                 buffers, sems):
    tap_count = taps_ref.shape[0]
    outputs = NFFT // 2
    length, channels = samples_ref.shape
    blocks = length // (2 * outputs)
    lanes = 3 * NF
    lane = lax.broadcasted_iota(jnp.int32, (1, lanes), 1)
    row = jnp.zeros((1, lanes), jnp.float32)
    for k in range(tap_count):
        row = jnp.where(lane == tap_count - 1 - k, taps_ref[k], row)
    matrices = []
    for part in split_three(row):
        rolled = pltpu.roll(
            jnp.broadcast_to(part.astype(jnp.float32), (outputs, lanes)), 0, 1, stride=2, stride_axis=0
        )
        matrices.append(rolled[:, : 2 * outputs + tap_count].astype(jnp.bfloat16))
    x = samples_ref[...]
    joined = jnp.concatenate(
        [
            jnp.zeros((tap_count, channels), x.dtype),
            x,
            jnp.zeros((2 * outputs - tap_count, channels), x.dtype),
        ],
        axis=0,
    )
    filtered = jnp.concatenate(
        [
            exact_dot(matrices, joined[b * 2 * outputs : b * 2 * outputs + 2 * outputs + tap_count])
            for b in range(blocks)
        ],
        axis=0,
    )
    filtered = filtered.astype(jnp.bfloat16)
    spectrum = exact_dot([table_ref[p] for p in range(table_ref.shape[0])], filtered)
    real_part = spectrum[:NF]
    imag_part = spectrum[NF:]
    powers = real_part * real_part + imag_part * imag_part
    mean_power = jnp.mean(powers, axis=0, keepdims=True)
    whitening = lax.rsqrt(powers + mean_power + 1e-06)
    whitened = jnp.concatenate([real_part * whitening, imag_part * whitening], axis=0)
    extended = whitened.astype(jnp.bfloat16).astype(jnp.float32).T
    span = shifted.shape[1]
    own_f32[...] = extended[:rows]
    for i in range(chunk):
        shifted[i] = extended[i : i + span]
    slots, parts = buffers.shape[0], sems.shape[1]
    part = chunk // parts
    copies = []
    for m in range(rows // chunk):
        slot = m % slots
        if m >= slots:
            for copy in copies[m - slots]:
                copy.wait()
        base = m * chunk
        for i in range(chunk):
            a = own_f32[base + i : base + i + 1, :]
            b = shifted[i, base : base + LAGS, :]
            acc_re, acc_im = product_terms(a, b)
            store_row(buffers.at[slot], i, acc_re, acc_im, 1)
        group = []
        for p in range(parts):
            copy = pltpu.make_async_copy(
                buffers.at[slot, pl.ds(p * part, part)],
                out_hbm.at[pl.ds(base + p * part, part)],
                sems.at[slot, p],
            )
            copy.start()
            group.append(copy)
        copies.append(group)
    for group in copies[-slots:]:
        for copy in group:
            copy.wait()


def fused_spectra(samples, filter_taps, table_t, rows):
    length, channels = samples.shape
    chunk = 8
    span = channels - chunk
    return pl.pallas_call(
        functools.partial(fused_kernel, rows, chunk),
        out_shape=jax.ShapeDtypeStruct((rows, LAGS, NFFT), jnp.bfloat16),
        in_specs=[pl.BlockSpec(memory_space=pltpu.SMEM)] + [pl.BlockSpec(memory_space=pltpu.VMEM)] * 2,
        out_specs=pl.BlockSpec(memory_space=pl.ANY),
        scratch_shapes=[
            pltpu.VMEM((rows, NFFT), jnp.float32),
            pltpu.VMEM((chunk, span, NFFT), jnp.float32),
            pltpu.VMEM((4, chunk, LAGS, NFFT), jnp.bfloat16),
            pltpu.SemaphoreType.DMA((4, 4)),
        ],
        cost_estimate=pl.CostEstimate(
            flops=6 * rows * LAGS * NF + 12 * channels * (NF * 320 * length // 256 + NFFT * NFFT),
            transcendentals=2 * NF * channels,
            bytes_accessed=rows * LAGS * NFFT * 2 + 2 * samples.size + 2 * table_t.size,
        ),
    )(filter_taps, samples, table_t)


def cross_spectra(own, extended):
    rows, segments, columns = own.shape
    reach_rows = extended.shape[0]
    own_flat = own.reshape(rows, segments * columns)
    ext_flat = extended.reshape(reach_rows, segments * columns)
    rows_per_step = 8
    span = reach_rows - rows_per_step
    scratch_bytes = rows_per_step * span * segments * columns * 4
    cost = pl.CostEstimate(
        flops=6 * rows * LAGS * NF * segments,
        transcendentals=0,
        bytes_accessed=rows * LAGS * columns * 2 + 2 * segments * (rows + reach_rows) * columns,
    )
    common = dict(
        out_shape=jax.ShapeDtypeStruct((rows, LAGS, columns), jnp.bfloat16),
        grid=(rows // rows_per_step,),
        in_specs=[
            pl.BlockSpec((rows, segments * columns), lambda i: (0, 0)),
            pl.BlockSpec((reach_rows, segments * columns), lambda i: (0, 0)),
        ],
        out_specs=pl.BlockSpec((rows_per_step, LAGS, columns), lambda i: (i, 0, 0)),
        cost_estimate=cost,
    )
    if scratch_bytes <= 8 * 1024 * 1024:
        return pl.pallas_call(
            functools.partial(cross_kernel_shifted, segments, rows_per_step),
            scratch_shapes=[
                pltpu.VMEM((rows, segments * columns), jnp.float32),
                pltpu.VMEM((rows_per_step, span, segments * columns), jnp.float32),
            ],
            compiler_params=pltpu.CompilerParams(dimension_semantics=("arbitrary",)),
            **common,
        )(own_flat, ext_flat)
    return pl.pallas_call(
        functools.partial(cross_kernel, segments, rows_per_step), **common
    )(own_flat, ext_flat)


def body(strain, filter_taps):
    extent = lax.axis_size("ta")
    columns_n = lax.axis_size("col")
    section_rows, slab = strain.shape
    block_rows = section_rows // extent
    reach = LAGS // block_rows
    turned = strain.T
    route = [(c + 1, c) for c in range(columns_n - 1)]
    following = lax.ppermute(turned, "col", route)
    tail = following[:, : reach * block_rows]
    width = (reach + 1) * block_rows
    windows = channel_windows(turned, tail, extent, width, reach * block_rows)
    gathered = lax.all_to_all(windows, "ta", split_axis=0, concat_axis=0, tiled=True)
    samples = gathered.reshape(extent * slab, width)
    if extent * slab == 2 * NFFT:
        table_parts = jnp.stack(split_three_kept(fourier_table_t()))
        return fused_spectra(samples, filter_taps, table_parts, block_rows)[None]
    filtered = decimate_t(samples.astype(jnp.float32), filter_taps)
    whitened_t = whiten_t(filtered)
    segments, columns, _ = whitened_t.shape
    if segments * 8 * width * columns * 4 <= 8 * 1024 * 1024:
        flat = whitened_t.reshape(segments * columns, width)
        return cross_spectra_pieces([flat])[None]
    extended = whitened_t.transpose(2, 0, 1)
    return cross_spectra(extended[:block_rows], extended)[None]


def solution(mesh):
    return jax.shard_map(
        body,
        mesh=mesh,
        in_specs=(P("col", "ta"), P()),
        out_specs=P("col", "ta", None, None),
        check_vma=False,
    )
```

```python
import functools

import jax
import jax.numpy as jnp
from jax import lax
from jax.experimental import pallas as pl
from jax.experimental.pallas import tpu as pltpu
from jax.sharding import PartitionSpec as P

NFFT = 256
NF = 128
LAGS = 128


def tap_rows(filter_taps, outputs):
    tap_count = filter_taps.shape[0]
    window = 2 * outputs + tap_count
    flipped = filter_taps[::-1]
    period = jnp.concatenate([flipped, jnp.zeros((window + 2 - tap_count,), jnp.float32)])
    repeated = jnp.tile(period, outputs)[: outputs * window]
    return repeated.reshape(outputs, window)


def decimate_t(samples, filter_taps):
    length, channels = samples.shape
    tap_count = filter_taps.shape[0]
    outputs = min(length, NFFT) // 2
    blocks = length // (2 * outputs)
    joined = jnp.concatenate(
        [
            jnp.zeros((tap_count, channels), jnp.float32),
            samples,
            jnp.zeros((2 * outputs - tap_count, channels), jnp.float32),
        ],
        axis=0,
    )
    joined = joined.reshape(blocks + 1, 2 * outputs, channels)
    windows = jnp.concatenate([joined[:-1], joined[1:, :tap_count]], axis=1)
    matrix = tap_rows(filter_taps, outputs)
    result = jnp.einsum("tw,bwc->btc", matrix, windows, precision=lax.Precision.HIGHEST)
    return result.reshape(blocks * outputs, channels).astype(jnp.bfloat16)


def fourier_table():
    moment = lax.broadcasted_iota(jnp.int32, (NFFT, NF), 0)
    frequency = lax.broadcasted_iota(jnp.int32, (NFFT, NF), 1) + 1
    phase_index = moment * frequency % NFFT
    angles = phase_index.astype(jnp.float32) * (2.0 * jnp.pi / NFFT)
    window_taper = 0.5 - 0.5 * jnp.cos(moment.astype(jnp.float32) * (2.0 * jnp.pi / NFFT))
    return jnp.concatenate(
        [window_taper * jnp.cos(angles), -window_taper * jnp.sin(angles)], axis=1
    )


def fourier_table_t():
    moment = lax.broadcasted_iota(jnp.int32, (NFFT, NFFT), 1)
    frequency = lax.broadcasted_iota(jnp.int32, (NFFT, NFFT), 0) % NF + 1
    phase_index = moment * frequency % NFFT
    angles = phase_index.astype(jnp.float32) * (2.0 * jnp.pi / NFFT)
    window_taper = 0.5 - 0.5 * jnp.cos(moment.astype(jnp.float32) * (2.0 * jnp.pi / NFFT))
    real_rows = lax.broadcasted_iota(jnp.int32, (NFFT, NFFT), 0) < NF
    return jnp.where(real_rows, window_taper * jnp.cos(angles), -window_taper * jnp.sin(angles))


def whiten_t(filtered):
    length, channels = filtered.shape
    pieces = filtered.reshape(length // NF, NF, channels)
    segment_rows = jnp.concatenate([pieces[:-1], pieces[1:]], axis=1)
    spectrum = jnp.einsum(
        "nf,snc->sfc",
        fourier_table(),
        segment_rows.astype(jnp.float32),
        precision=lax.Precision.HIGHEST,
    )
    real_part = spectrum[:, :NF]
    imag_part = spectrum[:, NF:]
    powers = real_part * real_part + imag_part * imag_part
    mean_power = jnp.mean(powers, axis=1, keepdims=True)
    whitening = 1.0 / jnp.sqrt(powers + mean_power + 1e-06)
    return jnp.concatenate([real_part * whitening, imag_part * whitening], axis=1).astype(
        jnp.bfloat16
    )


def windows_kernel(width, tail_rows, x_ref, out_ref):
    x = x_ref[...].astype(jnp.float32)
    padded = jnp.concatenate([x, jnp.zeros((x.shape[0], tail_rows), jnp.float32)], axis=1)
    step = (padded.shape[1] - width) // (out_ref.shape[0] - 1)
    for j in range(out_ref.shape[0]):
        out_ref[j] = padded[:, j * step : j * step + width].astype(out_ref.dtype)


def channel_windows(turned, tail, extent, width, tail_rows):
    slab, rows = turned.shape
    windows = pl.pallas_call(
        functools.partial(windows_kernel, width, tail_rows),
        out_shape=jax.ShapeDtypeStruct((extent, slab, width), turned.dtype),
        cost_estimate=pl.CostEstimate(
            flops=0, transcendentals=0, bytes_accessed=2 * (slab * rows + extent * slab * width)
        ),
    )(turned)
    step = (rows + tail_rows - width) // (extent - 1)
    count = -(-tail_rows // step)
    first = extent - count
    patch = jnp.stack(
        [
            jnp.concatenate(
                [windows[j, :, : rows - j * step], tail[:, : width - (rows - j * step)]], axis=1
            )
            for j in range(first, extent)
        ]
    )
    return lax.dynamic_update_slice(windows, patch, (first, 0, 0))


def cross_kernel(segments, rows_per_step, own_ref, ext_ref, out_ref):
    step = pl.program_id(0)
    base = pl.multiple_of(step * rows_per_step, rows_per_step)
    for i in range(rows_per_step):
        acc_re = None
        acc_im = None
        for s in range(segments):
            a = own_ref[pl.ds(base, rows_per_step), pl.ds(s * NFFT, NFFT)]
            a = a.astype(jnp.float32)[i : i + 1]
            window = ext_ref[pl.ds(base, LAGS + rows_per_step), pl.ds(s * NFFT, NFFT)]
            b = window.astype(jnp.float32)[i : i + LAGS]
            terms = product_terms(a, b)
            if acc_re is None:
                acc_re, acc_im = terms
            else:
                acc_re = [x + y for x, y in zip(acc_re, terms[0])]
                acc_im = [x + y for x, y in zip(acc_im, terms[1])]
        store_row(out_ref, i, acc_re, acc_im, segments)


def product_terms(a, b):
    ar = a[:, :NF]
    ai = a[:, NF:]
    br = b[:, :NF]
    bi = b[:, NF:]
    return [ar * br, ai * bi], [ai * br, ar * bi]


def store_row(out_ref, i, acc_re, acc_im, segments):
    re = acc_re[0] + acc_re[1]
    im = acc_im[0] - acc_im[1]
    if segments > 1:
        re = re / segments
        im = im / segments
    out_ref[i, :, :NF] = re.astype(out_ref.dtype)
    out_ref[i, :, NF:] = im.astype(out_ref.dtype)


def cross_kernel_shifted(segments, rows_per_step, own_ref, ext_ref, out_ref, own_f32, shifted):
    step = pl.program_id(0)
    span = shifted.shape[1]

    @pl.when(step == 0)
    def _():
        own_f32[...] = own_ref[...].astype(jnp.float32)
        whole = ext_ref[...].astype(jnp.float32)
        for i in range(rows_per_step):
            shifted[i] = whole[i : i + span]

    base = pl.multiple_of(step * rows_per_step, rows_per_step)
    for i in range(rows_per_step):
        acc_re = None
        acc_im = None
        for s in range(segments):
            a = own_f32[pl.ds(base + i, 1), pl.ds(s * NFFT, NFFT)]
            b = shifted[i, pl.ds(base, LAGS), pl.ds(s * NFFT, NFFT)]
            terms = product_terms(a, b)
            if acc_re is None:
                acc_re, acc_im = terms
            else:
                acc_re = [x + y for x, y in zip(acc_re, terms[0])]
                acc_im = [x + y for x, y in zip(acc_im, terms[1])]
        store_row(out_ref, i, acc_re, acc_im, segments)


def cross_kernel_pieces(segments, rows, chunk, *refs):
    pieces = refs[:-5]
    out_hbm, own_f32, shifted, buffers, sems = refs[-5:]
    span = shifted.shape[1]
    extended = jnp.concatenate(
        [
            jnp.concatenate(
                [piece[s * NFFT : (s + 1) * NFFT, :].astype(jnp.float32).T for s in range(segments)],
                axis=1,
            )
            for piece in pieces
        ],
        axis=0,
    )
    own_f32[...] = extended[:rows]
    for i in range(chunk):
        shifted[i] = extended[i : i + span]
    slots, parts = buffers.shape[0], sems.shape[1]
    part = chunk // parts
    copies = []
    for m in range(rows // chunk):
        slot = m % slots
        if m >= slots:
            for copy in copies[m - slots]:
                copy.wait()
        base = m * chunk
        for i in range(chunk):
            acc_re = None
            acc_im = None
            for s in range(segments):
                a = own_f32[base + i : base + i + 1, s * NFFT : (s + 1) * NFFT]
                b = shifted[i, base : base + LAGS, s * NFFT : (s + 1) * NFFT]
                terms = product_terms(a, b)
                if acc_re is None:
                    acc_re, acc_im = terms
                else:
                    acc_re = [x + y for x, y in zip(acc_re, terms[0])]
                    acc_im = [x + y for x, y in zip(acc_im, terms[1])]
            store_row(buffers.at[slot], i, acc_re, acc_im, segments)
        group = []
        for p in range(parts):
            copy = pltpu.make_async_copy(
                buffers.at[slot, pl.ds(p * part, part)],
                out_hbm.at[pl.ds(base + p * part, part)],
                sems.at[slot, p],
            )
            copy.start()
            group.append(copy)
        copies.append(group)
    for group in copies[-slots:]:
        for copy in group:
            copy.wait()


def cross_spectra_pieces(pieces):
    width = pieces[0].shape[0]
    rows = sum(piece.shape[1] for piece in pieces) - LAGS
    segments = width // NFFT
    chunk = 8
    span = rows + LAGS - chunk
    return pl.pallas_call(
        functools.partial(cross_kernel_pieces, segments, rows, chunk),
        out_shape=jax.ShapeDtypeStruct((rows, LAGS, NFFT), jnp.bfloat16),
        in_specs=[pl.BlockSpec(memory_space=pltpu.VMEM)] * len(pieces),
        out_specs=pl.BlockSpec(memory_space=pl.ANY),
        scratch_shapes=[
            pltpu.VMEM((rows, width), jnp.float32),
            pltpu.VMEM((chunk, span, width), jnp.float32),
            pltpu.VMEM((4, chunk, LAGS, NFFT), jnp.bfloat16),
            pltpu.SemaphoreType.DMA((4, 4)),
        ],
        cost_estimate=pl.CostEstimate(
            flops=6 * rows * LAGS * NF * segments,
            transcendentals=0,
            bytes_accessed=rows * LAGS * NFFT * 2 + 2 * (rows + LAGS) * width,
        ),
    )(*pieces)


def split_three(values):
    high = values.astype(jnp.bfloat16)
    rest = values - high.astype(jnp.float32)
    middle = rest.astype(jnp.bfloat16)
    low = (rest - middle.astype(jnp.float32)).astype(jnp.bfloat16)
    return [high, middle, low]


def split_three_kept(values):
    high = lax.reduce_precision(values, exponent_bits=8, mantissa_bits=7)
    rest = values - high
    middle = lax.reduce_precision(rest, exponent_bits=8, mantissa_bits=7)
    low = rest - middle
    return [part.astype(jnp.bfloat16) for part in (high, middle, low)]


def exact_dot(parts, operand):
    total = None
    for part in parts:
        term = jnp.dot(part, operand, preferred_element_type=jnp.float32)
        total = term if total is None else total + term
    return total


def fused_kernel(rows, chunk, taps_ref, samples_ref, table_ref, out_hbm, own_f32, shifted,
                 buffers, sems):
    tap_count = taps_ref.shape[0]
    outputs = NFFT // 2
    length, channels = samples_ref.shape
    blocks = length // (2 * outputs)
    lanes = 3 * NF
    lane = lax.broadcasted_iota(jnp.int32, (1, lanes), 1)
    row = jnp.zeros((1, lanes), jnp.float32)
    for k in range(tap_count):
        row = jnp.where(lane == tap_count - 1 - k, taps_ref[k], row)
    matrices = []
    for part in split_three(row):
        rolled = pltpu.roll(
            jnp.broadcast_to(part.astype(jnp.float32), (outputs, lanes)), 0, 1, stride=2, stride_axis=0
        )
        matrices.append(rolled[:, : 2 * outputs + tap_count].astype(jnp.bfloat16))
    x = samples_ref[...]
    joined = jnp.concatenate(
        [
            jnp.zeros((tap_count, channels), x.dtype),
            x,
            jnp.zeros((2 * outputs - tap_count, channels), x.dtype),
        ],
        axis=0,
    )
    filtered = jnp.concatenate(
        [
            exact_dot(matrices, joined[b * 2 * outputs : b * 2 * outputs + 2 * outputs + tap_count])
            for b in range(blocks)
        ],
        axis=0,
    )
    filtered = filtered.astype(jnp.bfloat16)
    spectrum = exact_dot([table_ref[p] for p in range(table_ref.shape[0])], filtered)
    real_part = spectrum[:NF]
    imag_part = spectrum[NF:]
    powers = real_part * real_part + imag_part * imag_part
    mean_power = jnp.mean(powers, axis=0, keepdims=True)
    whitening = lax.rsqrt(powers + mean_power + 1e-06)
    whitened = jnp.concatenate([real_part * whitening, imag_part * whitening], axis=0)
    extended = whitened.astype(jnp.bfloat16).astype(jnp.float32).T
    span = shifted.shape[1]
    own_f32[...] = extended[:rows]
    for i in range(chunk):
        shifted[i] = extended[i : i + span]
    slots, parts = buffers.shape[0], sems.shape[1]
    part = chunk // parts
    copies = []
    for m in range(rows // chunk):
        slot = m % slots
        if m >= slots:
            for copy in copies[m - slots]:
                copy.wait()
        base = m * chunk
        for i in range(chunk):
            a = own_f32[base + i : base + i + 1, :]
            b = shifted[i, base : base + LAGS, :]
            acc_re, acc_im = product_terms(a, b)
            store_row(buffers.at[slot], i, acc_re, acc_im, 1)
        group = []
        for p in range(parts):
            copy = pltpu.make_async_copy(
                buffers.at[slot, pl.ds(p * part, part)],
                out_hbm.at[pl.ds(base + p * part, part)],
                sems.at[slot, p],
            )
            copy.start()
            group.append(copy)
        copies.append(group)
    for group in copies[-slots:]:
        for copy in group:
            copy.wait()


def fused_spectra(samples, filter_taps, table_t, rows):
    length, channels = samples.shape
    chunk = 8
    span = channels - chunk
    return pl.pallas_call(
        functools.partial(fused_kernel, rows, chunk),
        out_shape=jax.ShapeDtypeStruct((rows, LAGS, NFFT), jnp.bfloat16),
        in_specs=[pl.BlockSpec(memory_space=pltpu.SMEM)] + [pl.BlockSpec(memory_space=pltpu.VMEM)] * 2,
        out_specs=pl.BlockSpec(memory_space=pl.ANY),
        scratch_shapes=[
            pltpu.VMEM((rows, NFFT), jnp.float32),
            pltpu.VMEM((chunk, span, NFFT), jnp.float32),
            pltpu.VMEM((4, chunk, LAGS, NFFT), jnp.bfloat16),
            pltpu.SemaphoreType.DMA((4, 4)),
        ],
        cost_estimate=pl.CostEstimate(
            flops=6 * rows * LAGS * NF + 12 * channels * (NF * 320 * length // 256 + NFFT * NFFT),
            transcendentals=2 * NF * channels,
            bytes_accessed=rows * LAGS * NFFT * 2 + 2 * samples.size + 2 * table_t.size,
        ),
    )(filter_taps, samples, table_t)


def cross_spectra(own, extended):
    rows, segments, columns = own.shape
    reach_rows = extended.shape[0]
    own_flat = own.reshape(rows, segments * columns)
    ext_flat = extended.reshape(reach_rows, segments * columns)
    rows_per_step = 8
    span = reach_rows - rows_per_step
    scratch_bytes = rows_per_step * span * segments * columns * 4
    cost = pl.CostEstimate(
        flops=6 * rows * LAGS * NF * segments,
        transcendentals=0,
        bytes_accessed=rows * LAGS * columns * 2 + 2 * segments * (rows + reach_rows) * columns,
    )
    common = dict(
        out_shape=jax.ShapeDtypeStruct((rows, LAGS, columns), jnp.bfloat16),
        grid=(rows // rows_per_step,),
        in_specs=[
            pl.BlockSpec((rows, segments * columns), lambda i: (0, 0)),
            pl.BlockSpec((reach_rows, segments * columns), lambda i: (0, 0)),
        ],
        out_specs=pl.BlockSpec((rows_per_step, LAGS, columns), lambda i: (i, 0, 0)),
        cost_estimate=cost,
    )
    if scratch_bytes <= 8 * 1024 * 1024:
        return pl.pallas_call(
            functools.partial(cross_kernel_shifted, segments, rows_per_step),
            scratch_shapes=[
                pltpu.VMEM((rows, segments * columns), jnp.float32),
                pltpu.VMEM((rows_per_step, span, segments * columns), jnp.float32),
            ],
            compiler_params=pltpu.CompilerParams(dimension_semantics=("arbitrary",)),
            **common,
        )(own_flat, ext_flat)
    return pl.pallas_call(
        functools.partial(cross_kernel, segments, rows_per_step), **common
    )(own_flat, ext_flat)


def body(strain, filter_taps):
    extent = lax.axis_size("ta")
    columns_n = lax.axis_size("col")
    section_rows, slab = strain.shape
    block_rows = section_rows // extent
    reach = LAGS // block_rows
    turned = strain.T
    route = [(c + 1, c) for c in range(columns_n - 1)]
    following = lax.ppermute(turned, "col", route)
    tail = following[:, : reach * block_rows]
    width = (reach + 1) * block_rows
    windows = channel_windows(turned, tail, extent, width, reach * block_rows)
    gathered = lax.all_to_all(windows, "ta", split_axis=0, concat_axis=0, tiled=True)
    samples = gathered.reshape(extent * slab, width)
    if extent * slab == 2 * NFFT:
        table_parts = jnp.stack(split_three_kept(fourier_table_t()))
        return fused_spectra(samples, filter_taps, table_parts, block_rows)[None]
    filtered = decimate_t(samples.astype(jnp.float32), filter_taps)
    whitened_t = whiten_t(filtered)
    segments, columns, _ = whitened_t.shape
    if segments * 8 * width * columns * 4 <= 8 * 1024 * 1024:
        flat = whitened_t.reshape(segments * columns, width)
        return cross_spectra_pieces([flat])[None]
    extended = whitened_t.transpose(2, 0, 1)
    return cross_spectra(extended[:block_rows], extended)[None]


def solution(mesh):
    return jax.shard_map(
        body,
        mesh=mesh,
        in_specs=(P("col", "ta"), P()),
        out_specs=P("col", "ta", None, None),
        check_vma=False,
    )
```

```python
import functools

import jax
import jax.numpy as jnp
from jax import lax
from jax.experimental import pallas as pl
from jax.experimental.pallas import tpu as pltpu
from jax.sharding import PartitionSpec as P

NFFT = 256
NF = 128
LAGS = 128


def tap_rows(filter_taps, outputs):
    tap_count = filter_taps.shape[0]
    window = 2 * outputs + tap_count
    flipped = filter_taps[::-1]
    period = jnp.concatenate([flipped, jnp.zeros((window + 2 - tap_count,), jnp.float32)])
    repeated = jnp.tile(period, outputs)[: outputs * window]
    return repeated.reshape(outputs, window)


def decimate_t(samples, filter_taps):
    length, channels = samples.shape
    tap_count = filter_taps.shape[0]
    outputs = min(length, NFFT) // 2
    blocks = length // (2 * outputs)
    joined = jnp.concatenate(
        [
            jnp.zeros((tap_count, channels), jnp.float32),
            samples,
            jnp.zeros((2 * outputs - tap_count, channels), jnp.float32),
        ],
        axis=0,
    )
    joined = joined.reshape(blocks + 1, 2 * outputs, channels)
    windows = jnp.concatenate([joined[:-1], joined[1:, :tap_count]], axis=1)
    matrix = tap_rows(filter_taps, outputs)
    result = jnp.einsum("tw,bwc->btc", matrix, windows, precision=lax.Precision.HIGHEST)
    return result.reshape(blocks * outputs, channels).astype(jnp.bfloat16)


def fourier_table():
    moment = lax.broadcasted_iota(jnp.int32, (NFFT, NF), 0)
    frequency = lax.broadcasted_iota(jnp.int32, (NFFT, NF), 1) + 1
    phase_index = moment * frequency % NFFT
    angles = phase_index.astype(jnp.float32) * (2.0 * jnp.pi / NFFT)
    window_taper = 0.5 - 0.5 * jnp.cos(moment.astype(jnp.float32) * (2.0 * jnp.pi / NFFT))
    return jnp.concatenate(
        [window_taper * jnp.cos(angles), -window_taper * jnp.sin(angles)], axis=1
    )


def fourier_table_t():
    moment = lax.broadcasted_iota(jnp.int32, (NFFT, NFFT), 1)
    frequency = lax.broadcasted_iota(jnp.int32, (NFFT, NFFT), 0) % NF + 1
    phase_index = moment * frequency % NFFT
    angles = phase_index.astype(jnp.float32) * (2.0 * jnp.pi / NFFT)
    window_taper = 0.5 - 0.5 * jnp.cos(moment.astype(jnp.float32) * (2.0 * jnp.pi / NFFT))
    real_rows = lax.broadcasted_iota(jnp.int32, (NFFT, NFFT), 0) < NF
    return jnp.where(real_rows, window_taper * jnp.cos(angles), -window_taper * jnp.sin(angles))


def whiten_t(filtered):
    length, channels = filtered.shape
    pieces = filtered.reshape(length // NF, NF, channels)
    segment_rows = jnp.concatenate([pieces[:-1], pieces[1:]], axis=1)
    spectrum = jnp.einsum(
        "nf,snc->sfc",
        fourier_table(),
        segment_rows.astype(jnp.float32),
        precision=lax.Precision.HIGHEST,
    )
    real_part = spectrum[:, :NF]
    imag_part = spectrum[:, NF:]
    powers = real_part * real_part + imag_part * imag_part
    mean_power = jnp.mean(powers, axis=1, keepdims=True)
    whitening = 1.0 / jnp.sqrt(powers + mean_power + 1e-06)
    return jnp.concatenate([real_part * whitening, imag_part * whitening], axis=1).astype(
        jnp.bfloat16
    )


def windows_kernel(width, tail_rows, x_ref, out_ref):
    x = x_ref[...].astype(jnp.float32)
    padded = jnp.concatenate([x, jnp.zeros((x.shape[0], tail_rows), jnp.float32)], axis=1)
    step = (padded.shape[1] - width) // (out_ref.shape[0] - 1)
    for j in range(out_ref.shape[0]):
        out_ref[j] = padded[:, j * step : j * step + width].astype(out_ref.dtype)


def channel_windows(turned, tail, extent, width, tail_rows):
    slab, rows = turned.shape
    windows = pl.pallas_call(
        functools.partial(windows_kernel, width, tail_rows),
        out_shape=jax.ShapeDtypeStruct((extent, slab, width), turned.dtype),
        cost_estimate=pl.CostEstimate(
            flops=0, transcendentals=0, bytes_accessed=2 * (slab * rows + extent * slab * width)
        ),
    )(turned)
    step = (rows + tail_rows - width) // (extent - 1)
    count = -(-tail_rows // step)
    first = extent - count
    padded = jnp.concatenate([turned[:, first * step :], tail], axis=1)
    patch = jnp.stack([padded[:, j * step : j * step + width] for j in range(count)])
    return lax.dynamic_update_slice(windows, patch, (first, 0, 0))


def cross_kernel(segments, rows_per_step, own_ref, ext_ref, out_ref):
    step = pl.program_id(0)
    base = pl.multiple_of(step * rows_per_step, rows_per_step)
    for i in range(rows_per_step):
        acc_re = None
        acc_im = None
        for s in range(segments):
            a = own_ref[pl.ds(base, rows_per_step), pl.ds(s * NFFT, NFFT)]
            a = a.astype(jnp.float32)[i : i + 1]
            window = ext_ref[pl.ds(base, LAGS + rows_per_step), pl.ds(s * NFFT, NFFT)]
            b = window.astype(jnp.float32)[i : i + LAGS]
            terms = product_terms(a, b)
            if acc_re is None:
                acc_re, acc_im = terms
            else:
                acc_re = [x + y for x, y in zip(acc_re, terms[0])]
                acc_im = [x + y for x, y in zip(acc_im, terms[1])]
        store_row(out_ref, i, acc_re, acc_im, segments)


def product_terms(a, b):
    ar = a[:, :NF]
    ai = a[:, NF:]
    br = b[:, :NF]
    bi = b[:, NF:]
    return [ar * br, ai * bi], [ai * br, ar * bi]


def store_row(out_ref, i, acc_re, acc_im, segments):
    re = acc_re[0] + acc_re[1]
    im = acc_im[0] - acc_im[1]
    if segments > 1:
        re = re / segments
        im = im / segments
    out_ref[i, :, :NF] = re.astype(out_ref.dtype)
    out_ref[i, :, NF:] = im.astype(out_ref.dtype)


def cross_kernel_shifted(segments, rows_per_step, own_ref, ext_ref, out_ref, own_f32, shifted):
    step = pl.program_id(0)
    span = shifted.shape[1]

    @pl.when(step == 0)
    def _():
        own_f32[...] = own_ref[...].astype(jnp.float32)
        whole = ext_ref[...].astype(jnp.float32)
        for i in range(rows_per_step):
            shifted[i] = whole[i : i + span]

    base = pl.multiple_of(step * rows_per_step, rows_per_step)
    for i in range(rows_per_step):
        acc_re = None
        acc_im = None
        for s in range(segments):
            a = own_f32[pl.ds(base + i, 1), pl.ds(s * NFFT, NFFT)]
            b = shifted[i, pl.ds(base, LAGS), pl.ds(s * NFFT, NFFT)]
            terms = product_terms(a, b)
            if acc_re is None:
                acc_re, acc_im = terms
            else:
                acc_re = [x + y for x, y in zip(acc_re, terms[0])]
                acc_im = [x + y for x, y in zip(acc_im, terms[1])]
        store_row(out_ref, i, acc_re, acc_im, segments)


def cross_kernel_pieces(segments, rows, chunk, *refs):
    pieces = refs[:-5]
    out_hbm, own_f32, shifted, buffers, sems = refs[-5:]
    span = shifted.shape[1]
    extended = jnp.concatenate(
        [
            jnp.concatenate(
                [piece[s * NFFT : (s + 1) * NFFT, :].astype(jnp.float32).T for s in range(segments)],
                axis=1,
            )
            for piece in pieces
        ],
        axis=0,
    )
    own_f32[...] = extended[:rows]
    for i in range(chunk):
        shifted[i] = extended[i : i + span]
    slots, parts = buffers.shape[0], sems.shape[1]
    part = chunk // parts
    copies = []
    for m in range(rows // chunk):
        slot = m % slots
        if m >= slots:
            for copy in copies[m - slots]:
                copy.wait()
        base = m * chunk
        for i in range(chunk):
            acc_re = None
            acc_im = None
            for s in range(segments):
                a = own_f32[base + i : base + i + 1, s * NFFT : (s + 1) * NFFT]
                b = shifted[i, base : base + LAGS, s * NFFT : (s + 1) * NFFT]
                terms = product_terms(a, b)
                if acc_re is None:
                    acc_re, acc_im = terms
                else:
                    acc_re = [x + y for x, y in zip(acc_re, terms[0])]
                    acc_im = [x + y for x, y in zip(acc_im, terms[1])]
            store_row(buffers.at[slot], i, acc_re, acc_im, segments)
        group = []
        for p in range(parts):
            copy = pltpu.make_async_copy(
                buffers.at[slot, pl.ds(p * part, part)],
                out_hbm.at[pl.ds(base + p * part, part)],
                sems.at[slot, p],
            )
            copy.start()
            group.append(copy)
        copies.append(group)
    for group in copies[-slots:]:
        for copy in group:
            copy.wait()


def cross_spectra_pieces(pieces):
    width = pieces[0].shape[0]
    rows = sum(piece.shape[1] for piece in pieces) - LAGS
    segments = width // NFFT
    chunk = 8
    span = rows + LAGS - chunk
    return pl.pallas_call(
        functools.partial(cross_kernel_pieces, segments, rows, chunk),
        out_shape=jax.ShapeDtypeStruct((rows, LAGS, NFFT), jnp.bfloat16),
        in_specs=[pl.BlockSpec(memory_space=pltpu.VMEM)] * len(pieces),
        out_specs=pl.BlockSpec(memory_space=pl.ANY),
        scratch_shapes=[
            pltpu.VMEM((rows, width), jnp.float32),
            pltpu.VMEM((chunk, span, width), jnp.float32),
            pltpu.VMEM((4, chunk, LAGS, NFFT), jnp.bfloat16),
            pltpu.SemaphoreType.DMA((4, 4)),
        ],
        cost_estimate=pl.CostEstimate(
            flops=6 * rows * LAGS * NF * segments,
            transcendentals=0,
            bytes_accessed=rows * LAGS * NFFT * 2 + 2 * (rows + LAGS) * width,
        ),
    )(*pieces)


def split_three(values):
    high = values.astype(jnp.bfloat16)
    rest = values - high.astype(jnp.float32)
    middle = rest.astype(jnp.bfloat16)
    low = (rest - middle.astype(jnp.float32)).astype(jnp.bfloat16)
    return [high, middle, low]


def split_three_kept(values):
    high = lax.reduce_precision(values, exponent_bits=8, mantissa_bits=7)
    rest = values - high
    middle = lax.reduce_precision(rest, exponent_bits=8, mantissa_bits=7)
    low = rest - middle
    return [part.astype(jnp.bfloat16) for part in (high, middle, low)]


def exact_dot(parts, operand):
    total = None
    for part in parts:
        term = jnp.dot(part, operand, preferred_element_type=jnp.float32)
        total = term if total is None else total + term
    return total


def fused_kernel(rows, chunk, taps_ref, samples_ref, table_ref, out_hbm, own_f32, shifted,
                 buffers, sems):
    tap_count = taps_ref.shape[0]
    outputs = NFFT // 2
    length, channels = samples_ref.shape
    blocks = length // (2 * outputs)
    lanes = 3 * NF
    lane = lax.broadcasted_iota(jnp.int32, (1, lanes), 1)
    row = jnp.zeros((1, lanes), jnp.float32)
    for k in range(tap_count):
        row = jnp.where(lane == tap_count - 1 - k, taps_ref[k], row)
    matrices = []
    for part in split_three(row):
        rolled = pltpu.roll(
            jnp.broadcast_to(part.astype(jnp.float32), (outputs, lanes)), 0, 1, stride=2, stride_axis=0
        )
        matrices.append(rolled[:, : 2 * outputs + tap_count].astype(jnp.bfloat16))
    x = samples_ref[...]
    joined = jnp.concatenate(
        [
            jnp.zeros((tap_count, channels), x.dtype),
            x,
            jnp.zeros((2 * outputs - tap_count, channels), x.dtype),
        ],
        axis=0,
    )
    filtered = jnp.concatenate(
        [
            exact_dot(matrices, joined[b * 2 * outputs : b * 2 * outputs + 2 * outputs + tap_count])
            for b in range(blocks)
        ],
        axis=0,
    )
    filtered = filtered.astype(jnp.bfloat16)
    spectrum = exact_dot([table_ref[p] for p in range(table_ref.shape[0])], filtered)
    real_part = spectrum[:NF]
    imag_part = spectrum[NF:]
    powers = real_part * real_part + imag_part * imag_part
    mean_power = jnp.mean(powers, axis=0, keepdims=True)
    whitening = lax.rsqrt(powers + mean_power + 1e-06)
    whitened = jnp.concatenate([real_part * whitening, imag_part * whitening], axis=0)
    extended = whitened.astype(jnp.bfloat16).astype(jnp.float32).T
    span = shifted.shape[1]
    own_f32[...] = extended[:rows]
    for i in range(chunk):
        shifted[i] = extended[i : i + span]
    slots, parts = buffers.shape[0], sems.shape[1]
    part = chunk // parts
    copies = []
    for m in range(rows // chunk):
        slot = m % slots
        if m >= slots:
            for copy in copies[m - slots]:
                copy.wait()
        base = m * chunk
        for i in range(chunk):
            a = own_f32[base + i : base + i + 1, :]
            b = shifted[i, base : base + LAGS, :]
            acc_re, acc_im = product_terms(a, b)
            store_row(buffers.at[slot], i, acc_re, acc_im, 1)
        group = []
        for p in range(parts):
            copy = pltpu.make_async_copy(
                buffers.at[slot, pl.ds(p * part, part)],
                out_hbm.at[pl.ds(base + p * part, part)],
                sems.at[slot, p],
            )
            copy.start()
            group.append(copy)
        copies.append(group)
    for group in copies[-slots:]:
        for copy in group:
            copy.wait()


def fused_spectra(samples, filter_taps, table_t, rows):
    length, channels = samples.shape
    chunk = 8
    span = channels - chunk
    return pl.pallas_call(
        functools.partial(fused_kernel, rows, chunk),
        out_shape=jax.ShapeDtypeStruct((rows, LAGS, NFFT), jnp.bfloat16),
        in_specs=[pl.BlockSpec(memory_space=pltpu.SMEM)] + [pl.BlockSpec(memory_space=pltpu.VMEM)] * 2,
        out_specs=pl.BlockSpec(memory_space=pl.ANY),
        scratch_shapes=[
            pltpu.VMEM((rows, NFFT), jnp.float32),
            pltpu.VMEM((chunk, span, NFFT), jnp.float32),
            pltpu.VMEM((rows // chunk, chunk, LAGS, NFFT), jnp.bfloat16),
            pltpu.SemaphoreType.DMA((rows // chunk, 4)),
        ],
        cost_estimate=pl.CostEstimate(
            flops=6 * rows * LAGS * NF + 12 * channels * (NF * 320 * length // 256 + NFFT * NFFT),
            transcendentals=2 * NF * channels,
            bytes_accessed=rows * LAGS * NFFT * 2 + 2 * samples.size + 2 * table_t.size,
        ),
    )(filter_taps, samples, table_t)


def cross_spectra(own, extended):
    rows, segments, columns = own.shape
    reach_rows = extended.shape[0]
    own_flat = own.reshape(rows, segments * columns)
    ext_flat = extended.reshape(reach_rows, segments * columns)
    rows_per_step = 8
    span = reach_rows - rows_per_step
    scratch_bytes = rows_per_step * span * segments * columns * 4
    cost = pl.CostEstimate(
        flops=6 * rows * LAGS * NF * segments,
        transcendentals=0,
        bytes_accessed=rows * LAGS * columns * 2 + 2 * segments * (rows + reach_rows) * columns,
    )
    common = dict(
        out_shape=jax.ShapeDtypeStruct((rows, LAGS, columns), jnp.bfloat16),
        grid=(rows // rows_per_step,),
        in_specs=[
            pl.BlockSpec((rows, segments * columns), lambda i: (0, 0)),
            pl.BlockSpec((reach_rows, segments * columns), lambda i: (0, 0)),
        ],
        out_specs=pl.BlockSpec((rows_per_step, LAGS, columns), lambda i: (i, 0, 0)),
        cost_estimate=cost,
    )
    if scratch_bytes <= 8 * 1024 * 1024:
        return pl.pallas_call(
            functools.partial(cross_kernel_shifted, segments, rows_per_step),
            scratch_shapes=[
                pltpu.VMEM((rows, segments * columns), jnp.float32),
                pltpu.VMEM((rows_per_step, span, segments * columns), jnp.float32),
            ],
            compiler_params=pltpu.CompilerParams(dimension_semantics=("arbitrary",)),
            **common,
        )(own_flat, ext_flat)
    return pl.pallas_call(
        functools.partial(cross_kernel, segments, rows_per_step), **common
    )(own_flat, ext_flat)


def body(strain, filter_taps):
    extent = lax.axis_size("ta")
    columns_n = lax.axis_size("col")
    section_rows, slab = strain.shape
    block_rows = section_rows // extent
    reach = LAGS // block_rows
    turned = strain.T
    route = [(c + 1, c) for c in range(columns_n - 1)]
    following = lax.ppermute(turned, "col", route)
    tail = following[:, : reach * block_rows]
    width = (reach + 1) * block_rows
    windows = channel_windows(turned, tail, extent, width, reach * block_rows)
    gathered = lax.all_to_all(windows, "ta", split_axis=0, concat_axis=0, tiled=True)
    samples = gathered.reshape(extent * slab, width)
    if extent * slab == 2 * NFFT:
        table_parts = jnp.stack(split_three_kept(fourier_table_t()))
        return fused_spectra(samples, filter_taps, table_parts, block_rows)[None]
    filtered = decimate_t(samples.astype(jnp.float32), filter_taps)
    whitened_t = whiten_t(filtered)
    segments, columns, _ = whitened_t.shape
    if segments * 8 * width * columns * 4 <= 8 * 1024 * 1024:
        flat = whitened_t.reshape(segments * columns, width)
        return cross_spectra_pieces([flat])[None]
    extended = whitened_t.transpose(2, 0, 1)
    return cross_spectra(extended[:block_rows], extended)[None]


def solution(mesh):
    return jax.shard_map(
        body,
        mesh=mesh,
        in_specs=(P("col", "ta"), P()),
        out_specs=P("col", "ta", None, None),
        check_vma=False,
    )
```

```python
import functools

import jax
import jax.numpy as jnp
from jax import lax
from jax.experimental import pallas as pl
from jax.experimental.pallas import tpu as pltpu
from jax.sharding import PartitionSpec as P

NFFT = 256
NF = 128
LAGS = 128


def tap_rows(filter_taps, outputs):
    tap_count = filter_taps.shape[0]
    window = 2 * outputs + tap_count
    flipped = filter_taps[::-1]
    period = jnp.concatenate([flipped, jnp.zeros((window + 2 - tap_count,), jnp.float32)])
    repeated = jnp.tile(period, outputs)[: outputs * window]
    return repeated.reshape(outputs, window)


def decimate_t(samples, filter_taps):
    length, channels = samples.shape
    tap_count = filter_taps.shape[0]
    outputs = min(length, NFFT) // 2
    blocks = length // (2 * outputs)
    joined = jnp.concatenate(
        [
            jnp.zeros((tap_count, channels), jnp.float32),
            samples,
            jnp.zeros((2 * outputs - tap_count, channels), jnp.float32),
        ],
        axis=0,
    )
    joined = joined.reshape(blocks + 1, 2 * outputs, channels)
    windows = jnp.concatenate([joined[:-1], joined[1:, :tap_count]], axis=1)
    matrix = tap_rows(filter_taps, outputs)
    result = jnp.einsum("tw,bwc->btc", matrix, windows, precision=lax.Precision.HIGHEST)
    return result.reshape(blocks * outputs, channels).astype(jnp.bfloat16)


def fourier_table():
    moment = lax.broadcasted_iota(jnp.int32, (NFFT, NF), 0)
    frequency = lax.broadcasted_iota(jnp.int32, (NFFT, NF), 1) + 1
    phase_index = moment * frequency % NFFT
    angles = phase_index.astype(jnp.float32) * (2.0 * jnp.pi / NFFT)
    window_taper = 0.5 - 0.5 * jnp.cos(moment.astype(jnp.float32) * (2.0 * jnp.pi / NFFT))
    return jnp.concatenate(
        [window_taper * jnp.cos(angles), -window_taper * jnp.sin(angles)], axis=1
    )


def fourier_table_t():
    moment = lax.broadcasted_iota(jnp.int32, (NFFT, NFFT), 1)
    frequency = lax.broadcasted_iota(jnp.int32, (NFFT, NFFT), 0) % NF + 1
    phase_index = moment * frequency % NFFT
    angles = phase_index.astype(jnp.float32) * (2.0 * jnp.pi / NFFT)
    window_taper = 0.5 - 0.5 * jnp.cos(moment.astype(jnp.float32) * (2.0 * jnp.pi / NFFT))
    real_rows = lax.broadcasted_iota(jnp.int32, (NFFT, NFFT), 0) < NF
    return jnp.where(real_rows, window_taper * jnp.cos(angles), -window_taper * jnp.sin(angles))


def whiten_t(filtered):
    length, channels = filtered.shape
    pieces = filtered.reshape(length // NF, NF, channels)
    segment_rows = jnp.concatenate([pieces[:-1], pieces[1:]], axis=1)
    spectrum = jnp.einsum(
        "nf,snc->sfc",
        fourier_table(),
        segment_rows.astype(jnp.float32),
        precision=lax.Precision.HIGHEST,
    )
    real_part = spectrum[:, :NF]
    imag_part = spectrum[:, NF:]
    powers = real_part * real_part + imag_part * imag_part
    mean_power = jnp.mean(powers, axis=1, keepdims=True)
    whitening = 1.0 / jnp.sqrt(powers + mean_power + 1e-06)
    return jnp.concatenate([real_part * whitening, imag_part * whitening], axis=1).astype(
        jnp.bfloat16
    )


def windows_kernel(width, tail_rows, x_ref, out_ref):
    x = x_ref[...].astype(jnp.float32)
    padded = jnp.concatenate([x, jnp.zeros((x.shape[0], tail_rows), jnp.float32)], axis=1)
    step = (padded.shape[1] - width) // (out_ref.shape[0] - 1)
    for j in range(out_ref.shape[0]):
        out_ref[j] = padded[:, j * step : j * step + width].astype(out_ref.dtype)


def channel_windows(turned, tail, extent, width, tail_rows):
    slab, rows = turned.shape
    windows = pl.pallas_call(
        functools.partial(windows_kernel, width, tail_rows),
        out_shape=jax.ShapeDtypeStruct((extent, slab, width), turned.dtype),
        cost_estimate=pl.CostEstimate(
            flops=0, transcendentals=0, bytes_accessed=2 * (slab * rows + extent * slab * width)
        ),
    )(turned)
    step = (rows + tail_rows - width) // (extent - 1)
    count = -(-tail_rows // step)
    first = extent - count
    padded = jnp.concatenate([turned[:, first * step :], tail], axis=1)
    patch = jnp.stack([padded[:, j * step : j * step + width] for j in range(count)])
    return lax.dynamic_update_slice(windows, patch, (first, 0, 0))


def cross_kernel(segments, rows_per_step, own_ref, ext_ref, out_ref):
    step = pl.program_id(0)
    base = pl.multiple_of(step * rows_per_step, rows_per_step)
    for i in range(rows_per_step):
        acc_re = None
        acc_im = None
        for s in range(segments):
            a = own_ref[pl.ds(base, rows_per_step), pl.ds(s * NFFT, NFFT)]
            a = a.astype(jnp.float32)[i : i + 1]
            window = ext_ref[pl.ds(base, LAGS + rows_per_step), pl.ds(s * NFFT, NFFT)]
            b = window.astype(jnp.float32)[i : i + LAGS]
            terms = product_terms(a, b)
            if acc_re is None:
                acc_re, acc_im = terms
            else:
                acc_re = [x + y for x, y in zip(acc_re, terms[0])]
                acc_im = [x + y for x, y in zip(acc_im, terms[1])]
        store_row(out_ref, i, acc_re, acc_im, segments)


def product_terms(a, b):
    ar = a[:, :NF]
    ai = a[:, NF:]
    br = b[:, :NF]
    bi = b[:, NF:]
    return [ar * br, ai * bi], [ai * br, ar * bi]


def store_row(out_ref, i, acc_re, acc_im, segments):
    re = acc_re[0] + acc_re[1]
    im = acc_im[0] - acc_im[1]
    if segments > 1:
        re = re / segments
        im = im / segments
    out_ref[i, :, :NF] = re.astype(out_ref.dtype)
    out_ref[i, :, NF:] = im.astype(out_ref.dtype)


def cross_kernel_shifted(segments, rows_per_step, own_ref, ext_ref, out_ref, own_f32, shifted):
    step = pl.program_id(0)
    span = shifted.shape[1]

    @pl.when(step == 0)
    def _():
        own_f32[...] = own_ref[...].astype(jnp.float32)
        whole = ext_ref[...].astype(jnp.float32)
        for i in range(rows_per_step):
            shifted[i] = whole[i : i + span]

    base = pl.multiple_of(step * rows_per_step, rows_per_step)
    for i in range(rows_per_step):
        acc_re = None
        acc_im = None
        for s in range(segments):
            a = own_f32[pl.ds(base + i, 1), pl.ds(s * NFFT, NFFT)]
            b = shifted[i, pl.ds(base, LAGS), pl.ds(s * NFFT, NFFT)]
            terms = product_terms(a, b)
            if acc_re is None:
                acc_re, acc_im = terms
            else:
                acc_re = [x + y for x, y in zip(acc_re, terms[0])]
                acc_im = [x + y for x, y in zip(acc_im, terms[1])]
        store_row(out_ref, i, acc_re, acc_im, segments)


def cross_kernel_pieces(segments, rows, chunk, *refs):
    pieces = refs[:-5]
    out_hbm, own_f32, shifted, buffers, sems = refs[-5:]
    span = shifted.shape[1]
    extended = jnp.concatenate(
        [
            jnp.concatenate(
                [piece[s * NFFT : (s + 1) * NFFT, :].astype(jnp.float32).T for s in range(segments)],
                axis=1,
            )
            for piece in pieces
        ],
        axis=0,
    )
    own_f32[...] = extended[:rows]
    for i in range(chunk):
        shifted[i] = extended[i : i + span]
    slots, parts = buffers.shape[0], sems.shape[1]
    part = chunk // parts
    copies = []
    for m in range(rows // chunk):
        slot = m % slots
        if m >= slots:
            for copy in copies[m - slots]:
                copy.wait()
        base = m * chunk
        for i in range(chunk):
            acc_re = None
            acc_im = None
            for s in range(segments):
                a = own_f32[base + i : base + i + 1, s * NFFT : (s + 1) * NFFT]
                b = shifted[i, base : base + LAGS, s * NFFT : (s + 1) * NFFT]
                terms = product_terms(a, b)
                if acc_re is None:
                    acc_re, acc_im = terms
                else:
                    acc_re = [x + y for x, y in zip(acc_re, terms[0])]
                    acc_im = [x + y for x, y in zip(acc_im, terms[1])]
            store_row(buffers.at[slot], i, acc_re, acc_im, segments)
        group = []
        for p in range(parts):
            copy = pltpu.make_async_copy(
                buffers.at[slot, pl.ds(p * part, part)],
                out_hbm.at[pl.ds(base + p * part, part)],
                sems.at[slot, p],
            )
            copy.start()
            group.append(copy)
        copies.append(group)
    for group in copies[-slots:]:
        for copy in group:
            copy.wait()


def cross_spectra_pieces(pieces):
    width = pieces[0].shape[0]
    rows = sum(piece.shape[1] for piece in pieces) - LAGS
    segments = width // NFFT
    chunk = 8
    span = rows + LAGS - chunk
    return pl.pallas_call(
        functools.partial(cross_kernel_pieces, segments, rows, chunk),
        out_shape=jax.ShapeDtypeStruct((rows, LAGS, NFFT), jnp.bfloat16),
        in_specs=[pl.BlockSpec(memory_space=pltpu.VMEM)] * len(pieces),
        out_specs=pl.BlockSpec(memory_space=pl.ANY),
        scratch_shapes=[
            pltpu.VMEM((rows, width), jnp.float32),
            pltpu.VMEM((chunk, span, width), jnp.float32),
            pltpu.VMEM((4, chunk, LAGS, NFFT), jnp.bfloat16),
            pltpu.SemaphoreType.DMA((4, 4)),
        ],
        cost_estimate=pl.CostEstimate(
            flops=6 * rows * LAGS * NF * segments,
            transcendentals=0,
            bytes_accessed=rows * LAGS * NFFT * 2 + 2 * (rows + LAGS) * width,
        ),
    )(*pieces)


def split_three(values):
    high = values.astype(jnp.bfloat16)
    rest = values - high.astype(jnp.float32)
    middle = rest.astype(jnp.bfloat16)
    low = (rest - middle.astype(jnp.float32)).astype(jnp.bfloat16)
    return [high, middle, low]


def split_three_kept(values):
    high = lax.reduce_precision(values, exponent_bits=8, mantissa_bits=7)
    rest = values - high
    middle = lax.reduce_precision(rest, exponent_bits=8, mantissa_bits=7)
    low = rest - middle
    return [part.astype(jnp.bfloat16) for part in (high, middle, low)]


def exact_dot(parts, operand):
    total = None
    for part in parts:
        term = jnp.dot(part, operand, preferred_element_type=jnp.float32)
        total = term if total is None else total + term
    return total


def fused_kernel(rows, chunk, taps_ref, samples_ref, table_ref, out_hbm, own_f32, shifted,
                 buffers, sems):
    tap_count = taps_ref.shape[0]
    outputs = NFFT // 2
    length, channels = samples_ref.shape
    blocks = length // (2 * outputs)
    lanes = 3 * NF
    lane = lax.broadcasted_iota(jnp.int32, (1, lanes), 1)
    row = jnp.zeros((1, lanes), jnp.float32)
    for k in range(tap_count):
        row = jnp.where(lane == tap_count - 1 - k, taps_ref[k], row)
    matrices = []
    for part in split_three(row):
        rolled = pltpu.roll(
            jnp.broadcast_to(part.astype(jnp.float32), (outputs, lanes)), 0, 1, stride=2, stride_axis=0
        )
        matrices.append(rolled[:, : 2 * outputs + tap_count].astype(jnp.bfloat16))
    x = samples_ref[...]
    joined = jnp.concatenate(
        [
            jnp.zeros((tap_count, channels), x.dtype),
            x,
            jnp.zeros((2 * outputs - tap_count, channels), x.dtype),
        ],
        axis=0,
    )
    filtered = jnp.concatenate(
        [
            exact_dot(matrices, joined[b * 2 * outputs : b * 2 * outputs + 2 * outputs + tap_count])
            for b in range(blocks)
        ],
        axis=0,
    )
    filtered = filtered.astype(jnp.bfloat16)
    spectrum = exact_dot(split_three(table_ref[...]), filtered)
    real_part = spectrum[:NF]
    imag_part = spectrum[NF:]
    powers = real_part * real_part + imag_part * imag_part
    mean_power = jnp.mean(powers, axis=0, keepdims=True)
    whitening = lax.rsqrt(powers + mean_power + 1e-06)
    whitened = jnp.concatenate([real_part * whitening, imag_part * whitening], axis=0)
    extended = whitened.astype(jnp.bfloat16).astype(jnp.float32).T
    span = shifted.shape[1]
    own_f32[...] = extended[:rows]
    for i in range(chunk):
        shifted[i] = extended[i : i + span]
    slots, parts = buffers.shape[0], sems.shape[1]
    part = chunk // parts
    copies = []
    for m in range(rows // chunk):
        slot = m % slots
        if m >= slots:
            for copy in copies[m - slots]:
                copy.wait()
        base = m * chunk
        for i in range(chunk):
            a = own_f32[base + i : base + i + 1, :]
            b = shifted[i, base : base + LAGS, :]
            acc_re, acc_im = product_terms(a, b)
            store_row(buffers.at[slot], i, acc_re, acc_im, 1)
        group = []
        for p in range(parts):
            copy = pltpu.make_async_copy(
                buffers.at[slot, pl.ds(p * part, part)],
                out_hbm.at[pl.ds(base + p * part, part)],
                sems.at[slot, p],
            )
            copy.start()
            group.append(copy)
        copies.append(group)
    for group in copies[-slots:]:
        for copy in group:
            copy.wait()


def fused_spectra(samples, filter_taps, table_t, rows):
    length, channels = samples.shape
    chunk = 8
    span = channels - chunk
    return pl.pallas_call(
        functools.partial(fused_kernel, rows, chunk),
        out_shape=jax.ShapeDtypeStruct((rows, LAGS, NFFT), jnp.bfloat16),
        in_specs=[pl.BlockSpec(memory_space=pltpu.SMEM)] + [pl.BlockSpec(memory_space=pltpu.VMEM)] * 2,
        out_specs=pl.BlockSpec(memory_space=pl.ANY),
        scratch_shapes=[
            pltpu.VMEM((rows, NFFT), jnp.float32),
            pltpu.VMEM((chunk, span, NFFT), jnp.float32),
            pltpu.VMEM((4, chunk, LAGS, NFFT), jnp.bfloat16),
            pltpu.SemaphoreType.DMA((4, 4)),
        ],
        cost_estimate=pl.CostEstimate(
            flops=6 * rows * LAGS * NF + 12 * channels * (NF * 320 * length // 256 + NFFT * NFFT),
            transcendentals=2 * NF * channels,
            bytes_accessed=rows * LAGS * NFFT * 2 + 2 * samples.size + 4 * table_t.size,
        ),
    )(filter_taps, samples, table_t)


def cross_spectra(own, extended):
    rows, segments, columns = own.shape
    reach_rows = extended.shape[0]
    own_flat = own.reshape(rows, segments * columns)
    ext_flat = extended.reshape(reach_rows, segments * columns)
    rows_per_step = 8
    span = reach_rows - rows_per_step
    scratch_bytes = rows_per_step * span * segments * columns * 4
    cost = pl.CostEstimate(
        flops=6 * rows * LAGS * NF * segments,
        transcendentals=0,
        bytes_accessed=rows * LAGS * columns * 2 + 2 * segments * (rows + reach_rows) * columns,
    )
    common = dict(
        out_shape=jax.ShapeDtypeStruct((rows, LAGS, columns), jnp.bfloat16),
        grid=(rows // rows_per_step,),
        in_specs=[
            pl.BlockSpec((rows, segments * columns), lambda i: (0, 0)),
            pl.BlockSpec((reach_rows, segments * columns), lambda i: (0, 0)),
        ],
        out_specs=pl.BlockSpec((rows_per_step, LAGS, columns), lambda i: (i, 0, 0)),
        cost_estimate=cost,
    )
    if scratch_bytes <= 8 * 1024 * 1024:
        return pl.pallas_call(
            functools.partial(cross_kernel_shifted, segments, rows_per_step),
            scratch_shapes=[
                pltpu.VMEM((rows, segments * columns), jnp.float32),
                pltpu.VMEM((rows_per_step, span, segments * columns), jnp.float32),
            ],
            compiler_params=pltpu.CompilerParams(dimension_semantics=("arbitrary",)),
            **common,
        )(own_flat, ext_flat)
    return pl.pallas_call(
        functools.partial(cross_kernel, segments, rows_per_step), **common
    )(own_flat, ext_flat)


def body(strain, filter_taps):
    extent = lax.axis_size("ta")
    columns_n = lax.axis_size("col")
    section_rows, slab = strain.shape
    block_rows = section_rows // extent
    reach = LAGS // block_rows
    turned = strain.T
    route = [(c + 1, c) for c in range(columns_n - 1)]
    following = lax.ppermute(turned, "col", route)
    tail = following[:, : reach * block_rows]
    width = (reach + 1) * block_rows
    windows = channel_windows(turned, tail, extent, width, reach * block_rows)
    gathered = lax.all_to_all(windows, "ta", split_axis=0, concat_axis=0, tiled=True)
    samples = gathered.reshape(extent * slab, width)
    if extent * slab == 2 * NFFT:
        return fused_spectra(samples, filter_taps, fourier_table_t(), block_rows)[None]
    filtered = decimate_t(samples.astype(jnp.float32), filter_taps)
    whitened_t = whiten_t(filtered)
    segments, columns, _ = whitened_t.shape
    if segments * 8 * width * columns * 4 <= 8 * 1024 * 1024:
        flat = whitened_t.reshape(segments * columns, width)
        return cross_spectra_pieces([flat])[None]
    extended = whitened_t.transpose(2, 0, 1)
    return cross_spectra(extended[:block_rows], extended)[None]


def solution(mesh):
    return jax.shard_map(
        body,
        mesh=mesh,
        in_specs=(P("col", "ta"), P()),
        out_specs=P("col", "ta", None, None),
        check_vma=False,
    )
```
